128 devices in a mesh: row: 8 (over x, core), col: 16 (over z, y).
Axes of the slice: x: 4, y: 4, z: 4, core: 2. Of those that a mesh axis runs over, the one named last changes fastest.
Arguments:
- inputs: bfloat16 [2048, 2048, 128], P('row', 'col'), may hold values from -6 to 6
- hidden: bfloat16 [2048, 2048, 128], P('row', 'col'), may hold values from -6 to 6
- motion: int32 [2, 128, 128], replicated, may hold values from 0 to 127, as said below
- kern_in: float32 [3, 3, 128], replicated, may hold values from -2 to 2
- kern_hid: float32 [3, 3, 128], replicated, may hold values from -2 to 2
- w_in: bfloat16 [128, 384], replicated, may hold values from -0.5 to 0.5
- w_hid: bfloat16 [128, 384], replicated, may hold values from -0.5 to 0.5
- bias_in: float32 [384], replicated, may hold values from -3 to 3
- bias_hid: float32 [384], replicated, may hold values from -3 to 3
Outputs:
- new_hidden: bfloat16 [2048, 2048, 128], P('row', 'col')
The draws below stay inside these ranges and needn't reach their ends.
Inputs may be any that keep to these rules, and one draw needn't show every extreme that they name: `motion`: for every destination block, the source block row differs from its own block row by at most 4 and the source block column from its own block column by at most 4; some block is displaced by exactly 4 in each direction along each dimension. Sources lie inside the image.
All inputs are finite; a program needn't handle non-finite values.
Results may differ from the reference program's by a relative error of at most 0.004.
Values may be sent and summed in bfloat16 or wider, within the bound.
No kernel may reach another device: no remote copies, remote signals or barrier semaphores. Data moves between devices by JAX's collectives and lax.ppermute only.
A program may use at most 256 MiB of HBM per device.

```python
import jax
import jax.numpy as jnp
from jax import lax

CIN = 128
CH = 128
BLOCK = 16
DISP = 4
GH = 2048
GW = 2048
NBR = 128
NBC = 128


def draw_motion(key, part):
    key_rows = jax.random.fold_in(key, 11)
    key_cols = jax.random.fold_in(key, 23)
    shift_rows = jax.random.randint(key_rows, (NBR, NBC), -DISP, DISP + 1, dtype=jnp.int32)
    shift_cols = jax.random.randint(key_cols, (NBR, NBC), -DISP, DISP + 1, dtype=jnp.int32)
    block_rows = jnp.arange(NBR, dtype=jnp.int32)[:, None] + jnp.zeros((NBR, NBC), jnp.int32)
    block_cols = jnp.arange(NBC, dtype=jnp.int32)[None, :] + jnp.zeros((NBR, NBC), jnp.int32)
    first_spot = (block_rows == NBR // 2) & (block_cols == NBC // 2)
    second_spot = (block_rows == NBR // 2 - 1) & (block_cols == NBC // 2 - 1)
    shift_rows = jnp.where(first_spot, DISP, jnp.where(second_spot, -DISP, shift_rows))
    shift_cols = jnp.where(first_spot, -DISP, jnp.where(second_spot, DISP, shift_cols))
    src_rows = jnp.clip(block_rows + shift_rows, 0, NBR - 1)
    src_cols = jnp.clip(block_cols + shift_cols, 0, NBC - 1)
    return jnp.stack([src_rows, src_cols]).astype(jnp.int32)


def level_of(key, shape, split, low, top_value):
    level, own = 1.0, jax.random.fold_in(key, 6)
    for position, parts in split:
        heights = jnp.exp(jax.random.uniform(jax.random.fold_in(own, position), (parts,), jnp.float32, low / len(split), top_value / len(split)))
        level = level * jnp.repeat(heights, shape[position] // parts).reshape([-1 if axis == position else 1 for axis in range(len(shape))])
    return level


def bell_draw(key, dims, deviation, bound, pieces=(), held_as=jnp.bfloat16):
    entries = jax.random.normal(key, dims, jnp.float32) * deviation
    if len(pieces) > 0:
        entries = level_of(key, dims, pieces, -0.22, 0.18) * entries
    return jnp.clip(entries, min=-bound, max=bound).astype(held_as)


def setup_inputs(seed: int = 0) -> dict:
    key_list = jax.random.split(jax.random.key(seed), 10)
    inputs = bell_draw(key_list[0], (GH, GW, CIN), 1.0, 6.0, ((0, 8), (1, 16)))
    hidden = bell_draw(key_list[1], (GH, GW, CH), 1.0, 6.0, ((0, 8), (1, 16)))
    motion = draw_motion(jax.random.fold_in(key_list[9], 71), 0)
    kern_in = bell_draw(key_list[3], (3, 3, CIN), 9 ** -0.5, 2.0, (), jnp.float32)
    kern_hid = bell_draw(key_list[4], (3, 3, CH), 9 ** -0.5, 2.0, (), jnp.float32)
    w_in = bell_draw(key_list[5], (CIN, 3 * CH), CIN ** -0.5, 0.5)
    w_hid = bell_draw(key_list[6], (CH, 3 * CH), CH ** -0.5, 0.5)
    bias_in = bell_draw(key_list[7], (3 * CH,), 0.5, 3.0, (), jnp.float32)
    bias_hid = bell_draw(key_list[8], (3 * CH,), 0.5, 3.0, (), jnp.float32)
    return dict(inputs=inputs, hidden=hidden, motion=motion, kern_in=kern_in, kern_hid=kern_hid, w_in=w_in, w_hid=w_hid, bias_in=bias_in, bias_hid=bias_hid)


def warp_blocks(source, src_rows, src_cols, channels):
    height, breadth = source.shape[0], source.shape[1]
    grouped = source.reshape(height // BLOCK, BLOCK, breadth // BLOCK, BLOCK * channels)
    count_r, count_c = src_rows.shape
    inner = jnp.arange(BLOCK, dtype=jnp.int32)
    picked = grouped[src_rows.astype(jnp.int32)[:, None, :], inner[None, :, None], src_cols.astype(jnp.int32)[:, None, :]]
    return picked.reshape(count_r * BLOCK, count_c * BLOCK, channels)


def depthwise(padded, kernel):
    height = padded.shape[0] - 2
    breadth = padded.shape[1] - 2
    summed = jnp.zeros((height, breadth, padded.shape[2]), jnp.float32)
    for a in range(3):
        for b in range(3):
            summed = summed + padded[a:a + height, b:b + breadth].astype(jnp.float32) * kernel[a, b]
    return summed.astype(jnp.bfloat16)


def gru_update(in_slab, hid_slab, previous, kern_in, kern_hid, w_in, w_hid, bias_in, bias_hid):
    depth_in = depthwise(in_slab, kern_in)
    depth_hid = depthwise(hid_slab, kern_hid)
    height, breadth, input_width = depth_in.shape
    hidden_width = depth_hid.shape[2]
    gates_in = jnp.dot(depth_in.reshape(height * breadth, input_width), w_in, preferred_element_type=jnp.float32) + bias_in
    gates_hid = jnp.dot(depth_hid.reshape(height * breadth, hidden_width), w_hid, preferred_element_type=jnp.float32) + bias_hid
    update = jax.nn.sigmoid(gates_in[:, :hidden_width] + gates_hid[:, :hidden_width])
    reset_gate = jax.nn.sigmoid(gates_in[:, hidden_width:2 * hidden_width] + gates_hid[:, hidden_width:2 * hidden_width])
    candidate = jnp.tanh(gates_in[:, 2 * hidden_width:] + reset_gate * gates_hid[:, 2 * hidden_width:])
    prior_state = previous.reshape(height * breadth, hidden_width).astype(jnp.float32)
    result = (1.0 - update) * candidate + update * prior_state
    return result.astype(jnp.bfloat16).reshape(height, breadth, hidden_width)


def reference(inputs, hidden, motion, kern_in, kern_hid, w_in, w_hid, bias_in, bias_hid):
    warped = warp_blocks(hidden, motion[0], motion[1], CH)
    inputs_pad = jnp.pad(inputs, ((1, 1), (1, 1), (0, 0)))
    warped_pad = jnp.pad(warped, ((1, 1), (1, 1), (0, 0)))

    def band_step(band_index):
        first_row = (band_index * BLOCK).astype(jnp.int32)
        in_slab = lax.dynamic_slice_in_dim(inputs_pad, first_row, BLOCK + 2, 0)
        hid_slab = lax.dynamic_slice_in_dim(warped_pad, first_row, BLOCK + 2, 0)
        previous = lax.dynamic_slice_in_dim(warped, first_row, BLOCK, 0)
        return gru_update(in_slab, hid_slab, previous, kern_in, kern_hid, w_in, w_hid, bias_in, bias_hid)

    bands = lax.map(band_step, jnp.arange(NBR, dtype=jnp.int32))
    return bands.reshape(GH, GW, CH)
```

```python
import jax
import jax.numpy as jnp
from jax import lax
from jax.experimental import pallas as pl
from jax.experimental.pallas import tpu as pltpu
from jax.sharding import PartitionSpec as P

BLOCK = 16
DISP = 4
HALO = DISP * BLOCK
RC = 4


def exchange(x, axis, dim, width):
    count = lax.axis_size(axis)
    forward = [(i, i + 1) for i in range(count - 1)]
    backward = [(i + 1, i) for i in range(count - 1)]
    size = x.shape[dim]
    low = lax.ppermute(lax.slice_in_dim(x, size - width, size, axis=dim), axis, forward)
    high = lax.ppermute(lax.slice_in_dim(x, 0, width, axis=dim), axis, backward)
    return low, high


def pad_one(x):
    left, right = exchange(x, "col", 1, 1)
    x = jnp.concatenate([left, x, right], axis=1)
    top, bottom = exchange(x, "row", 0, 1)
    return jnp.concatenate([top, x, bottom], axis=0)


def warp_kernel(srel_ref, c_ref, l_ref, r_ref, t_ref, b_ref, out_ref, sem):
    tile_h, tile_w = c_ref.shape[0], c_ref.shape[1]
    per_row = tile_w // BLOCK

    def issue(k, carry):
        i = k // per_row
        j = k % per_row
        r0 = srel_ref[2 * k] * BLOCK
        c0 = srel_ref[2 * k + 1] * BLOCK
        dst = out_ref.at[pl.ds(i * BLOCK, BLOCK), pl.ds(j * BLOCK, BLOCK), :]

        def copy(src):
            pltpu.make_async_copy(src, dst, sem.at[0]).start()

        @pl.when(r0 < 0)
        def _():
            copy(t_ref.at[pl.ds(r0 + HALO, BLOCK), pl.ds(c0 + HALO, BLOCK), :])

        @pl.when(r0 >= tile_h)
        def _():
            copy(b_ref.at[pl.ds(r0 - tile_h, BLOCK), pl.ds(c0 + HALO, BLOCK), :])

        inside = (r0 >= 0) & (r0 < tile_h)

        @pl.when(inside & (c0 < 0))
        def _():
            copy(l_ref.at[pl.ds(r0, BLOCK), pl.ds(c0 + HALO, BLOCK), :])

        @pl.when(inside & (c0 >= tile_w))
        def _():
            copy(r_ref.at[pl.ds(r0, BLOCK), pl.ds(c0 - tile_w, BLOCK), :])

        @pl.when(inside & (c0 >= 0) & (c0 < tile_w))
        def _():
            copy(c_ref.at[pl.ds(r0, BLOCK), pl.ds(c0, BLOCK), :])

        return carry

    lax.fori_loop(0, (tile_h // BLOCK) * per_row, issue, 0)
    pltpu.make_async_copy(c_ref, out_ref, sem.at[0]).wait()


def warp(srel, hidden, left, right, top, bottom):
    any_spec = pl.BlockSpec(memory_space=pl.ANY)
    return pl.pallas_call(
        warp_kernel,
        grid_spec=pltpu.PrefetchScalarGridSpec(
            num_scalar_prefetch=1,
            grid=(1,),
            in_specs=[any_spec] * 5,
            out_specs=any_spec,
            scratch_shapes=[pltpu.SemaphoreType.DMA((1,))],
        ),
        out_shape=jax.ShapeDtypeStruct(hidden.shape, hidden.dtype),
    )(srel, hidden, left, right, top, bottom)


def gru_kernel(xin_hbm, xhid_hbm, kin_ref, khid_ref, win_ref, whid_ref, bin_ref, bhid_ref,
               out_ref, ibuf, hbuf, ifl, hfl, sem):
    band = pl.program_id(0)
    bands = pl.num_programs(0)
    height = out_ref.shape[0]
    width = out_ref.shape[1]
    ch = out_ref.shape[2]

    def fetch(which, slot):
        rows = pl.ds(which * height, height + 2)
        return (
            pltpu.make_async_copy(xin_hbm.at[rows], ibuf.at[slot], sem.at[0, slot]),
            pltpu.make_async_copy(xhid_hbm.at[rows], hbuf.at[slot], sem.at[1, slot]),
        )

    @pl.when(band == 0)
    def _():
        for c in fetch(band, 0):
            c.start()

    @pl.when(band + 1 < bands)
    def _():
        for c in fetch(band + 1, (band + 1) % 2):
            c.start()

    slot = band % 2
    for c in fetch(band, slot):
        c.wait()

    ifl[...] = ibuf[slot].astype(jnp.float32)
    hfl[...] = hbuf[slot].astype(jnp.float32)

    kin = kin_ref[...]
    khid = khid_ref[...]
    win = win_ref[...]
    whid = whid_ref[...]
    bin_ = bin_ref[...]
    bhid = bhid_ref[...]

    def depth(src, kern, r0):
        acc = jnp.zeros((RC, width, ch), jnp.float32)
        for a in range(3):
            for b in range(3):
                acc = acc + src[pl.ds(r0 + a, RC), pl.ds(b, width), :] * kern[a, b]
        return acc.astype(jnp.bfloat16).reshape(RC * width, ch)

    def chunk(step, carry):
        r0 = step * RC
        d_in = depth(ifl, kin, r0)
        d_hid = depth(hfl, khid, r0)
        gi = jnp.dot(d_in, win, preferred_element_type=jnp.float32) + bin_
        gh = jnp.dot(d_hid, whid, preferred_element_type=jnp.float32) + bhid
        update = jax.nn.sigmoid(gi[:, :ch] + gh[:, :ch])
        reset = jax.nn.sigmoid(gi[:, ch:2 * ch] + gh[:, ch:2 * ch])
        cand = jnp.tanh(gi[:, 2 * ch:] + reset * gh[:, 2 * ch:])
        prev = hfl[pl.ds(r0 + 1, RC), pl.ds(1, width), :].reshape(RC * width, ch)
        new = (1.0 - update) * cand + update * prev
        out_ref[pl.ds(r0, RC)] = new.astype(out_ref.dtype).reshape(RC, width, ch)
        return carry

    lax.fori_loop(0, height // RC, chunk, 0)


def gru(inputs_pad, warped_pad, kern_in, kern_hid, w_in, w_hid, bias_in, bias_hid):
    tile_h = inputs_pad.shape[0] - 2
    width = inputs_pad.shape[1] - 2
    ch = w_hid.shape[0]
    bands = tile_h // BLOCK
    any_spec = pl.BlockSpec(memory_space=pl.ANY)

    def full(shape):
        return pl.BlockSpec(shape, lambda b: (0,) * len(shape))

    win_shape = (2, BLOCK + 2, width + 2, ch)
    return pl.pallas_call(
        gru_kernel,
        grid=(bands,),
        in_specs=[
            any_spec,
            any_spec,
            full(kern_in.shape),
            full(kern_hid.shape),
            full(w_in.shape),
            full(w_hid.shape),
            full((1, w_in.shape[1])),
            full((1, w_hid.shape[1])),
        ],
        out_specs=pl.BlockSpec((BLOCK, width, ch), lambda b: (b, 0, 0)),
        out_shape=jax.ShapeDtypeStruct((tile_h, width, ch), jnp.bfloat16),
        scratch_shapes=[
            pltpu.VMEM(win_shape, jnp.bfloat16),
            pltpu.VMEM(win_shape, jnp.bfloat16),
            pltpu.VMEM(win_shape[1:], jnp.float32),
            pltpu.VMEM(win_shape[1:], jnp.float32),
            pltpu.SemaphoreType.DMA((2, 2)),
        ],
        compiler_params=pltpu.CompilerParams(dimension_semantics=("arbitrary",)),
    )(inputs_pad, warped_pad, kern_in, kern_hid, w_in, w_hid,
      bias_in.reshape(1, -1), bias_hid.reshape(1, -1))


def body(inputs, hidden, motion, kern_in, kern_hid, w_in, w_hid, bias_in, bias_hid):
    tile_h, tile_w, channels = hidden.shape
    block_count_r = tile_h // BLOCK
    block_count_c = tile_w // BLOCK
    row_base = lax.axis_index("row") * block_count_r
    col_base = lax.axis_index("col") * block_count_c
    anchor = jnp.zeros((), jnp.int32)

    left, right = exchange(hidden, "col", 1, HALO)
    wide = jnp.concatenate([left, hidden, right], axis=1)
    top, bottom = exchange(wide, "row", 0, HALO)

    sources = lax.dynamic_slice(
        motion, (anchor, row_base, col_base), (2, block_count_r, block_count_c)
    )
    src_r = jnp.clip(sources[0] - row_base, -DISP, block_count_r + DISP - 1)
    src_c = jnp.clip(sources[1] - col_base, -DISP, block_count_c + DISP - 1)
    srel = jnp.stack([src_r, src_c], axis=-1).reshape(-1).astype(jnp.int32)

    warped = warp(srel, hidden, left, right, top, bottom)
    warped_pad = pad_one(warped)
    inputs_pad = pad_one(inputs)
    return gru(inputs_pad, warped_pad, kern_in, kern_hid, w_in, w_hid, bias_in, bias_hid)


def solution(mesh):
    in_specs = (P("row", "col", None), P("row", "col", None), P(), P(), P(), P(), P(), P(), P())
    out_specs = P("row", "col", None)
    return jax.shard_map(body, mesh=mesh, in_specs=in_specs, out_specs=out_specs, check_vma=False)
```

```python
import jax
import jax.numpy as jnp
from jax import lax
from jax.experimental import pallas as pl
from jax.experimental.pallas import tpu as pltpu
from jax.sharding import PartitionSpec as P

BLOCK = 16
DISP = 4
HALO = DISP * BLOCK
RC = 4


def exchange(x, axis, dim, width):
    count = lax.axis_size(axis)
    forward = [(i, i + 1) for i in range(count - 1)]
    backward = [(i + 1, i) for i in range(count - 1)]
    size = x.shape[dim]
    low = lax.ppermute(lax.slice_in_dim(x, size - width, size, axis=dim), axis, forward)
    high = lax.ppermute(lax.slice_in_dim(x, 0, width, axis=dim), axis, backward)
    return low, high


def pad_one(x):
    left, right = exchange(x, "col", 1, 1)
    x = jnp.concatenate([left, x, right], axis=1)
    top, bottom = exchange(x, "row", 0, 1)
    return jnp.concatenate([top, x, bottom], axis=0)


def warp_kernel(srel_ref, c_hbm, l_hbm, r_hbm, t_hbm, b_hbm, out_ref, c_ref, l_ref, r_ref,
                t_ref, b_ref, sem):
    pieces = ((c_hbm, c_ref), (l_hbm, l_ref), (r_hbm, r_ref), (t_hbm, t_ref), (b_hbm, b_ref))
    copies = [pltpu.make_async_copy(h, v, sem.at[n]) for n, (h, v) in enumerate(pieces)]
    for c in copies:
        c.start()
    for c in copies:
        c.wait()
    tile_h, per_row = c_ref.shape[0], c_ref.shape[1]
    side = l_ref.shape[1]

    def gather(k, carry):
        i = k // per_row
        j = k % per_row
        r0 = srel_ref[2 * k] * BLOCK
        cb = srel_ref[2 * k + 1]
        rows = pl.ds(i * BLOCK, BLOCK)

        def put(src):
            out_ref[rows, j] = src

        @pl.when(r0 < 0)
        def _():
            put(t_ref[pl.ds(r0 + HALO, BLOCK), cb + side])

        @pl.when(r0 >= tile_h)
        def _():
            put(b_ref[pl.ds(r0 - tile_h, BLOCK), cb + side])

        inside = (r0 >= 0) & (r0 < tile_h)

        @pl.when(inside & (cb < 0))
        def _():
            put(l_ref[pl.ds(r0, BLOCK), cb + side])

        @pl.when(inside & (cb >= per_row))
        def _():
            put(r_ref[pl.ds(r0, BLOCK), cb - per_row])

        @pl.when(inside & (cb >= 0) & (cb < per_row))
        def _():
            put(c_ref[pl.ds(r0, BLOCK), cb])

        return carry

    lax.fori_loop(0, tile_h // BLOCK * per_row, gather, 0)


def warp(srel, hidden, left, right, top, bottom):
    def blocked(x):
        return x.reshape(x.shape[0], x.shape[1] // BLOCK, BLOCK, x.shape[2])

    parts = [blocked(x) for x in (hidden, left, right, top, bottom)]
    any_spec = pl.BlockSpec(memory_space=pl.ANY)
    shape = parts[0].shape
    out = pl.pallas_call(
        warp_kernel,
        grid_spec=pltpu.PrefetchScalarGridSpec(
            num_scalar_prefetch=1,
            grid=(1,),
            in_specs=[any_spec] * 5,
            out_specs=pl.BlockSpec(shape, lambda g, s: (0, 0, 0, 0)),
            scratch_shapes=[pltpu.VMEM(x.shape, x.dtype) for x in parts]
            + [pltpu.SemaphoreType.DMA((5,))],
        ),
        out_shape=jax.ShapeDtypeStruct(shape, hidden.dtype),
        compiler_params=pltpu.CompilerParams(vmem_limit_bytes=60 * 1024 * 1024),
    )(srel, *parts)
    return out.reshape(hidden.shape)


def gru_kernel(xin_hbm, xhid_hbm, kin_ref, khid_ref, win_ref, whid_ref, bin_ref, bhid_ref,
               out_ref, ibuf, hbuf, ifl, hfl, sem):
    band = pl.program_id(0)
    bands = pl.num_programs(0)
    height = out_ref.shape[0]
    width = out_ref.shape[1]
    ch = out_ref.shape[2]

    def fetch(which, slot):
        rows = pl.ds(which * height, height + 2)
        return (
            pltpu.make_async_copy(xin_hbm.at[rows], ibuf.at[slot], sem.at[0, slot]),
            pltpu.make_async_copy(xhid_hbm.at[rows], hbuf.at[slot], sem.at[1, slot]),
        )

    @pl.when(band == 0)
    def _():
        for c in fetch(band, 0):
            c.start()

    @pl.when(band + 1 < bands)
    def _():
        for c in fetch(band + 1, (band + 1) % 2):
            c.start()

    slot = band % 2
    for c in fetch(band, slot):
        c.wait()

    ifl[...] = ibuf[slot].astype(jnp.float32)
    hfl[...] = hbuf[slot].astype(jnp.float32)

    kin = kin_ref[...]
    khid = khid_ref[...]
    win = win_ref[...]
    whid = whid_ref[...]
    bin_ = bin_ref[...]
    bhid = bhid_ref[...]

    def depth(src, kern, r0):
        acc = jnp.zeros((RC, width, ch), jnp.float32)
        for a in range(3):
            for b in range(3):
                acc = acc + src[pl.ds(r0 + a, RC), pl.ds(b, width), :] * kern[a, b]
        return acc.astype(jnp.bfloat16).reshape(RC * width, ch)

    def chunk(step, carry):
        r0 = step * RC
        d_in = depth(ifl, kin, r0)
        d_hid = depth(hfl, khid, r0)
        gi = jnp.dot(d_in, win, preferred_element_type=jnp.float32) + bin_
        gh = jnp.dot(d_hid, whid, preferred_element_type=jnp.float32) + bhid
        update = jax.nn.sigmoid(gi[:, :ch] + gh[:, :ch])
        reset = jax.nn.sigmoid(gi[:, ch:2 * ch] + gh[:, ch:2 * ch])
        cand = jnp.tanh(gi[:, 2 * ch:] + reset * gh[:, 2 * ch:])
        prev = hfl[pl.ds(r0 + 1, RC), pl.ds(1, width), :].reshape(RC * width, ch)
        new = (1.0 - update) * cand + update * prev
        out_ref[pl.ds(r0, RC)] = new.astype(out_ref.dtype).reshape(RC, width, ch)
        return carry

    lax.fori_loop(0, height // RC, chunk, 0)


def gru(inputs_pad, warped_pad, kern_in, kern_hid, w_in, w_hid, bias_in, bias_hid):
    tile_h = inputs_pad.shape[0] - 2
    width = inputs_pad.shape[1] - 2
    ch = w_hid.shape[0]
    bands = tile_h // BLOCK
    any_spec = pl.BlockSpec(memory_space=pl.ANY)

    def full(shape):
        return pl.BlockSpec(shape, lambda b: (0,) * len(shape))

    win_shape = (2, BLOCK + 2, width + 2, ch)
    return pl.pallas_call(
        gru_kernel,
        grid=(bands,),
        in_specs=[
            any_spec,
            any_spec,
            full(kern_in.shape),
            full(kern_hid.shape),
            full(w_in.shape),
            full(w_hid.shape),
            full((1, w_in.shape[1])),
            full((1, w_hid.shape[1])),
        ],
        out_specs=pl.BlockSpec((BLOCK, width, ch), lambda b: (b, 0, 0)),
        out_shape=jax.ShapeDtypeStruct((tile_h, width, ch), jnp.bfloat16),
        scratch_shapes=[
            pltpu.VMEM(win_shape, jnp.bfloat16),
            pltpu.VMEM(win_shape, jnp.bfloat16),
            pltpu.VMEM(win_shape[1:], jnp.float32),
            pltpu.VMEM(win_shape[1:], jnp.float32),
            pltpu.SemaphoreType.DMA((2, 2)),
        ],
        compiler_params=pltpu.CompilerParams(dimension_semantics=("arbitrary",)),
    )(inputs_pad, warped_pad, kern_in, kern_hid, w_in, w_hid,
      bias_in.reshape(1, -1), bias_hid.reshape(1, -1))


def body(inputs, hidden, motion, kern_in, kern_hid, w_in, w_hid, bias_in, bias_hid):
    tile_h, tile_w, channels = hidden.shape
    block_count_r = tile_h // BLOCK
    block_count_c = tile_w // BLOCK
    row_base = lax.axis_index("row") * block_count_r
    col_base = lax.axis_index("col") * block_count_c
    anchor = jnp.zeros((), jnp.int32)

    left, right = exchange(hidden, "col", 1, HALO)
    count = lax.axis_size("row")
    forward = [(i, i + 1) for i in range(count - 1)]
    backward = [(i + 1, i) for i in range(count - 1)]
    down = jnp.concatenate([left[tile_h - HALO:], hidden[tile_h - HALO:], right[tile_h - HALO:]], axis=1)
    up = jnp.concatenate([left[:HALO], hidden[:HALO], right[:HALO]], axis=1)
    top = lax.ppermute(down, "row", forward)
    bottom = lax.ppermute(up, "row", backward)

    sources = lax.dynamic_slice(
        motion, (anchor, row_base, col_base), (2, block_count_r, block_count_c)
    )
    src_r = jnp.clip(sources[0] - row_base, -DISP, block_count_r + DISP - 1)
    src_c = jnp.clip(sources[1] - col_base, -DISP, block_count_c + DISP - 1)
    srel = jnp.stack([src_r, src_c], axis=-1).reshape(-1).astype(jnp.int32)

    warped = warp(srel, hidden, left, right, top, bottom)
    warped_pad = pad_one(warped)
    inputs_pad = pad_one(inputs)
    return gru(inputs_pad, warped_pad, kern_in, kern_hid, w_in, w_hid, bias_in, bias_hid)


def solution(mesh):
    in_specs = (P("row", "col", None), P("row", "col", None), P(), P(), P(), P(), P(), P(), P())
    out_specs = P("row", "col", None)
    return jax.shard_map(body, mesh=mesh, in_specs=in_specs, out_specs=out_specs, check_vma=False)
```

```python
import jax
import jax.numpy as jnp
from jax import lax
from jax.experimental import pallas as pl
from jax.experimental.pallas import tpu as pltpu
from jax.sharding import PartitionSpec as P

BLOCK = 16
DISP = 4
HALO = DISP * BLOCK
RC = 4


def exchange(x, axis, dim, width):
    count = lax.axis_size(axis)
    forward = [(i, i + 1) for i in range(count - 1)]
    backward = [(i + 1, i) for i in range(count - 1)]
    size = x.shape[dim]
    low = lax.ppermute(lax.slice_in_dim(x, size - width, size, axis=dim), axis, forward)
    high = lax.ppermute(lax.slice_in_dim(x, 0, width, axis=dim), axis, backward)
    return low, high


def ring(x):
    left, right = exchange(x, "col", 1, 1)
    last = x.shape[0] - 1
    count = lax.axis_size("row")
    forward = [(i, i + 1) for i in range(count - 1)]
    backward = [(i + 1, i) for i in range(count - 1)]
    down = jnp.concatenate([left[last:], x[last:], right[last:]], axis=1)
    up = jnp.concatenate([left[:1], x[:1], right[:1]], axis=1)
    top = lax.ppermute(down, "row", forward)[0]
    bottom = lax.ppermute(up, "row", backward)[0]
    width = x.shape[1]
    side_l = jnp.concatenate([top[:1], left[:, 0], bottom[:1]], axis=0)
    side_r = jnp.concatenate([top[width + 1:], right[:, 0], bottom[width + 1:]], axis=0)
    return side_l, side_r, top, bottom


def warp_kernel(srel_ref, *refs):
    hbm = refs[:9]
    out_ref = refs[9]
    vmem = refs[10:19]
    sem = refs[19]
    copies = [pltpu.make_async_copy(h, v, sem.at[n]) for n, (h, v) in enumerate(zip(hbm, vmem))]
    for c in copies:
        c.start()
    for c in copies:
        c.wait()
    c_ref, l_ref, r_ref, t_ref, b_ref, tl_ref, tr_ref, bl_ref, br_ref = vmem
    tile_h, per_row = c_ref.shape[0], c_ref.shape[1]
    side = l_ref.shape[1]

    def gather(k, carry):
        i = k // per_row
        j = k % per_row
        r0 = srel_ref[2 * k] * BLOCK
        cb = srel_ref[2 * k + 1]
        rows = pl.ds(i * BLOCK, BLOCK)
        above = r0 < 0
        below = r0 >= tile_h
        middle = jnp.logical_not(above | below)
        west = cb < 0
        east = cb >= per_row
        centre = jnp.logical_not(west | east)
        cases = (
            (above & west, tl_ref, r0 + HALO, cb + side),
            (above & centre, t_ref, r0 + HALO, cb),
            (above & east, tr_ref, r0 + HALO, cb - per_row),
            (middle & west, l_ref, r0, cb + side),
            (middle & centre, c_ref, r0, cb),
            (middle & east, r_ref, r0, cb - per_row),
            (below & west, bl_ref, r0 - tile_h, cb + side),
            (below & centre, b_ref, r0 - tile_h, cb),
            (below & east, br_ref, r0 - tile_h, cb - per_row),
        )
        for cond, ref, rr, cc in cases:
            @pl.when(cond)
            def _():
                out_ref[rows, j] = ref[pl.ds(rr, BLOCK), cc]

        return carry

    lax.fori_loop(0, tile_h // BLOCK * per_row, gather, 0)


def warp(srel, pieces):
    def blocked(x):
        return x.reshape(x.shape[0], x.shape[1] // BLOCK, BLOCK, x.shape[2])

    parts = [blocked(x) for x in pieces]
    any_spec = pl.BlockSpec(memory_space=pl.ANY)
    shape = parts[0].shape
    out = pl.pallas_call(
        warp_kernel,
        grid_spec=pltpu.PrefetchScalarGridSpec(
            num_scalar_prefetch=1,
            grid=(1,),
            in_specs=[any_spec] * len(parts),
            out_specs=pl.BlockSpec(shape, lambda g, s: (0, 0, 0, 0)),
            scratch_shapes=[pltpu.VMEM(x.shape, x.dtype) for x in parts]
            + [pltpu.SemaphoreType.DMA((len(parts),))],
        ),
        out_shape=jax.ShapeDtypeStruct(shape, pieces[0].dtype),
        compiler_params=pltpu.CompilerParams(vmem_limit_bytes=60 * 1024 * 1024),
    )(srel, *parts)
    return out.reshape(pieces[0].shape)


OFF = 8


def gru_kernel(xin_hbm, xhid_hbm, il_ref, ir_ref, it_ref, ib_ref, hl_ref, hr_ref, ht_ref, hb_ref,
               kin_ref, khid_ref, win_ref, whid_ref, bin_ref, bhid_ref,
               out_ref, ibuf, hbuf, ifl, hfl, sem):
    band = pl.program_id(0)
    bands = pl.num_programs(0)
    height = out_ref.shape[0]
    width = out_ref.shape[1]
    ch = out_ref.shape[2]

    def copies(which, slot, lo, hi):
        src = pl.ds(which * height - 1 + lo, height + 2 - lo - hi)
        dst = pl.ds(lo, height + 2 - lo - hi)
        return (
            pltpu.make_async_copy(xin_hbm.at[src], ibuf.at[slot, dst], sem.at[0, slot]),
            pltpu.make_async_copy(xhid_hbm.at[src], hbuf.at[slot, dst], sem.at[1, slot]),
        )

    def each_case(which, slot, fn):
        first = which == 0
        last = which == bands - 1

        @pl.when(first)
        def _():
            fn(copies(which, slot, 1, 0))

        @pl.when(last)
        def _():
            fn(copies(which, slot, 0, 1))

        @pl.when(jnp.logical_not(first | last))
        def _():
            fn(copies(which, slot, 0, 0))

    def start(cs):
        for c in cs:
            c.start()

    def wait(cs):
        for c in cs:
            c.wait()

    @pl.when(band == 0)
    def _():
        each_case(band, 0, start)

    @pl.when(band + 1 < bands)
    def _():
        each_case(band + 1, (band + 1) % 2, start)

    slot = band % 2
    each_case(band, slot, wait)

    span = pl.ds(band * height, height + 2)
    for buf, fl, l_ref, r_ref, t_ref, b_ref in (
        (ibuf, ifl, il_ref, ir_ref, it_ref, ib_ref),
        (hbuf, hfl, hl_ref, hr_ref, ht_ref, hb_ref),
    ):
        fl[:, pl.ds(OFF, width), :] = buf[slot].astype(jnp.float32)
        fl[:, pl.ds(OFF - 1, 1), :] = l_ref[span].astype(jnp.float32)[:, None, :]
        fl[:, pl.ds(OFF + width, 1), :] = r_ref[span].astype(jnp.float32)[:, None, :]

        @pl.when(band == 0)
        def _():
            fl[0, pl.ds(OFF - 1, width + 2), :] = t_ref[...].astype(jnp.float32)

        @pl.when(band == bands - 1)
        def _():
            fl[height + 1, pl.ds(OFF - 1, width + 2), :] = b_ref[...].astype(jnp.float32)

    kin = kin_ref[...]
    khid = khid_ref[...]
    win = win_ref[...]
    whid = whid_ref[...]
    bin_ = bin_ref[...]
    bhid = bhid_ref[...]

    def depth(src, kern, r0):
        acc = jnp.zeros((RC, width, ch), jnp.float32)
        for a in range(3):
            for b in range(3):
                acc = acc + src[pl.ds(r0 + a, RC), pl.ds(OFF - 1 + b, width), :] * kern[a, b]
        return acc.astype(jnp.bfloat16).reshape(RC * width, ch)

    def chunk(step, carry):
        r0 = step * RC
        d_in = depth(ifl, kin, r0)
        d_hid = depth(hfl, khid, r0)
        gi = jnp.dot(d_in, win, preferred_element_type=jnp.float32) + bin_
        gh = jnp.dot(d_hid, whid, preferred_element_type=jnp.float32) + bhid
        update = jax.nn.sigmoid(gi[:, :ch] + gh[:, :ch])
        reset = jax.nn.sigmoid(gi[:, ch:2 * ch] + gh[:, ch:2 * ch])
        cand = jnp.tanh(gi[:, 2 * ch:] + reset * gh[:, 2 * ch:])
        prev = hfl[pl.ds(r0 + 1, RC), pl.ds(OFF, width), :].reshape(RC * width, ch)
        new = (1.0 - update) * cand + update * prev
        out_ref[pl.ds(r0, RC)] = new.astype(out_ref.dtype).reshape(RC, width, ch)
        return carry

    lax.fori_loop(0, height // RC, chunk, 0)


def gru(inputs, warped, in_ring, hid_ring, kern_in, kern_hid, w_in, w_hid, bias_in, bias_hid):
    tile_h, width, ch = warped.shape
    bands = tile_h // BLOCK
    any_spec = pl.BlockSpec(memory_space=pl.ANY)

    def full(shape):
        return pl.BlockSpec(shape, lambda b: (0,) * len(shape))

    rings = list(in_ring) + list(hid_ring)
    return pl.pallas_call(
        gru_kernel,
        grid=(bands,),
        in_specs=[any_spec, any_spec]
        + [full(r.shape) for r in rings]
        + [
            full(kern_in.shape),
            full(kern_hid.shape),
            full(w_in.shape),
            full(w_hid.shape),
            full((1, w_in.shape[1])),
            full((1, w_hid.shape[1])),
        ],
        out_specs=pl.BlockSpec((BLOCK, width, ch), lambda b: (b, 0, 0)),
        out_shape=jax.ShapeDtypeStruct((tile_h, width, ch), jnp.bfloat16),
        scratch_shapes=[
            pltpu.VMEM((2, BLOCK + 2, width, ch), jnp.bfloat16),
            pltpu.VMEM((2, BLOCK + 2, width, ch), jnp.bfloat16),
            pltpu.VMEM((BLOCK + 2, width + 2 * OFF, ch), jnp.float32),
            pltpu.VMEM((BLOCK + 2, width + 2 * OFF, ch), jnp.float32),
            pltpu.SemaphoreType.DMA((2, 2)),
        ],
        compiler_params=pltpu.CompilerParams(dimension_semantics=("arbitrary",)),
    )(inputs, warped, *rings, kern_in, kern_hid, w_in, w_hid,
      bias_in.reshape(1, -1), bias_hid.reshape(1, -1))


def body(inputs, hidden, motion, kern_in, kern_hid, w_in, w_hid, bias_in, bias_hid):
    tile_h, tile_w, channels = hidden.shape
    block_count_r = tile_h // BLOCK
    block_count_c = tile_w // BLOCK
    row_base = lax.axis_index("row") * block_count_r
    col_base = lax.axis_index("col") * block_count_c
    anchor = jnp.zeros((), jnp.int32)

    left, right = exchange(hidden, "col", 1, HALO)
    top, bottom = exchange(hidden, "row", 0, HALO)
    top_left, bottom_left = exchange(left, "row", 0, HALO)
    top_right, bottom_right = exchange(right, "row", 0, HALO)

    sources = lax.dynamic_slice(
        motion, (anchor, row_base, col_base), (2, block_count_r, block_count_c)
    )
    src_r = jnp.clip(sources[0] - row_base, -DISP, block_count_r + DISP - 1)
    src_c = jnp.clip(sources[1] - col_base, -DISP, block_count_c + DISP - 1)
    srel = jnp.stack([src_r, src_c], axis=-1).reshape(-1).astype(jnp.int32)

    in_ring = ring(inputs)
    warped = warp(
        srel,
        (hidden, left, right, top, bottom, top_left, top_right, bottom_left, bottom_right),
    )
    hid_ring = ring(warped)
    return gru(inputs, warped, in_ring, hid_ring, kern_in, kern_hid, w_in, w_hid, bias_in, bias_hid)


def solution(mesh):
    in_specs = (P("row", "col", None), P("row", "col", None), P(), P(), P(), P(), P(), P(), P())
    out_specs = P("row", "col", None)
    return jax.shard_map(body, mesh=mesh, in_specs=in_specs, out_specs=out_specs, check_vma=False)
```

```python
import jax
import jax.numpy as jnp
from jax import lax
from jax.experimental import pallas as pl
from jax.experimental.pallas import tpu as pltpu
from jax.sharding import PartitionSpec as P

BLOCK = 16
DISP = 4
HALO = DISP * BLOCK
RC = 4


def exchange(x, axis, dim, width):
    count = lax.axis_size(axis)
    forward = [(i, i + 1) for i in range(count - 1)]
    backward = [(i + 1, i) for i in range(count - 1)]
    size = x.shape[dim]
    low = lax.ppermute(lax.slice_in_dim(x, size - width, size, axis=dim), axis, forward)
    high = lax.ppermute(lax.slice_in_dim(x, 0, width, axis=dim), axis, backward)
    return low, high


def ring(x):
    left, right = exchange(x, "col", 1, 1)
    last = x.shape[0] - 1
    count = lax.axis_size("row")
    forward = [(i, i + 1) for i in range(count - 1)]
    backward = [(i + 1, i) for i in range(count - 1)]
    down = jnp.concatenate([left[last:], x[last:], right[last:]], axis=1)
    up = jnp.concatenate([left[:1], x[:1], right[:1]], axis=1)
    top = lax.ppermute(down, "row", forward)[0]
    bottom = lax.ppermute(up, "row", backward)[0]
    width = x.shape[1]
    side_l = jnp.concatenate([top[:1], left[:, 0], bottom[:1]], axis=0)
    side_r = jnp.concatenate([top[width + 1:], right[:, 0], bottom[width + 1:]], axis=0)
    return side_l, side_r, top, bottom


def warp_kernel(srel_ref, *refs):
    hbm = refs[:11]
    out_ref = refs[11]
    vmem = refs[12:21]
    sem = refs[21]
    c_hbm, le_hbm, lm_hbm, re_hbm, rm_hbm = hbm[:5]
    edge = le_hbm.shape[0] // 2
    pairs = []
    for e_hbm, m_hbm, v in ((le_hbm, lm_hbm, vmem[1]), (re_hbm, rm_hbm, vmem[2])):
        tall = v.shape[0]
        pairs += [
            (e_hbm.at[pl.ds(0, edge)], v.at[pl.ds(0, edge)]),
            (e_hbm.at[pl.ds(edge, edge)], v.at[pl.ds(tall - edge, edge)]),
            (m_hbm, v.at[pl.ds(edge, tall - 2 * edge)]),
        ]
    pairs = [(c_hbm, vmem[0])] + pairs + list(zip(hbm[5:], vmem[3:]))
    copies = [pltpu.make_async_copy(h, v, sem.at[n]) for n, (h, v) in enumerate(pairs)]
    for c in copies:
        c.start()
    for c in copies:
        c.wait()
    c_ref, l_ref, r_ref, t_ref, b_ref, tl_ref, tr_ref, bl_ref, br_ref = vmem
    tile_h, per_row = c_ref.shape[0], c_ref.shape[1]
    side = l_ref.shape[1]

    def gather(k, carry):
        i = k // per_row
        j = k % per_row
        r0 = srel_ref[2 * k] * BLOCK
        cb = srel_ref[2 * k + 1]
        rows = pl.ds(i * BLOCK, BLOCK)
        above = r0 < 0
        below = r0 >= tile_h
        middle = jnp.logical_not(above | below)
        west = cb < 0
        east = cb >= per_row
        centre = jnp.logical_not(west | east)
        cases = (
            (above & west, tl_ref, r0 + HALO, cb + side),
            (above & centre, t_ref, r0 + HALO, cb),
            (above & east, tr_ref, r0 + HALO, cb - per_row),
            (middle & west, l_ref, r0, cb + side),
            (middle & centre, c_ref, r0, cb),
            (middle & east, r_ref, r0, cb - per_row),
            (below & west, bl_ref, r0 - tile_h, cb + side),
            (below & centre, b_ref, r0 - tile_h, cb),
            (below & east, br_ref, r0 - tile_h, cb - per_row),
        )
        for cond, ref, rr, cc in cases:
            @pl.when(cond)
            def _():
                out_ref[rows, j] = ref[pl.ds(rr, BLOCK), cc]

        return carry

    lax.fori_loop(0, tile_h // BLOCK * per_row, gather, 0)


def warp(srel, pieces):
    def blocked(x):
        return x.reshape(x.shape[0], x.shape[1] // BLOCK, BLOCK, x.shape[2])

    parts = [blocked(x) for x in pieces]
    any_spec = pl.BlockSpec(memory_space=pl.ANY)
    shape = parts[0].shape
    side = parts[1].shape[1:]
    vmem = [parts[0].shape, (shape[0],) + side, (shape[0],) + side] + [x.shape for x in parts[5:]]
    out = pl.pallas_call(
        warp_kernel,
        grid_spec=pltpu.PrefetchScalarGridSpec(
            num_scalar_prefetch=1,
            grid=(1,),
            in_specs=[any_spec] * len(parts),
            out_specs=pl.BlockSpec(shape, lambda g, s: (0, 0, 0, 0)),
            scratch_shapes=[pltpu.VMEM(v, parts[0].dtype) for v in vmem]
            + [pltpu.SemaphoreType.DMA((len(parts) + 2,))],
        ),
        out_shape=jax.ShapeDtypeStruct(shape, pieces[0].dtype),
        compiler_params=pltpu.CompilerParams(vmem_limit_bytes=60 * 1024 * 1024),
    )(srel, *parts)
    return out.reshape(pieces[0].shape)


OFF = 8


def windows(band, bands, height, sources, sem):
    def copies(which, slot, lo, hi):
        src = pl.ds(which * height - 1 + lo, height + 2 - lo - hi)
        dst = pl.ds(lo, height + 2 - lo - hi)
        return [
            pltpu.make_async_copy(x_hbm.at[src], buf.at[slot, dst], sem.at[n, slot])
            for n, (x_hbm, buf, _, _) in enumerate(sources)
        ]

    def each_case(which, slot, fn):
        first = which == 0
        last = which == bands - 1

        @pl.when(first)
        def _():
            fn(copies(which, slot, 1, 0))

        @pl.when(last)
        def _():
            fn(copies(which, slot, 0, 1))

        @pl.when(jnp.logical_not(first | last))
        def _():
            fn(copies(which, slot, 0, 0))

    def start(cs):
        for c in cs:
            c.start()

    def wait(cs):
        for c in cs:
            c.wait()

    @pl.when(band == 0)
    def _():
        each_case(band, 0, start)

    @pl.when(band + 1 < bands)
    def _():
        each_case(band + 1, (band + 1) % 2, start)

    slot = band % 2
    each_case(band, slot, wait)

    span = pl.ds(band * height, height + 2)
    for _, buf, fl, (l_ref, r_ref, t_ref, b_ref) in sources:
        width = buf.shape[2]
        fl[:, pl.ds(OFF, width), :] = buf[slot].astype(jnp.float32)
        fl[:, pl.ds(OFF - 1, 1), :] = l_ref[span].astype(jnp.float32)[:, None, :]
        fl[:, pl.ds(OFF + width, 1), :] = r_ref[span].astype(jnp.float32)[:, None, :]

        @pl.when(band == 0)
        def _():
            fl[0, pl.ds(OFF - 1, width + 2), :] = t_ref[...].astype(jnp.float32)

        @pl.when(band == bands - 1)
        def _():
            fl[height + 1, pl.ds(OFF - 1, width + 2), :] = b_ref[...].astype(jnp.float32)


def depth(src, kern, r0, width):
    acc = jnp.zeros((RC, width, src.shape[2]), jnp.float32)
    for a in range(3):
        for b in range(3):
            acc = acc + src[pl.ds(r0 + a, RC), pl.ds(OFF - 1 + b, width), :] * kern[a, b]
    return acc.astype(jnp.bfloat16).reshape(RC * width, src.shape[2])


def depth_kernel(x_hbm, l_ref, r_ref, t_ref, b_ref, k_ref, out_ref, buf, fl, sem):
    band = pl.program_id(0)
    height, width, ch = out_ref.shape
    windows(band, pl.num_programs(0), height, [(x_hbm, buf, fl, (l_ref, r_ref, t_ref, b_ref))], sem)
    kern = k_ref[...]

    def chunk(step, carry):
        r0 = step * RC
        out_ref[pl.ds(r0, RC)] = depth(fl, kern, r0, width).reshape(RC, width, ch)
        return carry

    lax.fori_loop(0, height // RC, chunk, 0)


def gru_kernel(din_ref, xhid_hbm, hl_ref, hr_ref, ht_ref, hb_ref,
               khid_ref, win_ref, whid_ref, bin_ref, bhid_ref,
               out_ref, hbuf, hfl, sem):
    band = pl.program_id(0)
    height, width, ch = out_ref.shape
    windows(band, pl.num_programs(0), height,
            [(xhid_hbm, hbuf, hfl, (hl_ref, hr_ref, ht_ref, hb_ref))], sem)

    khid = khid_ref[...]
    win = win_ref[...]
    whid = whid_ref[...]
    bin_ = bin_ref[...]
    bhid = bhid_ref[...]

    def chunk(step, carry):
        r0 = step * RC
        d_in = din_ref[pl.ds(r0, RC)].reshape(RC * width, ch)
        d_hid = depth(hfl, khid, r0, width)
        gi = jnp.dot(d_in, win, preferred_element_type=jnp.float32) + bin_
        gh = jnp.dot(d_hid, whid, preferred_element_type=jnp.float32) + bhid
        update = jax.nn.sigmoid(gi[:, :ch] + gh[:, :ch])
        reset = jax.nn.sigmoid(gi[:, ch:2 * ch] + gh[:, ch:2 * ch])
        cand = jnp.tanh(gi[:, 2 * ch:] + reset * gh[:, 2 * ch:])
        prev = hfl[pl.ds(r0 + 1, RC), pl.ds(OFF, width), :].reshape(RC * width, ch)
        new = (1.0 - update) * cand + update * prev
        out_ref[pl.ds(r0, RC)] = new.astype(out_ref.dtype).reshape(RC, width, ch)
        return carry

    lax.fori_loop(0, height // RC, chunk, 0)


def full(shape):
    return pl.BlockSpec(shape, lambda b: (0,) * len(shape))


def window_scratch(width, ch):
    return [
        pltpu.VMEM((2, BLOCK + 2, width, ch), jnp.bfloat16),
        pltpu.VMEM((BLOCK + 2, width + 2 * OFF, ch), jnp.float32),
        pltpu.SemaphoreType.DMA((1, 2)),
    ]


def depth_in(inputs, in_ring, kern_in):
    tile_h, width, ch = inputs.shape
    return pl.pallas_call(
        depth_kernel,
        grid=(tile_h // BLOCK,),
        in_specs=[pl.BlockSpec(memory_space=pl.ANY)]
        + [full(r.shape) for r in in_ring]
        + [full(kern_in.shape)],
        out_specs=pl.BlockSpec((BLOCK, width, ch), lambda b: (b, 0, 0)),
        out_shape=jax.ShapeDtypeStruct((tile_h, width, ch), jnp.bfloat16),
        scratch_shapes=window_scratch(width, ch),
        compiler_params=pltpu.CompilerParams(dimension_semantics=("arbitrary",)),
    )(inputs, *in_ring, kern_in)


def gru(d_in, warped, hid_ring, kern_hid, w_in, w_hid, bias_in, bias_hid):
    tile_h, width, ch = warped.shape
    band_spec = pl.BlockSpec((BLOCK, width, ch), lambda b: (b, 0, 0))
    return pl.pallas_call(
        gru_kernel,
        grid=(tile_h // BLOCK,),
        in_specs=[band_spec, pl.BlockSpec(memory_space=pl.ANY)]
        + [full(r.shape) for r in hid_ring]
        + [
            full(kern_hid.shape),
            full(w_in.shape),
            full(w_hid.shape),
            full((1, w_in.shape[1])),
            full((1, w_hid.shape[1])),
        ],
        out_specs=band_spec,
        out_shape=jax.ShapeDtypeStruct((tile_h, width, ch), jnp.bfloat16),
        scratch_shapes=window_scratch(width, ch),
        compiler_params=pltpu.CompilerParams(dimension_semantics=("arbitrary",)),
    )(d_in, warped, *hid_ring, kern_hid, w_in, w_hid,
      bias_in.reshape(1, -1), bias_hid.reshape(1, -1))


def body(inputs, hidden, motion, kern_in, kern_hid, w_in, w_hid, bias_in, bias_hid):
    tile_h, tile_w, channels = hidden.shape
    block_count_r = tile_h // BLOCK
    block_count_c = tile_w // BLOCK
    row_base = lax.axis_index("row") * block_count_r
    col_base = lax.axis_index("col") * block_count_c
    anchor = jnp.zeros((), jnp.int32)

    edge_rows = jnp.concatenate([hidden[:HALO], hidden[tile_h - HALO:]], axis=0)
    left_edge, right_edge = exchange(edge_rows, "col", 1, HALO)
    top, bottom = exchange(hidden, "row", 0, HALO)
    top_left, bottom_left = exchange(left_edge, "row", 0, HALO)
    top_right, bottom_right = exchange(right_edge, "row", 0, HALO)
    middle, _, _ = lax.optimization_barrier((hidden[HALO:tile_h - HALO], left_edge, right_edge))
    left_mid, right_mid = exchange(middle, "col", 1, HALO)

    sources = lax.dynamic_slice(
        motion, (anchor, row_base, col_base), (2, block_count_r, block_count_c)
    )
    src_r = jnp.clip(sources[0] - row_base, -DISP, block_count_r + DISP - 1)
    src_c = jnp.clip(sources[1] - col_base, -DISP, block_count_c + DISP - 1)
    srel = jnp.stack([src_r, src_c], axis=-1).reshape(-1).astype(jnp.int32)

    d_in = depth_in(inputs, ring(inputs), kern_in)
    warped = warp(
        srel,
        (hidden, left_edge, left_mid, right_edge, right_mid, top, bottom,
         top_left, top_right, bottom_left, bottom_right),
    )
    return gru(d_in, warped, ring(warped), kern_hid, w_in, w_hid, bias_in, bias_hid)


def solution(mesh):
    in_specs = (P("row", "col", None), P("row", "col", None), P(), P(), P(), P(), P(), P(), P())
    out_specs = P("row", "col", None)
    return jax.shard_map(body, mesh=mesh, in_specs=in_specs, out_specs=out_specs, check_vma=False)
```

```python
import jax
import jax.numpy as jnp
from jax import lax
from jax.experimental import pallas as pl
from jax.experimental.pallas import tpu as pltpu
from jax.sharding import PartitionSpec as P

BLOCK = 16
DISP = 4
HALO = DISP * BLOCK
RC = 4


def exchange(x, axis, dim, width):
    count = lax.axis_size(axis)
    forward = [(i, i + 1) for i in range(count - 1)]
    backward = [(i + 1, i) for i in range(count - 1)]
    size = x.shape[dim]
    low = lax.ppermute(lax.slice_in_dim(x, size - width, size, axis=dim), axis, forward)
    high = lax.ppermute(lax.slice_in_dim(x, 0, width, axis=dim), axis, backward)
    return low, high


def ring(x):
    left, right = exchange(x, "col", 1, 1)
    above, below = exchange(x, "row", 0, 1)
    rows = lax.axis_size("row")
    cols = lax.axis_size("col")
    last_r, last_c = x.shape[0] - 1, x.shape[1] - 1

    def diagonal(pixel, dr, dc):
        pairs = [
            (r * cols + c, (r + dr) * cols + c + dc)
            for r in range(rows)
            for c in range(cols)
            if 0 <= r + dr < rows and 0 <= c + dc < cols
        ]
        return lax.ppermute(pixel, ("row", "col"), pairs)

    top_left = diagonal(x[last_r, last_c:], 1, 1)
    top_right = diagonal(x[last_r, :1], 1, -1)
    bottom_left = diagonal(x[0, last_c:], -1, 1)
    bottom_right = diagonal(x[0, :1], -1, -1)
    side_l = jnp.concatenate([top_left, left[:, 0], bottom_left], axis=0)
    side_r = jnp.concatenate([top_right, right[:, 0], bottom_right], axis=0)
    top = jnp.concatenate([top_left, above[0], top_right], axis=0)
    bottom = jnp.concatenate([bottom_left, below[0], bottom_right], axis=0)
    return side_l, side_r, top, bottom


def warp_kernel(srel_ref, *refs):
    hbm = refs[:11]
    out_ref = refs[11]
    vmem = refs[12:21]
    sem = refs[21]
    c_hbm, le_hbm, lm_hbm, re_hbm, rm_hbm = hbm[:5]
    edge = le_hbm.shape[0] // 2
    pairs = []
    for e_hbm, m_hbm, v in ((le_hbm, lm_hbm, vmem[1]), (re_hbm, rm_hbm, vmem[2])):
        tall = v.shape[0]
        pairs += [
            (e_hbm.at[pl.ds(0, edge)], v.at[pl.ds(0, edge)]),
            (e_hbm.at[pl.ds(edge, edge)], v.at[pl.ds(tall - edge, edge)]),
            (m_hbm, v.at[pl.ds(edge, tall - 2 * edge)]),
        ]
    pairs = [(c_hbm, vmem[0])] + pairs + list(zip(hbm[5:], vmem[3:]))
    copies = [pltpu.make_async_copy(h, v, sem.at[n]) for n, (h, v) in enumerate(pairs)]
    for c in copies:
        c.start()
    for c in copies:
        c.wait()
    c_ref, l_ref, r_ref, t_ref, b_ref, tl_ref, tr_ref, bl_ref, br_ref = vmem
    tile_h, per_row = c_ref.shape[0], c_ref.shape[1]
    side = l_ref.shape[1]

    def gather(k, carry):
        i = k // per_row
        j = k % per_row
        r0 = srel_ref[2 * k] * BLOCK
        cb = srel_ref[2 * k + 1]
        rows = pl.ds(i * BLOCK, BLOCK)
        above = r0 < 0
        below = r0 >= tile_h
        middle = jnp.logical_not(above | below)
        west = cb < 0
        east = cb >= per_row
        centre = jnp.logical_not(west | east)
        cases = (
            (above & west, tl_ref, r0 + HALO, cb + side),
            (above & centre, t_ref, r0 + HALO, cb),
            (above & east, tr_ref, r0 + HALO, cb - per_row),
            (middle & west, l_ref, r0, cb + side),
            (middle & centre, c_ref, r0, cb),
            (middle & east, r_ref, r0, cb - per_row),
            (below & west, bl_ref, r0 - tile_h, cb + side),
            (below & centre, b_ref, r0 - tile_h, cb),
            (below & east, br_ref, r0 - tile_h, cb - per_row),
        )
        for cond, ref, rr, cc in cases:
            @pl.when(cond)
            def _():
                out_ref[rows, j] = ref[pl.ds(rr, BLOCK), cc]

        return carry

    lax.fori_loop(0, tile_h // BLOCK * per_row, gather, 0)


def warp(srel, pieces):
    def blocked(x):
        return x.reshape(x.shape[0], x.shape[1] // BLOCK, BLOCK, x.shape[2])

    parts = [blocked(x) for x in pieces]
    any_spec = pl.BlockSpec(memory_space=pl.ANY)
    shape = parts[0].shape
    side = parts[1].shape[1:]
    vmem = [parts[0].shape, (shape[0],) + side, (shape[0],) + side] + [x.shape for x in parts[5:]]
    out = pl.pallas_call(
        warp_kernel,
        grid_spec=pltpu.PrefetchScalarGridSpec(
            num_scalar_prefetch=1,
            grid=(1,),
            in_specs=[any_spec] * len(parts),
            out_specs=pl.BlockSpec(shape, lambda g, s: (0, 0, 0, 0)),
            scratch_shapes=[pltpu.VMEM(v, parts[0].dtype) for v in vmem]
            + [pltpu.SemaphoreType.DMA((len(parts) + 2,))],
        ),
        out_shape=jax.ShapeDtypeStruct(shape, pieces[0].dtype),
        compiler_params=pltpu.CompilerParams(vmem_limit_bytes=60 * 1024 * 1024),
    )(srel, *parts)
    return out.reshape(pieces[0].shape)


OFF = 8


def windows(band, bands, height, sources, sem):
    def copies(which, slot, lo, hi):
        src = pl.ds(which * height - 1 + lo, height + 2 - lo - hi)
        dst = pl.ds(lo, height + 2 - lo - hi)
        return [
            pltpu.make_async_copy(x_hbm.at[src], buf.at[slot, dst], sem.at[n, slot])
            for n, (x_hbm, buf, _, _) in enumerate(sources)
        ]

    def each_case(which, slot, fn):
        first = which == 0
        last = which == bands - 1

        @pl.when(first)
        def _():
            fn(copies(which, slot, 1, 0))

        @pl.when(last)
        def _():
            fn(copies(which, slot, 0, 1))

        @pl.when(jnp.logical_not(first | last))
        def _():
            fn(copies(which, slot, 0, 0))

    def start(cs):
        for c in cs:
            c.start()

    def wait(cs):
        for c in cs:
            c.wait()

    @pl.when(band == 0)
    def _():
        each_case(band, 0, start)

    @pl.when(band + 1 < bands)
    def _():
        each_case(band + 1, (band + 1) % 2, start)

    slot = band % 2
    each_case(band, slot, wait)

    span = pl.ds(band * height, height + 2)
    for _, buf, fl, (l_ref, r_ref, t_ref, b_ref) in sources:
        width = buf.shape[2]
        fl[:, pl.ds(OFF, width), :] = buf[slot].astype(jnp.float32)
        fl[:, pl.ds(OFF - 1, 1), :] = l_ref[span].astype(jnp.float32)[:, None, :]
        fl[:, pl.ds(OFF + width, 1), :] = r_ref[span].astype(jnp.float32)[:, None, :]

        @pl.when(band == 0)
        def _():
            fl[0, pl.ds(OFF - 1, width + 2), :] = t_ref[...].astype(jnp.float32)

        @pl.when(band == bands - 1)
        def _():
            fl[height + 1, pl.ds(OFF - 1, width + 2), :] = b_ref[...].astype(jnp.float32)


def depth(src, kern, r0, width):
    acc = jnp.zeros((RC, width, src.shape[2]), jnp.float32)
    for a in range(3):
        for b in range(3):
            acc = acc + src[pl.ds(r0 + a, RC), pl.ds(OFF - 1 + b, width), :] * kern[a, b]
    return acc.astype(jnp.bfloat16).reshape(RC * width, src.shape[2])


def depth_kernel(x_hbm, l_ref, r_ref, t_ref, b_ref, k_ref, out_ref, buf, fl, sem):
    band = pl.program_id(0)
    height, width, ch = out_ref.shape
    windows(band, pl.num_programs(0), height, [(x_hbm, buf, fl, (l_ref, r_ref, t_ref, b_ref))], sem)
    kern = k_ref[...]

    def chunk(step, carry):
        r0 = step * RC
        out_ref[pl.ds(r0, RC)] = depth(fl, kern, r0, width).reshape(RC, width, ch)
        return carry

    lax.fori_loop(0, height // RC, chunk, 0)


def gru_kernel(din_ref, xhid_hbm, hl_ref, hr_ref, ht_ref, hb_ref,
               khid_ref, win_ref, whid_ref, bin_ref, bhid_ref,
               out_ref, hbuf, hfl, sem):
    band = pl.program_id(0)
    height, width, ch = out_ref.shape
    windows(band, pl.num_programs(0), height,
            [(xhid_hbm, hbuf, hfl, (hl_ref, hr_ref, ht_ref, hb_ref))], sem)

    khid = khid_ref[...]
    win = win_ref[...]
    whid = whid_ref[...]
    bin_ = bin_ref[...]
    bhid = bhid_ref[...]

    def chunk(step, carry):
        r0 = step * RC
        d_in = din_ref[pl.ds(r0, RC)].reshape(RC * width, ch)
        d_hid = depth(hfl, khid, r0, width)
        gi = jnp.dot(d_in, win, preferred_element_type=jnp.float32) + bin_
        gh = jnp.dot(d_hid, whid, preferred_element_type=jnp.float32) + bhid
        update = jax.nn.sigmoid(gi[:, :ch] + gh[:, :ch])
        reset = jax.nn.sigmoid(gi[:, ch:2 * ch] + gh[:, ch:2 * ch])
        cand = jnp.tanh(gi[:, 2 * ch:] + reset * gh[:, 2 * ch:])
        prev = hfl[pl.ds(r0 + 1, RC), pl.ds(OFF, width), :].reshape(RC * width, ch)
        new = (1.0 - update) * cand + update * prev
        out_ref[pl.ds(r0, RC)] = new.astype(out_ref.dtype).reshape(RC, width, ch)
        return carry

    lax.fori_loop(0, height // RC, chunk, 0)


def full(shape):
    return pl.BlockSpec(shape, lambda b: (0,) * len(shape))


def window_scratch(width, ch):
    return [
        pltpu.VMEM((2, BLOCK + 2, width, ch), jnp.bfloat16),
        pltpu.VMEM((BLOCK + 2, width + 2 * OFF, ch), jnp.float32),
        pltpu.SemaphoreType.DMA((1, 2)),
    ]


def depth_in(inputs, in_ring, kern_in):
    tile_h, width, ch = inputs.shape
    return pl.pallas_call(
        depth_kernel,
        grid=(tile_h // BLOCK,),
        in_specs=[pl.BlockSpec(memory_space=pl.ANY)]
        + [full(r.shape) for r in in_ring]
        + [full(kern_in.shape)],
        out_specs=pl.BlockSpec((BLOCK, width, ch), lambda b: (b, 0, 0)),
        out_shape=jax.ShapeDtypeStruct((tile_h, width, ch), jnp.bfloat16),
        scratch_shapes=window_scratch(width, ch),
        compiler_params=pltpu.CompilerParams(dimension_semantics=("arbitrary",)),
    )(inputs, *in_ring, kern_in)


def gru(d_in, warped, hid_ring, kern_hid, w_in, w_hid, bias_in, bias_hid):
    tile_h, width, ch = warped.shape
    band_spec = pl.BlockSpec((BLOCK, width, ch), lambda b: (b, 0, 0))
    return pl.pallas_call(
        gru_kernel,
        grid=(tile_h // BLOCK,),
        in_specs=[band_spec, pl.BlockSpec(memory_space=pl.ANY)]
        + [full(r.shape) for r in hid_ring]
        + [
            full(kern_hid.shape),
            full(w_in.shape),
            full(w_hid.shape),
            full((1, w_in.shape[1])),
            full((1, w_hid.shape[1])),
        ],
        out_specs=band_spec,
        out_shape=jax.ShapeDtypeStruct((tile_h, width, ch), jnp.bfloat16),
        scratch_shapes=window_scratch(width, ch),
        compiler_params=pltpu.CompilerParams(dimension_semantics=("arbitrary",)),
    )(d_in, warped, *hid_ring, kern_hid, w_in, w_hid,
      bias_in.reshape(1, -1), bias_hid.reshape(1, -1))


def body(inputs, hidden, motion, kern_in, kern_hid, w_in, w_hid, bias_in, bias_hid):
    tile_h, tile_w, channels = hidden.shape
    block_count_r = tile_h // BLOCK
    block_count_c = tile_w // BLOCK
    row_base = lax.axis_index("row") * block_count_r
    col_base = lax.axis_index("col") * block_count_c
    anchor = jnp.zeros((), jnp.int32)

    in_ring = ring(inputs)
    edge_rows = jnp.concatenate([hidden[:HALO], hidden[tile_h - HALO:]], axis=0)
    edge_rows, held, _ = lax.optimization_barrier((edge_rows, hidden, in_ring))
    left_edge, right_edge = exchange(edge_rows, "col", 1, HALO)
    left_mid, right_mid = exchange(held[HALO:tile_h - HALO], "col", 1, HALO)
    top, bottom = exchange(held, "row", 0, HALO)
    top_left, bottom_left = exchange(left_edge, "row", 0, HALO)
    top_right, bottom_right = exchange(right_edge, "row", 0, HALO)

    sources = lax.dynamic_slice(
        motion, (anchor, row_base, col_base), (2, block_count_r, block_count_c)
    )
    src_r = jnp.clip(sources[0] - row_base, -DISP, block_count_r + DISP - 1)
    src_c = jnp.clip(sources[1] - col_base, -DISP, block_count_c + DISP - 1)
    srel = jnp.stack([src_r, src_c], axis=-1).reshape(-1).astype(jnp.int32)

    d_in = depth_in(inputs, in_ring, kern_in)
    warped = warp(
        srel,
        (hidden, left_edge, left_mid, right_edge, right_mid, top, bottom,
         top_left, top_right, bottom_left, bottom_right),
    )
    return gru(d_in, warped, ring(warped), kern_hid, w_in, w_hid, bias_in, bias_hid)


def solution(mesh):
    in_specs = (P("row", "col", None), P("row", "col", None), P(), P(), P(), P(), P(), P(), P())
    out_specs = P("row", "col", None)
    return jax.shard_map(body, mesh=mesh, in_specs=in_specs, out_specs=out_specs, check_vma=False)
```

```python
import jax
import jax.numpy as jnp
from jax import lax
from jax.experimental import pallas as pl
from jax.experimental.pallas import tpu as pltpu
from jax.sharding import PartitionSpec as P

BLOCK = 16
DISP = 4
HALO = DISP * BLOCK
RC = 4


def exchange(x, axis, dim, width):
    count = lax.axis_size(axis)
    forward = [(i, i + 1) for i in range(count - 1)]
    backward = [(i + 1, i) for i in range(count - 1)]
    size = x.shape[dim]
    low = lax.ppermute(lax.slice_in_dim(x, size - width, size, axis=dim), axis, forward)
    high = lax.ppermute(lax.slice_in_dim(x, 0, width, axis=dim), axis, backward)
    return low, high


def ring(x, left=None, right=None):
    if left is None:
        left, right = exchange(x, "col", 1, 1)
    last = x.shape[0] - 1
    count = lax.axis_size("row")
    forward = [(i, i + 1) for i in range(count - 1)]
    backward = [(i + 1, i) for i in range(count - 1)]
    down = jnp.concatenate([left[last:], x[last:], right[last:]], axis=1)
    up = jnp.concatenate([left[:1], x[:1], right[:1]], axis=1)
    top = lax.ppermute(down, "row", forward)[0]
    bottom = lax.ppermute(up, "row", backward)[0]
    width = x.shape[1]
    side_l = jnp.concatenate([top[:1], left[:, 0], bottom[:1]], axis=0)
    side_r = jnp.concatenate([top[width + 1:], right[:, 0], bottom[width + 1:]], axis=0)
    return side_l, side_r, top, bottom


def warp_kernel(srel_ref, *refs):
    c_hbm, le_hbm, lm_hbm, re_hbm, rm_hbm, t_hbm, b_hbm = refs[:7]
    out_ref = refs[7]
    c_ref, l_ref, r_ref, t_ref, b_ref = refs[8:13]
    sem = refs[13]
    edge = le_hbm.shape[0] // 2
    tile_h, per_row = c_ref.shape[0], c_ref.shape[1]
    pairs = [(c_hbm, c_ref), (t_hbm, t_ref), (b_hbm, b_ref)]
    for e_hbm, m_hbm, v in ((le_hbm, lm_hbm, l_ref), (re_hbm, rm_hbm, r_ref)):
        pairs += [
            (e_hbm.at[pl.ds(0, edge)], v.at[pl.ds(0, edge)]),
            (e_hbm.at[pl.ds(edge, edge)], v.at[pl.ds(tile_h - edge, edge)]),
            (m_hbm, v.at[pl.ds(edge, tile_h - 2 * edge)]),
        ]
    copies = [pltpu.make_async_copy(h, v, sem.at[n]) for n, (h, v) in enumerate(pairs)]
    for c in copies:
        c.start()
    for c in copies:
        c.wait()
    side = l_ref.shape[1]

    def gather(k, carry):
        i = k // per_row
        j = k % per_row
        r0 = srel_ref[2 * k] * BLOCK
        cb = srel_ref[2 * k + 1]
        rows = pl.ds(i * BLOCK, BLOCK)
        above = r0 < 0
        below = r0 >= tile_h
        middle = jnp.logical_not(above | below)
        west = cb < 0
        east = cb >= per_row
        centre = jnp.logical_not(west | east)
        cases = (
            (above, t_ref, r0 + HALO, cb + side),
            (below, b_ref, r0 - tile_h, cb + side),
            (middle & west, l_ref, r0, cb + side),
            (middle & centre, c_ref, r0, cb),
            (middle & east, r_ref, r0, cb - per_row),
        )
        for cond, ref, rr, cc in cases:
            @pl.when(cond)
            def _():
                out_ref[rows, j] = ref[pl.ds(rr, BLOCK), cc]

        return carry

    lax.fori_loop(0, tile_h // BLOCK * per_row, gather, 0)


def warp(srel, pieces):
    def blocked(x):
        return x.reshape(x.shape[0], x.shape[1] // BLOCK, BLOCK, x.shape[2])

    parts = [blocked(x) for x in pieces]
    any_spec = pl.BlockSpec(memory_space=pl.ANY)
    shape = parts[0].shape
    side = parts[1].shape[1:]
    vmem = [shape, (shape[0],) + side, (shape[0],) + side, parts[5].shape, parts[6].shape]
    out = pl.pallas_call(
        warp_kernel,
        grid_spec=pltpu.PrefetchScalarGridSpec(
            num_scalar_prefetch=1,
            grid=(1,),
            in_specs=[any_spec] * len(parts),
            out_specs=pl.BlockSpec(shape, lambda g, s: (0, 0, 0, 0)),
            scratch_shapes=[pltpu.VMEM(v, parts[0].dtype) for v in vmem]
            + [pltpu.SemaphoreType.DMA((9,))],
        ),
        out_shape=jax.ShapeDtypeStruct(shape, pieces[0].dtype),
        compiler_params=pltpu.CompilerParams(vmem_limit_bytes=60 * 1024 * 1024),
    )(srel, *parts)
    return out.reshape(pieces[0].shape)


OFF = 8


def windows(band, bands, height, sources, sem):
    def copies(which, slot, lo, hi):
        src = pl.ds(which * height - 1 + lo, height + 2 - lo - hi)
        dst = pl.ds(lo, height + 2 - lo - hi)
        return [
            pltpu.make_async_copy(x_hbm.at[src], buf.at[slot, dst], sem.at[n, slot])
            for n, (x_hbm, buf, _, _) in enumerate(sources)
        ]

    def each_case(which, slot, fn):
        first = which == 0
        last = which == bands - 1

        @pl.when(first)
        def _():
            fn(copies(which, slot, 1, 0))

        @pl.when(last)
        def _():
            fn(copies(which, slot, 0, 1))

        @pl.when(jnp.logical_not(first | last))
        def _():
            fn(copies(which, slot, 0, 0))

    def start(cs):
        for c in cs:
            c.start()

    def wait(cs):
        for c in cs:
            c.wait()

    @pl.when(band == 0)
    def _():
        each_case(band, 0, start)

    @pl.when(band + 1 < bands)
    def _():
        each_case(band + 1, (band + 1) % 2, start)

    slot = band % 2
    each_case(band, slot, wait)

    span = pl.ds(band * height, height + 2)
    for _, buf, fl, (l_ref, r_ref, t_ref, b_ref) in sources:
        width = buf.shape[2]
        fl[:, pl.ds(OFF, width), :] = buf[slot].astype(jnp.float32)
        fl[:, pl.ds(OFF - 1, 1), :] = l_ref[span].astype(jnp.float32)[:, None, :]
        fl[:, pl.ds(OFF + width, 1), :] = r_ref[span].astype(jnp.float32)[:, None, :]

        @pl.when(band == 0)
        def _():
            fl[0, pl.ds(OFF - 1, width + 2), :] = t_ref[...].astype(jnp.float32)

        @pl.when(band == bands - 1)
        def _():
            fl[height + 1, pl.ds(OFF - 1, width + 2), :] = b_ref[...].astype(jnp.float32)


def depth(src, kern, r0, width):
    acc = jnp.zeros((RC, width, src.shape[2]), jnp.float32)
    for a in range(3):
        for b in range(3):
            acc = acc + src[pl.ds(r0 + a, RC), pl.ds(OFF - 1 + b, width), :] * kern[a, b]
    return acc.astype(jnp.bfloat16).reshape(RC * width, src.shape[2])


def depth_kernel(x_hbm, l_ref, r_ref, t_ref, b_ref, k_ref, out_ref, buf, fl, sem):
    band = pl.program_id(0)
    height, width, ch = out_ref.shape
    windows(band, pl.num_programs(0), height, [(x_hbm, buf, fl, (l_ref, r_ref, t_ref, b_ref))], sem)
    kern = k_ref[...]

    def chunk(step, carry):
        r0 = step * RC
        out_ref[pl.ds(r0, RC)] = depth(fl, kern, r0, width).reshape(RC, width, ch)
        return carry

    lax.fori_loop(0, height // RC, chunk, 0)


def gru_kernel(din_ref, xhid_hbm, hl_ref, hr_ref, ht_ref, hb_ref,
               khid_ref, win_ref, whid_ref, bin_ref, bhid_ref,
               out_ref, hbuf, hfl, sem):
    band = pl.program_id(0)
    height, width, ch = out_ref.shape
    windows(band, pl.num_programs(0), height,
            [(xhid_hbm, hbuf, hfl, (hl_ref, hr_ref, ht_ref, hb_ref))], sem)

    khid = khid_ref[...]
    win = win_ref[...]
    whid = whid_ref[...]
    bin_ = bin_ref[...]
    bhid = bhid_ref[...]

    def chunk(step, carry):
        r0 = step * RC
        d_in = din_ref[pl.ds(r0, RC)].reshape(RC * width, ch)
        d_hid = depth(hfl, khid, r0, width)
        gi = jnp.dot(d_in, win, preferred_element_type=jnp.float32) + bin_
        gh = jnp.dot(d_hid, whid, preferred_element_type=jnp.float32) + bhid
        update = jax.nn.sigmoid(gi[:, :ch] + gh[:, :ch])
        reset = jax.nn.sigmoid(gi[:, ch:2 * ch] + gh[:, ch:2 * ch])
        cand = jnp.tanh(gi[:, 2 * ch:] + reset * gh[:, 2 * ch:])
        prev = hfl[pl.ds(r0 + 1, RC), pl.ds(OFF, width), :].reshape(RC * width, ch)
        new = (1.0 - update) * cand + update * prev
        out_ref[pl.ds(r0, RC)] = new.astype(out_ref.dtype).reshape(RC, width, ch)
        return carry

    lax.fori_loop(0, height // RC, chunk, 0)


def full(shape):
    return pl.BlockSpec(shape, lambda b: (0,) * len(shape))


def window_scratch(width, ch):
    return [
        pltpu.VMEM((2, BLOCK + 2, width, ch), jnp.bfloat16),
        pltpu.VMEM((BLOCK + 2, width + 2 * OFF, ch), jnp.float32),
        pltpu.SemaphoreType.DMA((1, 2)),
    ]


def depth_in(inputs, in_ring, kern_in):
    tile_h, width, ch = inputs.shape
    return pl.pallas_call(
        depth_kernel,
        grid=(tile_h // BLOCK,),
        in_specs=[pl.BlockSpec(memory_space=pl.ANY)]
        + [full(r.shape) for r in in_ring]
        + [full(kern_in.shape)],
        out_specs=pl.BlockSpec((BLOCK, width, ch), lambda b: (b, 0, 0)),
        out_shape=jax.ShapeDtypeStruct((tile_h, width, ch), jnp.bfloat16),
        scratch_shapes=window_scratch(width, ch),
        compiler_params=pltpu.CompilerParams(dimension_semantics=("arbitrary",)),
    )(inputs, *in_ring, kern_in)


def gru(d_in, warped, hid_ring, kern_hid, w_in, w_hid, bias_in, bias_hid):
    tile_h, width, ch = warped.shape
    band_spec = pl.BlockSpec((BLOCK, width, ch), lambda b: (b, 0, 0))
    return pl.pallas_call(
        gru_kernel,
        grid=(tile_h // BLOCK,),
        in_specs=[band_spec, pl.BlockSpec(memory_space=pl.ANY)]
        + [full(r.shape) for r in hid_ring]
        + [
            full(kern_hid.shape),
            full(w_in.shape),
            full(w_hid.shape),
            full((1, w_in.shape[1])),
            full((1, w_hid.shape[1])),
        ],
        out_specs=band_spec,
        out_shape=jax.ShapeDtypeStruct((tile_h, width, ch), jnp.bfloat16),
        scratch_shapes=window_scratch(width, ch),
        compiler_params=pltpu.CompilerParams(dimension_semantics=("arbitrary",)),
    )(d_in, warped, *hid_ring, kern_hid, w_in, w_hid,
      bias_in.reshape(1, -1), bias_hid.reshape(1, -1))


def body(inputs, hidden, motion, kern_in, kern_hid, w_in, w_hid, bias_in, bias_hid):
    tile_h, tile_w, channels = hidden.shape
    block_count_r = tile_h // BLOCK
    block_count_c = tile_w // BLOCK
    row_base = lax.axis_index("row") * block_count_r
    col_base = lax.axis_index("col") * block_count_c
    anchor = jnp.zeros((), jnp.int32)

    cols = lax.axis_size("col")
    forward = [(i, i + 1) for i in range(cols - 1)]
    backward = [(i + 1, i) for i in range(cols - 1)]
    edge_rows = jnp.concatenate([hidden[:HALO], hidden[tile_h - HALO:]], axis=0)
    half = edge_rows.shape[0]

    def with_column(block, column):
        return jnp.concatenate([block, column.reshape(half, -1, channels)], axis=1)

    from_left = lax.ppermute(
        with_column(edge_rows[:, tile_w - HALO:], inputs[:, tile_w - 1:]), "col", forward
    )
    from_right = lax.ppermute(with_column(edge_rows[:, :HALO], inputs[:, :1]), "col", backward)
    left_mid, right_mid = exchange(hidden[HALO:tile_h - HALO], "col", 1, HALO)
    left_edge = from_left[:, :HALO]
    right_edge = from_right[:, :HALO]
    in_left = from_left[:, HALO:].reshape(tile_h, 1, channels)
    in_right = from_right[:, HALO:].reshape(tile_h, 1, channels)

    def row_message(rows, lo, hi):
        block = jnp.concatenate([left_edge[lo:hi], hidden[rows], right_edge[lo:hi]], axis=1)
        edge = rows.stop - 1 if rows.start else 0
        frame = jnp.concatenate(
            [in_left[edge:edge + 1], inputs[edge:edge + 1], in_right[edge:edge + 1]], axis=1
        )
        frame = jnp.pad(frame, ((0, 0), (0, block.shape[1] - frame.shape[1]), (0, 0)))
        return jnp.concatenate([block, frame], axis=0)

    count = lax.axis_size("row")
    down_pairs = [(i, i + 1) for i in range(count - 1)]
    up_pairs = [(i + 1, i) for i in range(count - 1)]
    from_top = lax.ppermute(
        row_message(slice(tile_h - HALO, tile_h), half - HALO, half), "row", down_pairs
    )
    from_bottom = lax.ppermute(row_message(slice(0, HALO), 0, HALO), "row", up_pairs)
    top = from_top[:HALO]
    bottom = from_bottom[:HALO]
    in_top = from_top[HALO, :tile_w + 2]
    in_bottom = from_bottom[HALO, :tile_w + 2]
    in_ring = (
        jnp.concatenate([in_top[:1], in_left[:, 0], in_bottom[:1]], axis=0),
        jnp.concatenate([in_top[tile_w + 1:], in_right[:, 0], in_bottom[tile_w + 1:]], axis=0),
        in_top,
        in_bottom,
    )

    sources = lax.dynamic_slice(
        motion, (anchor, row_base, col_base), (2, block_count_r, block_count_c)
    )
    src_r = jnp.clip(sources[0] - row_base, -DISP, block_count_r + DISP - 1)
    src_c = jnp.clip(sources[1] - col_base, -DISP, block_count_c + DISP - 1)
    srel = jnp.stack([src_r, src_c], axis=-1).reshape(-1).astype(jnp.int32)

    d_in = depth_in(inputs, in_ring, kern_in)
    warped = warp(
        srel,
        (hidden, left_edge, left_mid, right_edge, right_mid, top, bottom),
    )
    return gru(d_in, warped, ring(warped), kern_hid, w_in, w_hid, bias_in, bias_hid)


def solution(mesh):
    in_specs = (P("row", "col", None), P("row", "col", None), P(), P(), P(), P(), P(), P(), P())
    out_specs = P("row", "col", None)
    return jax.shard_map(body, mesh=mesh, in_specs=in_specs, out_specs=out_specs, check_vma=False)
```

```python
import jax
import jax.numpy as jnp
from jax import lax
from jax.experimental import pallas as pl
from jax.experimental.pallas import tpu as pltpu
from jax.sharding import PartitionSpec as P

BLOCK = 16
DISP = 4
HALO = DISP * BLOCK
RC = 4


def exchange(x, axis, dim, width):
    count = lax.axis_size(axis)
    forward = [(i, i + 1) for i in range(count - 1)]
    backward = [(i + 1, i) for i in range(count - 1)]
    size = x.shape[dim]
    low = lax.ppermute(lax.slice_in_dim(x, size - width, size, axis=dim), axis, forward)
    high = lax.ppermute(lax.slice_in_dim(x, 0, width, axis=dim), axis, backward)
    return low, high


def ring(x):
    left, right = exchange(x, "col", 1, 1)
    last = x.shape[0] - 1
    count = lax.axis_size("row")
    forward = [(i, i + 1) for i in range(count - 1)]
    backward = [(i + 1, i) for i in range(count - 1)]
    down = jnp.concatenate([left[last:], x[last:], right[last:]], axis=1)
    up = jnp.concatenate([left[:1], x[:1], right[:1]], axis=1)
    top = lax.ppermute(down, "row", forward)[0]
    bottom = lax.ppermute(up, "row", backward)[0]
    width = x.shape[1]
    side_l = jnp.concatenate([top[:1], left[:, 0], bottom[:1]], axis=0)
    side_r = jnp.concatenate([top[width + 1:], right[:, 0], bottom[width + 1:]], axis=0)
    return side_l, side_r, top, bottom


def warp_kernel(srel_ref, *refs):
    hbm = refs[:11]
    out_ref = refs[11]
    vmem = refs[12:21]
    sem = refs[21]
    c_hbm, le_hbm, lm_hbm, re_hbm, rm_hbm = hbm[:5]
    edge = le_hbm.shape[0] // 2
    pairs = []
    for e_hbm, m_hbm, v in ((le_hbm, lm_hbm, vmem[1]), (re_hbm, rm_hbm, vmem[2])):
        tall = v.shape[0]
        pairs += [
            (e_hbm.at[pl.ds(0, edge)], v.at[pl.ds(0, edge)]),
            (e_hbm.at[pl.ds(edge, edge)], v.at[pl.ds(tall - edge, edge)]),
            (m_hbm, v.at[pl.ds(edge, tall - 2 * edge)]),
        ]
    pairs = [(c_hbm, vmem[0])] + pairs + list(zip(hbm[5:], vmem[3:]))
    copies = [pltpu.make_async_copy(h, v, sem.at[n]) for n, (h, v) in enumerate(pairs)]
    for c in copies:
        c.start()
    for c in copies:
        c.wait()
    c_ref, l_ref, r_ref, t_ref, b_ref, tl_ref, tr_ref, bl_ref, br_ref = vmem
    tile_h, per_row = c_ref.shape[0], c_ref.shape[1]
    side = l_ref.shape[1]

    def gather(k, carry):
        i = k // per_row
        j = k % per_row
        r0 = srel_ref[2 * k] * BLOCK
        cb = srel_ref[2 * k + 1]
        rows = pl.ds(i * BLOCK, BLOCK)
        above = r0 < 0
        below = r0 >= tile_h
        middle = jnp.logical_not(above | below)
        west = cb < 0
        east = cb >= per_row
        centre = jnp.logical_not(west | east)
        cases = (
            (above & west, tl_ref, r0 + HALO, cb + side),
            (above & centre, t_ref, r0 + HALO, cb),
            (above & east, tr_ref, r0 + HALO, cb - per_row),
            (middle & west, l_ref, r0, cb + side),
            (middle & centre, c_ref, r0, cb),
            (middle & east, r_ref, r0, cb - per_row),
            (below & west, bl_ref, r0 - tile_h, cb + side),
            (below & centre, b_ref, r0 - tile_h, cb),
            (below & east, br_ref, r0 - tile_h, cb - per_row),
        )
        for cond, ref, rr, cc in cases:
            @pl.when(cond)
            def _():
                out_ref[rows, j] = ref[pl.ds(rr, BLOCK), cc]

        return carry

    lax.fori_loop(0, tile_h // BLOCK * per_row, gather, 0)


def warp(srel, pieces):
    def blocked(x):
        return x.reshape(x.shape[0], x.shape[1] // BLOCK, BLOCK, x.shape[2])

    parts = [blocked(x) for x in pieces]
    any_spec = pl.BlockSpec(memory_space=pl.ANY)
    shape = parts[0].shape
    side = parts[1].shape[1:]
    vmem = [parts[0].shape, (shape[0],) + side, (shape[0],) + side] + [x.shape for x in parts[5:]]
    out = pl.pallas_call(
        warp_kernel,
        grid_spec=pltpu.PrefetchScalarGridSpec(
            num_scalar_prefetch=1,
            grid=(1,),
            in_specs=[any_spec] * len(parts),
            out_specs=pl.BlockSpec(shape, lambda g, s: (0, 0, 0, 0)),
            scratch_shapes=[pltpu.VMEM(v, parts[0].dtype) for v in vmem]
            + [pltpu.SemaphoreType.DMA((len(parts) + 2,))],
        ),
        out_shape=jax.ShapeDtypeStruct(shape, pieces[0].dtype),
        compiler_params=pltpu.CompilerParams(vmem_limit_bytes=60 * 1024 * 1024),
    )(srel, *parts)
    return out.reshape(pieces[0].shape)


OFF = 8


def windows(band, bands, height, sources, sem):
    def copies(which, slot, lo, hi):
        src = pl.ds(which * height - 1 + lo, height + 2 - lo - hi)
        dst = pl.ds(lo, height + 2 - lo - hi)
        return [
            pltpu.make_async_copy(x_hbm.at[src], buf.at[slot, dst], sem.at[n, slot])
            for n, (x_hbm, buf, _, _) in enumerate(sources)
        ]

    def each_case(which, slot, fn):
        first = which == 0
        last = which == bands - 1

        @pl.when(first)
        def _():
            fn(copies(which, slot, 1, 0))

        @pl.when(last)
        def _():
            fn(copies(which, slot, 0, 1))

        @pl.when(jnp.logical_not(first | last))
        def _():
            fn(copies(which, slot, 0, 0))

    def start(cs):
        for c in cs:
            c.start()

    def wait(cs):
        for c in cs:
            c.wait()

    @pl.when(band == 0)
    def _():
        each_case(band, 0, start)

    @pl.when(band + 1 < bands)
    def _():
        each_case(band + 1, (band + 1) % 2, start)

    slot = band % 2
    each_case(band, slot, wait)

    span = pl.ds(band * height, height + 2)
    for _, buf, fl, (l_ref, r_ref, t_ref, b_ref) in sources:
        width = buf.shape[2]
        fl[:, pl.ds(OFF, width), :] = buf[slot].astype(jnp.float32)
        fl[:, pl.ds(OFF - 1, 1), :] = l_ref[span].astype(jnp.float32)[:, None, :]
        fl[:, pl.ds(OFF + width, 1), :] = r_ref[span].astype(jnp.float32)[:, None, :]

        @pl.when(band == 0)
        def _():
            fl[0, pl.ds(OFF - 1, width + 2), :] = t_ref[...].astype(jnp.float32)

        @pl.when(band == bands - 1)
        def _():
            fl[height + 1, pl.ds(OFF - 1, width + 2), :] = b_ref[...].astype(jnp.float32)


def depth(src, kern, r0, width):
    acc = jnp.zeros((RC, width, src.shape[2]), jnp.float32)
    for a in range(3):
        for b in range(3):
            acc = acc + src[pl.ds(r0 + a, RC), pl.ds(OFF - 1 + b, width), :] * kern[a, b]
    return acc.astype(jnp.bfloat16).reshape(RC * width, src.shape[2])


def depth_kernel(x_hbm, l_ref, r_ref, t_ref, b_ref, k_ref, out_ref, buf, fl, sem):
    band = pl.program_id(0)
    height, width, ch = out_ref.shape
    windows(band, pl.num_programs(0), height, [(x_hbm, buf, fl, (l_ref, r_ref, t_ref, b_ref))], sem)
    kern = k_ref[...]

    def chunk(step, carry):
        r0 = step * RC
        out_ref[pl.ds(r0, RC)] = depth(fl, kern, r0, width).reshape(RC, width, ch)
        return carry

    lax.fori_loop(0, height // RC, chunk, 0)


def sigmoid(x):
    return 0.5 * jnp.tanh(0.5 * x) + 0.5


def gru_kernel(din_ref, xhid_hbm, hl_ref, hr_ref, ht_ref, hb_ref,
               khid_ref, w_ref, bias_ref,
               out_ref, hbuf, hfl, sem):
    band = pl.program_id(0)
    height, width, ch = out_ref.shape
    windows(band, pl.num_programs(0), height,
            [(xhid_hbm, hbuf, hfl, (hl_ref, hr_ref, ht_ref, hb_ref))], sem)

    khid = khid_ref[...]
    weights = w_ref[...]
    bias = bias_ref[...]

    def chunk(step, carry):
        r0 = step * RC
        d_in = din_ref[pl.ds(r0, RC)].reshape(RC * width, ch)
        d_hid = depth(hfl, khid, r0, width)
        both = jnp.concatenate([d_in, d_hid], axis=1)
        gates = jnp.dot(both, weights, preferred_element_type=jnp.float32) + bias
        update = sigmoid(gates[:, :ch])
        reset = sigmoid(gates[:, ch:2 * ch])
        cand = jnp.tanh(gates[:, 2 * ch:3 * ch] + reset * gates[:, 3 * ch:])
        prev = hfl[pl.ds(r0 + 1, RC), pl.ds(OFF, width), :].reshape(RC * width, ch)
        new = (1.0 - update) * cand + update * prev
        out_ref[pl.ds(r0, RC)] = new.astype(out_ref.dtype).reshape(RC, width, ch)
        return carry

    lax.fori_loop(0, height // RC, chunk, 0)


def full(shape):
    return pl.BlockSpec(shape, lambda b: (0,) * len(shape))


def window_scratch(width, ch):
    return [
        pltpu.VMEM((2, BLOCK + 2, width, ch), jnp.bfloat16),
        pltpu.VMEM((BLOCK + 2, width + 2 * OFF, ch), jnp.float32),
        pltpu.SemaphoreType.DMA((1, 2)),
    ]


def depth_in(inputs, in_ring, kern_in):
    tile_h, width, ch = inputs.shape
    return pl.pallas_call(
        depth_kernel,
        grid=(tile_h // BLOCK,),
        in_specs=[pl.BlockSpec(memory_space=pl.ANY)]
        + [full(r.shape) for r in in_ring]
        + [full(kern_in.shape)],
        out_specs=pl.BlockSpec((BLOCK, width, ch), lambda b: (b, 0, 0)),
        out_shape=jax.ShapeDtypeStruct((tile_h, width, ch), jnp.bfloat16),
        scratch_shapes=window_scratch(width, ch),
        compiler_params=pltpu.CompilerParams(dimension_semantics=("arbitrary",)),
    )(inputs, *in_ring, kern_in)


def gru(d_in, warped, hid_ring, kern_hid, w_in, w_hid, bias_in, bias_hid):
    tile_h, width, ch = warped.shape
    band_spec = pl.BlockSpec((BLOCK, width, ch), lambda b: (b, 0, 0))
    zeros = jnp.zeros((ch, ch), w_in.dtype)
    weights = jnp.concatenate(
        [
            jnp.concatenate([w_in[:, :2 * ch], w_in[:, 2 * ch:], zeros], axis=1),
            jnp.concatenate([w_hid[:, :2 * ch], zeros, w_hid[:, 2 * ch:]], axis=1),
        ],
        axis=0,
    )
    bias = jnp.concatenate(
        [bias_in[:2 * ch] + bias_hid[:2 * ch], bias_in[2 * ch:], bias_hid[2 * ch:]]
    ).reshape(1, -1)
    return pl.pallas_call(
        gru_kernel,
        grid=(tile_h // BLOCK,),
        in_specs=[band_spec, pl.BlockSpec(memory_space=pl.ANY)]
        + [full(r.shape) for r in hid_ring]
        + [full(kern_hid.shape), full(weights.shape), full(bias.shape)],
        out_specs=band_spec,
        out_shape=jax.ShapeDtypeStruct((tile_h, width, ch), jnp.bfloat16),
        scratch_shapes=window_scratch(width, ch),
        compiler_params=pltpu.CompilerParams(dimension_semantics=("arbitrary",)),
    )(d_in, warped, *hid_ring, kern_hid, weights, bias)


def body(inputs, hidden, motion, kern_in, kern_hid, w_in, w_hid, bias_in, bias_hid):
    tile_h, tile_w, channels = hidden.shape
    block_count_r = tile_h // BLOCK
    block_count_c = tile_w // BLOCK
    row_base = lax.axis_index("row") * block_count_r
    col_base = lax.axis_index("col") * block_count_c
    anchor = jnp.zeros((), jnp.int32)

    edge_rows = jnp.concatenate([hidden[:HALO], hidden[tile_h - HALO:]], axis=0)
    left_edge, right_edge = exchange(edge_rows, "col", 1, HALO)
    top, bottom = exchange(hidden, "row", 0, HALO)
    top_left, bottom_left = exchange(left_edge, "row", 0, HALO)
    top_right, bottom_right = exchange(right_edge, "row", 0, HALO)
    middle, _, _ = lax.optimization_barrier((hidden[HALO:tile_h - HALO], left_edge, right_edge))
    left_mid, right_mid = exchange(middle, "col", 1, HALO)

    sources = lax.dynamic_slice(
        motion, (anchor, row_base, col_base), (2, block_count_r, block_count_c)
    )
    src_r = jnp.clip(sources[0] - row_base, -DISP, block_count_r + DISP - 1)
    src_c = jnp.clip(sources[1] - col_base, -DISP, block_count_c + DISP - 1)
    srel = jnp.stack([src_r, src_c], axis=-1).reshape(-1).astype(jnp.int32)

    d_in = depth_in(inputs, ring(inputs), kern_in)
    warped = warp(
        srel,
        (hidden, left_edge, left_mid, right_edge, right_mid, top, bottom,
         top_left, top_right, bottom_left, bottom_right),
    )
    return gru(d_in, warped, ring(warped), kern_hid, w_in, w_hid, bias_in, bias_hid)


def solution(mesh):
    in_specs = (P("row", "col", None), P("row", "col", None), P(), P(), P(), P(), P(), P(), P())
    out_specs = P("row", "col", None)
    return jax.shard_map(body, mesh=mesh, in_specs=in_specs, out_specs=out_specs, check_vma=False)
```

```python
import jax
import jax.numpy as jnp
from jax import lax
from jax.experimental import pallas as pl
from jax.experimental.pallas import tpu as pltpu
from jax.sharding import PartitionSpec as P

BLOCK = 16
DISP = 4
HALO = DISP * BLOCK
RC = 4


def exchange(x, axis, dim, width):
    count = lax.axis_size(axis)
    forward = [(i, i + 1) for i in range(count - 1)]
    backward = [(i + 1, i) for i in range(count - 1)]
    size = x.shape[dim]
    low = lax.ppermute(lax.slice_in_dim(x, size - width, size, axis=dim), axis, forward)
    high = lax.ppermute(lax.slice_in_dim(x, 0, width, axis=dim), axis, backward)
    return low, high


def ring(x):
    left, right = exchange(x, "col", 1, 1)
    last = x.shape[0] - 1
    count = lax.axis_size("row")
    forward = [(i, i + 1) for i in range(count - 1)]
    backward = [(i + 1, i) for i in range(count - 1)]
    down = jnp.concatenate([left[last:], x[last:], right[last:]], axis=1)
    up = jnp.concatenate([left[:1], x[:1], right[:1]], axis=1)
    top = lax.ppermute(down, "row", forward)[0]
    bottom = lax.ppermute(up, "row", backward)[0]
    width = x.shape[1]
    side_l = jnp.concatenate([top[:1], left[:, 0], bottom[:1]], axis=0)
    side_r = jnp.concatenate([top[width + 1:], right[:, 0], bottom[width + 1:]], axis=0)
    return side_l, side_r, top, bottom


def warp_kernel(srel_ref, *refs):
    hbm = refs[:11]
    out_ref = refs[11]
    vmem = refs[12:21]
    sem = refs[21]
    c_hbm, le_hbm, lm_hbm, re_hbm, rm_hbm = hbm[:5]
    edge = le_hbm.shape[0] // 2
    pairs = []
    for e_hbm, m_hbm, v in ((le_hbm, lm_hbm, vmem[1]), (re_hbm, rm_hbm, vmem[2])):
        tall = v.shape[0]
        pairs += [
            (e_hbm.at[pl.ds(0, edge)], v.at[pl.ds(0, edge)]),
            (e_hbm.at[pl.ds(edge, edge)], v.at[pl.ds(tall - edge, edge)]),
            (m_hbm, v.at[pl.ds(edge, tall - 2 * edge)]),
        ]
    pairs = [(c_hbm, vmem[0])] + pairs + list(zip(hbm[5:], vmem[3:]))
    copies = [pltpu.make_async_copy(h, v, sem.at[n]) for n, (h, v) in enumerate(pairs)]
    for c in copies:
        c.start()
    for c in copies:
        c.wait()
    c_ref, l_ref, r_ref, t_ref, b_ref, tl_ref, tr_ref, bl_ref, br_ref = vmem
    tile_h, per_row = c_ref.shape[0], c_ref.shape[1]
    side = l_ref.shape[1]

    def gather(k, carry):
        i = k // per_row
        j = k % per_row
        r0 = srel_ref[2 * k] * BLOCK
        cb = srel_ref[2 * k + 1]
        rows = pl.ds(i * BLOCK, BLOCK)
        above = r0 < 0
        below = r0 >= tile_h
        middle = jnp.logical_not(above | below)
        west = cb < 0
        east = cb >= per_row
        centre = jnp.logical_not(west | east)
        cases = (
            (above & west, tl_ref, r0 + HALO, cb + side),
            (above & centre, t_ref, r0 + HALO, cb),
            (above & east, tr_ref, r0 + HALO, cb - per_row),
            (middle & west, l_ref, r0, cb + side),
            (middle & centre, c_ref, r0, cb),
            (middle & east, r_ref, r0, cb - per_row),
            (below & west, bl_ref, r0 - tile_h, cb + side),
            (below & centre, b_ref, r0 - tile_h, cb),
            (below & east, br_ref, r0 - tile_h, cb - per_row),
        )
        for cond, ref, rr, cc in cases:
            @pl.when(cond)
            def _():
                out_ref[rows, j] = ref[pl.ds(rr, BLOCK), cc]

        return carry

    lax.fori_loop(0, tile_h // BLOCK * per_row, gather, 0)


def warp(srel, pieces):
    def blocked(x):
        return x.reshape(x.shape[0], x.shape[1] // BLOCK, BLOCK, x.shape[2])

    parts = [blocked(x) for x in pieces]
    any_spec = pl.BlockSpec(memory_space=pl.ANY)
    shape = parts[0].shape
    side = parts[1].shape[1:]
    vmem = [parts[0].shape, (shape[0],) + side, (shape[0],) + side] + [x.shape for x in parts[5:]]
    out = pl.pallas_call(
        warp_kernel,
        grid_spec=pltpu.PrefetchScalarGridSpec(
            num_scalar_prefetch=1,
            grid=(1,),
            in_specs=[any_spec] * len(parts),
            out_specs=pl.BlockSpec(shape, lambda g, s: (0, 0, 0, 0)),
            scratch_shapes=[pltpu.VMEM(v, parts[0].dtype) for v in vmem]
            + [pltpu.SemaphoreType.DMA((len(parts) + 2,))],
        ),
        out_shape=jax.ShapeDtypeStruct(shape, pieces[0].dtype),
        compiler_params=pltpu.CompilerParams(vmem_limit_bytes=60 * 1024 * 1024),
    )(srel, *parts)
    return out.reshape(pieces[0].shape)


OFF = 8


def windows(band, bands, height, sources, sem):
    def copies(which, slot, lo, hi):
        src = pl.ds(which * height - 1 + lo, height + 2 - lo - hi)
        dst = pl.ds(lo, height + 2 - lo - hi)
        return [
            pltpu.make_async_copy(x_hbm.at[src], buf.at[slot, dst], sem.at[n, slot])
            for n, (x_hbm, buf, _, _) in enumerate(sources)
        ]

    def each_case(which, slot, fn):
        first = which == 0
        last = which == bands - 1

        @pl.when(first)
        def _():
            fn(copies(which, slot, 1, 0))

        @pl.when(last)
        def _():
            fn(copies(which, slot, 0, 1))

        @pl.when(jnp.logical_not(first | last))
        def _():
            fn(copies(which, slot, 0, 0))

    def start(cs):
        for c in cs:
            c.start()

    def wait(cs):
        for c in cs:
            c.wait()

    @pl.when(band == 0)
    def _():
        each_case(band, 0, start)

    @pl.when(band + 1 < bands)
    def _():
        each_case(band + 1, (band + 1) % 2, start)

    slot = band % 2
    each_case(band, slot, wait)

    span = pl.ds(band * height, height + 2)
    for _, buf, fl, (l_ref, r_ref, t_ref, b_ref) in sources:
        width = buf.shape[2]
        fl[:, pl.ds(OFF, width), :] = buf[slot].astype(jnp.float32)
        fl[:, pl.ds(OFF - 1, 1), :] = l_ref[span].astype(jnp.float32)[:, None, :]
        fl[:, pl.ds(OFF + width, 1), :] = r_ref[span].astype(jnp.float32)[:, None, :]

        @pl.when(band == 0)
        def _():
            fl[0, pl.ds(OFF - 1, width + 2), :] = t_ref[...].astype(jnp.float32)

        @pl.when(band == bands - 1)
        def _():
            fl[height + 1, pl.ds(OFF - 1, width + 2), :] = b_ref[...].astype(jnp.float32)


def depth(src, kern, r0, width):
    acc = jnp.zeros((RC, width, src.shape[2]), jnp.float32)
    for a in range(3):
        for b in range(3):
            acc = acc + src[pl.ds(r0 + a, RC), pl.ds(OFF - 1 + b, width), :] * kern[a, b]
    return acc.astype(jnp.bfloat16).reshape(RC * width, src.shape[2])


def depth_kernel(x_hbm, l_ref, r_ref, t_ref, b_ref, k_ref, out_ref, buf, fl, sem):
    band = pl.program_id(0)
    height, width, ch = out_ref.shape
    windows(band, pl.num_programs(0), height, [(x_hbm, buf, fl, (l_ref, r_ref, t_ref, b_ref))], sem)
    kern = k_ref[...]

    def chunk(step, carry):
        r0 = step * RC
        out_ref[pl.ds(r0, RC)] = depth(fl, kern, r0, width).reshape(RC, width, ch)
        return carry

    lax.fori_loop(0, height // RC, chunk, 0)


def sigmoid(x):
    return 0.5 * jnp.tanh(0.5 * x) + 0.5


def gru_kernel(din_ref, xhid_hbm, hl_ref, hr_ref, ht_ref, hb_ref,
               khid_ref, w_ref, bias_ref,
               out_ref, hbuf, hfl, sem):
    band = pl.program_id(0)
    height, width, ch = out_ref.shape
    windows(band, pl.num_programs(0), height,
            [(xhid_hbm, hbuf, hfl, (hl_ref, hr_ref, ht_ref, hb_ref))], sem)

    khid = khid_ref[...]
    weights = w_ref[...]
    bias = bias_ref[...]

    def chunk(step, carry):
        r0 = step * RC
        d_in = din_ref[pl.ds(r0, RC)].reshape(RC * width, ch)
        d_hid = depth(hfl, khid, r0, width)
        both = jnp.concatenate([d_in, d_hid], axis=1)
        gates = jnp.dot(both, weights, preferred_element_type=jnp.float32) + bias
        update = sigmoid(gates[:, :ch])
        reset = sigmoid(gates[:, ch:2 * ch])
        cand = jnp.tanh(gates[:, 2 * ch:3 * ch] + reset * gates[:, 3 * ch:])
        prev = hfl[pl.ds(r0 + 1, RC), pl.ds(OFF, width), :].reshape(RC * width, ch)
        new = (1.0 - update) * cand + update * prev
        out_ref[pl.ds(r0, RC)] = new.astype(out_ref.dtype).reshape(RC, width, ch)
        return carry

    lax.fori_loop(0, height // RC, chunk, 0)


def full(shape):
    return pl.BlockSpec(shape, lambda b: (0,) * len(shape))


def window_scratch(width, ch):
    return [
        pltpu.VMEM((2, BLOCK + 2, width, ch), jnp.bfloat16),
        pltpu.VMEM((BLOCK + 2, width + 2 * OFF, ch), jnp.float32),
        pltpu.SemaphoreType.DMA((1, 2)),
    ]


def depth_in(inputs, in_ring, kern_in):
    tile_h, width, ch = inputs.shape
    return pl.pallas_call(
        depth_kernel,
        grid=(tile_h // BLOCK,),
        in_specs=[pl.BlockSpec(memory_space=pl.ANY)]
        + [full(r.shape) for r in in_ring]
        + [full(kern_in.shape)],
        out_specs=pl.BlockSpec((BLOCK, width, ch), lambda b: (b, 0, 0)),
        out_shape=jax.ShapeDtypeStruct((tile_h, width, ch), jnp.bfloat16),
        scratch_shapes=window_scratch(width, ch),
        compiler_params=pltpu.CompilerParams(dimension_semantics=("arbitrary",)),
    )(inputs, *in_ring, kern_in)


def gru(d_in, warped, hid_ring, kern_hid, w_in, w_hid, bias_in, bias_hid):
    tile_h, width, ch = warped.shape
    band_spec = pl.BlockSpec((BLOCK, width, ch), lambda b: (b, 0, 0))
    zeros = jnp.zeros((ch, ch), w_in.dtype)
    weights = jnp.concatenate(
        [
            jnp.concatenate([w_in[:, :2 * ch], w_in[:, 2 * ch:], zeros], axis=1),
            jnp.concatenate([w_hid[:, :2 * ch], zeros, w_hid[:, 2 * ch:]], axis=1),
        ],
        axis=0,
    )
    bias = jnp.concatenate(
        [bias_in[:2 * ch] + bias_hid[:2 * ch], bias_in[2 * ch:], bias_hid[2 * ch:]]
    ).reshape(1, -1)
    return pl.pallas_call(
        gru_kernel,
        grid=(tile_h // BLOCK,),
        in_specs=[band_spec, pl.BlockSpec(memory_space=pl.ANY)]
        + [full(r.shape) for r in hid_ring]
        + [full(kern_hid.shape), full(weights.shape), full(bias.shape)],
        out_specs=band_spec,
        out_shape=jax.ShapeDtypeStruct((tile_h, width, ch), jnp.bfloat16),
        scratch_shapes=window_scratch(width, ch),
        compiler_params=pltpu.CompilerParams(dimension_semantics=("arbitrary",)),
    )(d_in, warped, *hid_ring, kern_hid, weights, bias)


def body(inputs, hidden, motion, kern_in, kern_hid, w_in, w_hid, bias_in, bias_hid):
    tile_h, tile_w, channels = hidden.shape
    block_count_r = tile_h // BLOCK
    block_count_c = tile_w // BLOCK
    row_base = lax.axis_index("row") * block_count_r
    col_base = lax.axis_index("col") * block_count_c
    anchor = jnp.zeros((), jnp.int32)

    in_ring = ring(inputs)
    d_in = depth_in(inputs, in_ring, kern_in)
    edge_rows = jnp.concatenate([hidden[:HALO], hidden[tile_h - HALO:]], axis=0)
    edge_rows, held, _ = lax.optimization_barrier((edge_rows, hidden, in_ring))
    left_edge, right_edge = exchange(edge_rows, "col", 1, HALO)
    left_mid, right_mid = exchange(held[HALO:tile_h - HALO], "col", 1, HALO)
    top, bottom = exchange(held, "row", 0, HALO)
    left_c, right_c, d_in = lax.optimization_barrier((left_edge, right_edge, d_in))
    top_left, bottom_left = exchange(left_c, "row", 0, HALO)
    top_right, bottom_right = exchange(right_c, "row", 0, HALO)

    sources = lax.dynamic_slice(
        motion, (anchor, row_base, col_base), (2, block_count_r, block_count_c)
    )
    src_r = jnp.clip(sources[0] - row_base, -DISP, block_count_r + DISP - 1)
    src_c = jnp.clip(sources[1] - col_base, -DISP, block_count_c + DISP - 1)
    srel = jnp.stack([src_r, src_c], axis=-1).reshape(-1).astype(jnp.int32)

    warped = warp(
        srel,
        (hidden, left_edge, left_mid, right_edge, right_mid, top, bottom,
         top_left, top_right, bottom_left, bottom_right),
    )
    return gru(d_in, warped, ring(warped), kern_hid, w_in, w_hid, bias_in, bias_hid)


def solution(mesh):
    in_specs = (P("row", "col", None), P("row", "col", None), P(), P(), P(), P(), P(), P(), P())
    out_specs = P("row", "col", None)
    return jax.shard_map(body, mesh=mesh, in_specs=in_specs, out_specs=out_specs, check_vma=False)
```

```python
import jax
import jax.numpy as jnp
from jax import lax
from jax.experimental import pallas as pl
from jax.experimental.pallas import tpu as pltpu
from jax.sharding import PartitionSpec as P

BLOCK = 16
DISP = 4
HALO = DISP * BLOCK
RC = 4


def exchange(x, axis, dim, width):
    count = lax.axis_size(axis)
    forward = [(i, i + 1) for i in range(count - 1)]
    backward = [(i + 1, i) for i in range(count - 1)]
    size = x.shape[dim]
    low = lax.ppermute(lax.slice_in_dim(x, size - width, size, axis=dim), axis, forward)
    high = lax.ppermute(lax.slice_in_dim(x, 0, width, axis=dim), axis, backward)
    return low, high


def ring(x):
    left, right = exchange(x, "col", 1, 1)
    last = x.shape[0] - 1
    count = lax.axis_size("row")
    forward = [(i, i + 1) for i in range(count - 1)]
    backward = [(i + 1, i) for i in range(count - 1)]
    down = jnp.concatenate([left[last:], x[last:], right[last:]], axis=1)
    up = jnp.concatenate([left[:1], x[:1], right[:1]], axis=1)
    top = lax.ppermute(down, "row", forward)[0]
    bottom = lax.ppermute(up, "row", backward)[0]
    width = x.shape[1]
    side_l = jnp.concatenate([top[:1], left[:, 0], bottom[:1]], axis=0)
    side_r = jnp.concatenate([top[width + 1:], right[:, 0], bottom[width + 1:]], axis=0)
    return side_l, side_r, top, bottom


def warp_kernel(srel_ref, *refs):
    hbm = refs[:11]
    out_ref = refs[11]
    canvas = refs[12]
    sem = refs[13]
    c_hbm, le_hbm, lm_hbm, re_hbm, rm_hbm, t_hbm, b_hbm, tl_hbm, tr_hbm, bl_hbm, br_hbm = hbm
    tile_h, per_row = c_hbm.shape[0], c_hbm.shape[1]
    side = le_hbm.shape[1]
    edge = le_hbm.shape[0] // 2
    band = pl.program_id(0)
    bands = pl.num_programs(0)

    def place(rows, cols):
        return canvas.at[pl.ds(rows[0], rows[1]), pl.ds(cols[0], cols[1])]

    mid = (HALO, tile_h)
    west, centre, east = (0, side), (side, per_row), (side + per_row, side)
    pairs = [
        (c_hbm, place(mid, centre)),
        (le_hbm.at[pl.ds(0, edge)], place((HALO, edge), west)),
        (le_hbm.at[pl.ds(edge, edge)], place((HALO + tile_h - edge, edge), west)),
        (lm_hbm, place((HALO + edge, tile_h - 2 * edge), west)),
        (re_hbm.at[pl.ds(0, edge)], place((HALO, edge), east)),
        (re_hbm.at[pl.ds(edge, edge)], place((HALO + tile_h - edge, edge), east)),
        (rm_hbm, place((HALO + edge, tile_h - 2 * edge), east)),
        (t_hbm, place((0, HALO), centre)),
        (b_hbm, place((HALO + tile_h, HALO), centre)),
        (tl_hbm, place((0, HALO), west)),
        (tr_hbm, place((0, HALO), east)),
        (bl_hbm, place((HALO + tile_h, HALO), west)),
        (br_hbm, place((HALO + tile_h, HALO), east)),
    ]
    copies = [pltpu.make_async_copy(h, v, sem.at[n]) for n, (h, v) in enumerate(pairs)]

    @pl.when(band == 0)
    def _():
        for c in copies:
            c.start()
        for c in copies:
            c.wait()

    def gather(j, carry):
        k = band * per_row + j
        r0 = srel_ref[2 * k] * BLOCK + HALO
        cb = srel_ref[2 * k + 1] + side
        out_ref[:, j] = canvas[pl.ds(r0, BLOCK), cb]
        return carry

    lax.fori_loop(0, per_row, gather, 0, unroll=True)


def warp(srel, pieces):
    def blocked(x):
        return x.reshape(x.shape[0], x.shape[1] // BLOCK, BLOCK, x.shape[2])

    parts = [blocked(x) for x in pieces]
    any_spec = pl.BlockSpec(memory_space=pl.ANY)
    shape = parts[0].shape
    side = parts[1].shape[1]
    canvas = (shape[0] + 2 * HALO, shape[1] + 2 * side) + shape[2:]
    out = pl.pallas_call(
        warp_kernel,
        grid_spec=pltpu.PrefetchScalarGridSpec(
            num_scalar_prefetch=1,
            grid=(shape[0] // BLOCK,),
            in_specs=[any_spec] * len(parts),
            out_specs=pl.BlockSpec((BLOCK,) + shape[1:], lambda g, s: (g, 0, 0, 0)),
            scratch_shapes=[pltpu.VMEM(canvas, parts[0].dtype),
                            pltpu.SemaphoreType.DMA((len(parts) + 2,))],
        ),
        out_shape=jax.ShapeDtypeStruct(shape, pieces[0].dtype),
        compiler_params=pltpu.CompilerParams(
            dimension_semantics=("arbitrary",), vmem_limit_bytes=60 * 1024 * 1024
        ),
    )(srel, *parts)
    return out.reshape(pieces[0].shape)


OFF = 8


def windows(band, bands, height, sources, sem):
    def copies(which, slot, lo, hi):
        src = pl.ds(which * height - 1 + lo, height + 2 - lo - hi)
        dst = pl.ds(lo, height + 2 - lo - hi)
        return [
            pltpu.make_async_copy(x_hbm.at[src], buf.at[slot, dst], sem.at[n, slot])
            for n, (x_hbm, buf, _, _) in enumerate(sources)
        ]

    def each_case(which, slot, fn):
        first = which == 0
        last = which == bands - 1

        @pl.when(first)
        def _():
            fn(copies(which, slot, 1, 0))

        @pl.when(last)
        def _():
            fn(copies(which, slot, 0, 1))

        @pl.when(jnp.logical_not(first | last))
        def _():
            fn(copies(which, slot, 0, 0))

    def start(cs):
        for c in cs:
            c.start()

    def wait(cs):
        for c in cs:
            c.wait()

    @pl.when(band == 0)
    def _():
        each_case(band, 0, start)

    @pl.when(band + 1 < bands)
    def _():
        each_case(band + 1, (band + 1) % 2, start)

    slot = band % 2
    each_case(band, slot, wait)

    span = pl.ds(band * height, height + 2)
    for _, buf, fl, (l_ref, r_ref, t_ref, b_ref) in sources:
        width = buf.shape[2]
        fl[:, pl.ds(OFF, width), :] = buf[slot].astype(jnp.float32)
        fl[:, pl.ds(OFF - 1, 1), :] = l_ref[span].astype(jnp.float32)[:, None, :]
        fl[:, pl.ds(OFF + width, 1), :] = r_ref[span].astype(jnp.float32)[:, None, :]

        @pl.when(band == 0)
        def _():
            fl[0, pl.ds(OFF - 1, width + 2), :] = t_ref[...].astype(jnp.float32)

        @pl.when(band == bands - 1)
        def _():
            fl[height + 1, pl.ds(OFF - 1, width + 2), :] = b_ref[...].astype(jnp.float32)


def depth(src, kern, r0, width):
    acc = jnp.zeros((RC, width, src.shape[2]), jnp.float32)
    for a in range(3):
        for b in range(3):
            acc = acc + src[pl.ds(r0 + a, RC), pl.ds(OFF - 1 + b, width), :] * kern[a, b]
    return acc.astype(jnp.bfloat16).reshape(RC * width, src.shape[2])


def depth_kernel(x_hbm, l_ref, r_ref, t_ref, b_ref, k_ref, out_ref, buf, fl, sem):
    band = pl.program_id(0)
    height, width, ch = out_ref.shape
    windows(band, pl.num_programs(0), height, [(x_hbm, buf, fl, (l_ref, r_ref, t_ref, b_ref))], sem)
    kern = k_ref[...]

    def chunk(step, carry):
        r0 = step * RC
        out_ref[pl.ds(r0, RC)] = depth(fl, kern, r0, width).reshape(RC, width, ch)
        return carry

    lax.fori_loop(0, height // RC, chunk, 0)


def sigmoid(x):
    return 0.5 * jnp.tanh(0.5 * x) + 0.5


def gru_kernel(din_ref, xhid_hbm, hl_ref, hr_ref, ht_ref, hb_ref,
               khid_ref, w_ref, bias_ref,
               out_ref, hbuf, hfl, sem):
    band = pl.program_id(0)
    height, width, ch = out_ref.shape
    windows(band, pl.num_programs(0), height,
            [(xhid_hbm, hbuf, hfl, (hl_ref, hr_ref, ht_ref, hb_ref))], sem)

    khid = khid_ref[...]
    weights = w_ref[...]
    bias = bias_ref[...]

    def chunk(step, carry):
        r0 = step * RC
        d_in = din_ref[pl.ds(r0, RC)].reshape(RC * width, ch)
        d_hid = depth(hfl, khid, r0, width)
        both = jnp.concatenate([d_in, d_hid], axis=1)
        gates = jnp.dot(both, weights, preferred_element_type=jnp.float32) + bias
        update = sigmoid(gates[:, :ch])
        reset = sigmoid(gates[:, ch:2 * ch])
        cand = jnp.tanh(gates[:, 2 * ch:3 * ch] + reset * gates[:, 3 * ch:])
        prev = hfl[pl.ds(r0 + 1, RC), pl.ds(OFF, width), :].reshape(RC * width, ch)
        new = (1.0 - update) * cand + update * prev
        out_ref[pl.ds(r0, RC)] = new.astype(out_ref.dtype).reshape(RC, width, ch)
        return carry

    lax.fori_loop(0, height // RC, chunk, 0)


def full(shape):
    return pl.BlockSpec(shape, lambda b: (0,) * len(shape))


def window_scratch(width, ch):
    return [
        pltpu.VMEM((2, BLOCK + 2, width, ch), jnp.bfloat16),
        pltpu.VMEM((BLOCK + 2, width + 2 * OFF, ch), jnp.float32),
        pltpu.SemaphoreType.DMA((1, 2)),
    ]


def depth_in(inputs, in_ring, kern_in):
    tile_h, width, ch = inputs.shape
    return pl.pallas_call(
        depth_kernel,
        grid=(tile_h // BLOCK,),
        in_specs=[pl.BlockSpec(memory_space=pl.ANY)]
        + [full(r.shape) for r in in_ring]
        + [full(kern_in.shape)],
        out_specs=pl.BlockSpec((BLOCK, width, ch), lambda b: (b, 0, 0)),
        out_shape=jax.ShapeDtypeStruct((tile_h, width, ch), jnp.bfloat16),
        scratch_shapes=window_scratch(width, ch),
        compiler_params=pltpu.CompilerParams(dimension_semantics=("arbitrary",)),
    )(inputs, *in_ring, kern_in)


def gru(d_in, warped, hid_ring, kern_hid, w_in, w_hid, bias_in, bias_hid):
    tile_h, width, ch = warped.shape
    band_spec = pl.BlockSpec((BLOCK, width, ch), lambda b: (b, 0, 0))
    zeros = jnp.zeros((ch, ch), w_in.dtype)
    weights = jnp.concatenate(
        [
            jnp.concatenate([w_in[:, :2 * ch], w_in[:, 2 * ch:], zeros], axis=1),
            jnp.concatenate([w_hid[:, :2 * ch], zeros, w_hid[:, 2 * ch:]], axis=1),
        ],
        axis=0,
    )
    bias = jnp.concatenate(
        [bias_in[:2 * ch] + bias_hid[:2 * ch], bias_in[2 * ch:], bias_hid[2 * ch:]]
    ).reshape(1, -1)
    return pl.pallas_call(
        gru_kernel,
        grid=(tile_h // BLOCK,),
        in_specs=[band_spec, pl.BlockSpec(memory_space=pl.ANY)]
        + [full(r.shape) for r in hid_ring]
        + [full(kern_hid.shape), full(weights.shape), full(bias.shape)],
        out_specs=band_spec,
        out_shape=jax.ShapeDtypeStruct((tile_h, width, ch), jnp.bfloat16),
        scratch_shapes=window_scratch(width, ch),
        compiler_params=pltpu.CompilerParams(dimension_semantics=("arbitrary",)),
    )(d_in, warped, *hid_ring, kern_hid, weights, bias)


def body(inputs, hidden, motion, kern_in, kern_hid, w_in, w_hid, bias_in, bias_hid):
    tile_h, tile_w, channels = hidden.shape
    block_count_r = tile_h // BLOCK
    block_count_c = tile_w // BLOCK
    row_base = lax.axis_index("row") * block_count_r
    col_base = lax.axis_index("col") * block_count_c
    anchor = jnp.zeros((), jnp.int32)

    edge_rows = jnp.concatenate([hidden[:HALO], hidden[tile_h - HALO:]], axis=0)
    left_edge, right_edge = exchange(edge_rows, "col", 1, HALO)
    top, bottom = exchange(hidden, "row", 0, HALO)
    top_left, bottom_left = exchange(left_edge, "row", 0, HALO)
    top_right, bottom_right = exchange(right_edge, "row", 0, HALO)
    middle, _, _ = lax.optimization_barrier((hidden[HALO:tile_h - HALO], left_edge, right_edge))
    left_mid, right_mid = exchange(middle, "col", 1, HALO)

    sources = lax.dynamic_slice(
        motion, (anchor, row_base, col_base), (2, block_count_r, block_count_c)
    )
    src_r = jnp.clip(sources[0] - row_base, -DISP, block_count_r + DISP - 1)
    src_c = jnp.clip(sources[1] - col_base, -DISP, block_count_c + DISP - 1)
    srel = jnp.stack([src_r, src_c], axis=-1).reshape(-1).astype(jnp.int32)

    d_in = depth_in(inputs, ring(inputs), kern_in)
    warped = warp(
        srel,
        (hidden, left_edge, left_mid, right_edge, right_mid, top, bottom,
         top_left, top_right, bottom_left, bottom_right),
    )
    return gru(d_in, warped, ring(warped), kern_hid, w_in, w_hid, bias_in, bias_hid)


def solution(mesh):
    in_specs = (P("row", "col", None), P("row", "col", None), P(), P(), P(), P(), P(), P(), P())
    out_specs = P("row", "col", None)
    return jax.shard_map(body, mesh=mesh, in_specs=in_specs, out_specs=out_specs, check_vma=False)
```

```python
import jax
import jax.numpy as jnp
from jax import lax
from jax.experimental import pallas as pl
from jax.experimental.pallas import tpu as pltpu
from jax.sharding import PartitionSpec as P

BLOCK = 16
DISP = 4
HALO = DISP * BLOCK
RC = 8


def exchange(x, axis, dim, width):
    count = lax.axis_size(axis)
    forward = [(i, i + 1) for i in range(count - 1)]
    backward = [(i + 1, i) for i in range(count - 1)]
    size = x.shape[dim]
    low = lax.ppermute(lax.slice_in_dim(x, size - width, size, axis=dim), axis, forward)
    high = lax.ppermute(lax.slice_in_dim(x, 0, width, axis=dim), axis, backward)
    return low, high


def ring(x):
    left, right = exchange(x, "col", 1, 1)
    last = x.shape[0] - 1
    count = lax.axis_size("row")
    forward = [(i, i + 1) for i in range(count - 1)]
    backward = [(i + 1, i) for i in range(count - 1)]
    down = jnp.concatenate([left[last:], x[last:], right[last:]], axis=1)
    up = jnp.concatenate([left[:1], x[:1], right[:1]], axis=1)
    top = lax.ppermute(down, "row", forward)[0]
    bottom = lax.ppermute(up, "row", backward)[0]
    width = x.shape[1]
    side_l = jnp.concatenate([top[:1], left[:, 0], bottom[:1]], axis=0)
    side_r = jnp.concatenate([top[width + 1:], right[:, 0], bottom[width + 1:]], axis=0)
    return side_l, side_r, top, bottom


def warp_kernel(srel_ref, *refs):
    hbm = refs[:11]
    out_ref = refs[11]
    canvas = refs[12]
    sem = refs[13]
    c_hbm, le_hbm, lm_hbm, re_hbm, rm_hbm, t_hbm, b_hbm, tl_hbm, tr_hbm, bl_hbm, br_hbm = hbm
    tile_h, per_row = c_hbm.shape[0], c_hbm.shape[1]
    side = le_hbm.shape[1]
    edge = le_hbm.shape[0] // 2
    band = pl.program_id(0)
    bands = pl.num_programs(0)

    def place(rows, cols):
        return canvas.at[pl.ds(rows[0], rows[1]), pl.ds(cols[0], cols[1])]

    mid = (HALO, tile_h)
    west, centre, east = (0, side), (side, per_row), (side + per_row, side)
    pairs = [
        (c_hbm, place(mid, centre)),
        (le_hbm.at[pl.ds(0, edge)], place((HALO, edge), west)),
        (le_hbm.at[pl.ds(edge, edge)], place((HALO + tile_h - edge, edge), west)),
        (lm_hbm, place((HALO + edge, tile_h - 2 * edge), west)),
        (re_hbm.at[pl.ds(0, edge)], place((HALO, edge), east)),
        (re_hbm.at[pl.ds(edge, edge)], place((HALO + tile_h - edge, edge), east)),
        (rm_hbm, place((HALO + edge, tile_h - 2 * edge), east)),
        (t_hbm, place((0, HALO), centre)),
        (b_hbm, place((HALO + tile_h, HALO), centre)),
        (tl_hbm, place((0, HALO), west)),
        (tr_hbm, place((0, HALO), east)),
        (bl_hbm, place((HALO + tile_h, HALO), west)),
        (br_hbm, place((HALO + tile_h, HALO), east)),
    ]
    copies = [pltpu.make_async_copy(h, v, sem.at[n]) for n, (h, v) in enumerate(pairs)]

    @pl.when(band == 0)
    def _():
        for c in copies:
            c.start()
        for c in copies:
            c.wait()

    def gather(j, carry):
        k = band * per_row + j
        r0 = srel_ref[2 * k] * BLOCK + HALO
        cb = srel_ref[2 * k + 1] + side
        out_ref[:, j] = canvas[pl.ds(r0, BLOCK), cb]
        return carry

    lax.fori_loop(0, per_row, gather, 0, unroll=True)


def warp(srel, pieces):
    def blocked(x):
        return x.reshape(x.shape[0], x.shape[1] // BLOCK, BLOCK, x.shape[2])

    parts = [blocked(x) for x in pieces]
    any_spec = pl.BlockSpec(memory_space=pl.ANY)
    shape = parts[0].shape
    side = parts[1].shape[1]
    canvas = (shape[0] + 2 * HALO, shape[1] + 2 * side) + shape[2:]
    out = pl.pallas_call(
        warp_kernel,
        grid_spec=pltpu.PrefetchScalarGridSpec(
            num_scalar_prefetch=1,
            grid=(shape[0] // BLOCK,),
            in_specs=[any_spec] * len(parts),
            out_specs=pl.BlockSpec((BLOCK,) + shape[1:], lambda g, s: (g, 0, 0, 0)),
            scratch_shapes=[pltpu.VMEM(canvas, parts[0].dtype),
                            pltpu.SemaphoreType.DMA((len(parts) + 2,))],
        ),
        out_shape=jax.ShapeDtypeStruct(shape, pieces[0].dtype),
        compiler_params=pltpu.CompilerParams(
            dimension_semantics=("arbitrary",), vmem_limit_bytes=60 * 1024 * 1024
        ),
    )(srel, *parts)
    return out.reshape(pieces[0].shape)


OFF = 8


def windows(band, bands, height, sources, sem):
    def copies(which, slot, lo, hi):
        src = pl.ds(which * height - 1 + lo, height + 2 - lo - hi)
        dst = pl.ds(lo, height + 2 - lo - hi)
        return [
            pltpu.make_async_copy(x_hbm.at[src], buf.at[slot, dst], sem.at[n, slot])
            for n, (x_hbm, buf, _, _) in enumerate(sources)
        ]

    def each_case(which, slot, fn):
        first = which == 0
        last = which == bands - 1

        @pl.when(first)
        def _():
            fn(copies(which, slot, 1, 0))

        @pl.when(last)
        def _():
            fn(copies(which, slot, 0, 1))

        @pl.when(jnp.logical_not(first | last))
        def _():
            fn(copies(which, slot, 0, 0))

    def start(cs):
        for c in cs:
            c.start()

    def wait(cs):
        for c in cs:
            c.wait()

    @pl.when(band == 0)
    def _():
        each_case(band, 0, start)

    @pl.when(band + 1 < bands)
    def _():
        each_case(band + 1, (band + 1) % 2, start)

    slot = band % 2
    each_case(band, slot, wait)

    span = pl.ds(band * height, height + 2)
    for _, buf, fl, (l_ref, r_ref, t_ref, b_ref) in sources:
        width = buf.shape[2]
        fl[:, pl.ds(OFF, width), :] = buf[slot].astype(jnp.float32)
        fl[:, pl.ds(OFF - 1, 1), :] = l_ref[span].astype(jnp.float32)[:, None, :]
        fl[:, pl.ds(OFF + width, 1), :] = r_ref[span].astype(jnp.float32)[:, None, :]

        @pl.when(band == 0)
        def _():
            fl[0, pl.ds(OFF - 1, width + 2), :] = t_ref[...].astype(jnp.float32)

        @pl.when(band == bands - 1)
        def _():
            fl[height + 1, pl.ds(OFF - 1, width + 2), :] = b_ref[...].astype(jnp.float32)


def depth(src, kern, r0, width):
    acc = jnp.zeros((RC, width, src.shape[2]), jnp.float32)
    for a in range(3):
        for b in range(3):
            acc = acc + src[pl.ds(r0 + a, RC), pl.ds(OFF - 1 + b, width), :] * kern[a, b]
    return acc.astype(jnp.bfloat16).reshape(RC * width, src.shape[2])


def depth_kernel(x_hbm, l_ref, r_ref, t_ref, b_ref, k_ref, out_ref, buf, fl, sem):
    band = pl.program_id(0)
    height, width, ch = out_ref.shape
    windows(band, pl.num_programs(0), height, [(x_hbm, buf, fl, (l_ref, r_ref, t_ref, b_ref))], sem)
    kern = k_ref[...]

    def chunk(step, carry):
        r0 = step * RC
        out_ref[pl.ds(r0, RC)] = depth(fl, kern, r0, width).reshape(RC, width, ch)
        return carry

    lax.fori_loop(0, height // RC, chunk, 0)


def sigmoid(x):
    return 0.5 * jnp.tanh(0.5 * x) + 0.5


def gru_kernel(din_ref, xhid_hbm, hl_ref, hr_ref, ht_ref, hb_ref,
               khid_ref, w_ref, bias_ref,
               out_ref, hbuf, hfl, sem):
    band = pl.program_id(0)
    height, width, ch = out_ref.shape
    windows(band, pl.num_programs(0), height,
            [(xhid_hbm, hbuf, hfl, (hl_ref, hr_ref, ht_ref, hb_ref))], sem)

    khid = khid_ref[...]
    weights = w_ref[...]
    bias = bias_ref[...]

    def chunk(step, carry):
        r0 = step * RC
        d_in = din_ref[pl.ds(r0, RC)].reshape(RC * width, ch)
        d_hid = depth(hfl, khid, r0, width)
        both = jnp.concatenate([d_in, d_hid], axis=1)
        gates = jnp.dot(both, weights, preferred_element_type=jnp.float32) + bias
        update = sigmoid(gates[:, :ch])
        reset = sigmoid(gates[:, ch:2 * ch])
        cand = jnp.tanh(gates[:, 2 * ch:3 * ch] + reset * gates[:, 3 * ch:])
        prev = hfl[pl.ds(r0 + 1, RC), pl.ds(OFF, width), :].reshape(RC * width, ch)
        new = cand + update * (prev - cand)
        out_ref[pl.ds(r0, RC)] = new.astype(out_ref.dtype).reshape(RC, width, ch)
        return carry

    lax.fori_loop(0, height // RC, chunk, 0)


def full(shape):
    return pl.BlockSpec(shape, lambda b: (0,) * len(shape))


def window_scratch(width, ch):
    return [
        pltpu.VMEM((2, BLOCK + 2, width, ch), jnp.bfloat16),
        pltpu.VMEM((BLOCK + 2, width + 2 * OFF, ch), jnp.float32),
        pltpu.SemaphoreType.DMA((1, 2)),
    ]


def depth_in(inputs, in_ring, kern_in):
    tile_h, width, ch = inputs.shape
    return pl.pallas_call(
        depth_kernel,
        grid=(tile_h // BLOCK,),
        in_specs=[pl.BlockSpec(memory_space=pl.ANY)]
        + [full(r.shape) for r in in_ring]
        + [full(kern_in.shape)],
        out_specs=pl.BlockSpec((BLOCK, width, ch), lambda b: (b, 0, 0)),
        out_shape=jax.ShapeDtypeStruct((tile_h, width, ch), jnp.bfloat16),
        scratch_shapes=window_scratch(width, ch),
        compiler_params=pltpu.CompilerParams(dimension_semantics=("arbitrary",)),
    )(inputs, *in_ring, kern_in)


def gru(d_in, warped, hid_ring, kern_hid, w_in, w_hid, bias_in, bias_hid):
    tile_h, width, ch = warped.shape
    band_spec = pl.BlockSpec((BLOCK, width, ch), lambda b: (b, 0, 0))
    zeros = jnp.zeros((ch, ch), w_in.dtype)
    weights = jnp.concatenate(
        [
            jnp.concatenate([w_in[:, :2 * ch], w_in[:, 2 * ch:], zeros], axis=1),
            jnp.concatenate([w_hid[:, :2 * ch], zeros, w_hid[:, 2 * ch:]], axis=1),
        ],
        axis=0,
    )
    bias = jnp.concatenate(
        [bias_in[:2 * ch] + bias_hid[:2 * ch], bias_in[2 * ch:], bias_hid[2 * ch:]]
    ).reshape(1, -1)
    return pl.pallas_call(
        gru_kernel,
        grid=(tile_h // BLOCK,),
        in_specs=[band_spec, pl.BlockSpec(memory_space=pl.ANY)]
        + [full(r.shape) for r in hid_ring]
        + [full(kern_hid.shape), full(weights.shape), full(bias.shape)],
        out_specs=band_spec,
        out_shape=jax.ShapeDtypeStruct((tile_h, width, ch), jnp.bfloat16),
        scratch_shapes=window_scratch(width, ch),
        compiler_params=pltpu.CompilerParams(dimension_semantics=("arbitrary",)),
    )(d_in, warped, *hid_ring, kern_hid, weights, bias)


def body(inputs, hidden, motion, kern_in, kern_hid, w_in, w_hid, bias_in, bias_hid):
    tile_h, tile_w, channels = hidden.shape
    block_count_r = tile_h // BLOCK
    block_count_c = tile_w // BLOCK
    row_base = lax.axis_index("row") * block_count_r
    col_base = lax.axis_index("col") * block_count_c
    anchor = jnp.zeros((), jnp.int32)

    edge_rows = jnp.concatenate([hidden[:HALO], hidden[tile_h - HALO:]], axis=0)
    left_edge, right_edge = exchange(edge_rows, "col", 1, HALO)
    top, bottom = exchange(hidden, "row", 0, HALO)
    top_left, bottom_left = exchange(left_edge, "row", 0, HALO)
    top_right, bottom_right = exchange(right_edge, "row", 0, HALO)
    middle, _, _ = lax.optimization_barrier((hidden[HALO:tile_h - HALO], left_edge, right_edge))
    left_mid, right_mid = exchange(middle, "col", 1, HALO)

    sources = lax.dynamic_slice(
        motion, (anchor, row_base, col_base), (2, block_count_r, block_count_c)
    )
    src_r = jnp.clip(sources[0] - row_base, -DISP, block_count_r + DISP - 1)
    src_c = jnp.clip(sources[1] - col_base, -DISP, block_count_c + DISP - 1)
    srel = jnp.stack([src_r, src_c], axis=-1).reshape(-1).astype(jnp.int32)

    d_in = depth_in(inputs, ring(inputs), kern_in)
    warped = warp(
        srel,
        (hidden, left_edge, left_mid, right_edge, right_mid, top, bottom,
         top_left, top_right, bottom_left, bottom_right),
    )
    return gru(d_in, warped, ring(warped), kern_hid, w_in, w_hid, bias_in, bias_hid)


def solution(mesh):
    in_specs = (P("row", "col", None), P("row", "col", None), P(), P(), P(), P(), P(), P(), P())
    out_specs = P("row", "col", None)
    return jax.shard_map(body, mesh=mesh, in_specs=in_specs, out_specs=out_specs, check_vma=False)
```

```python
import jax
import jax.numpy as jnp
from jax import lax
from jax.experimental import pallas as pl
from jax.experimental.pallas import tpu as pltpu
from jax.sharding import PartitionSpec as P

BLOCK = 16
DISP = 4
HALO = DISP * BLOCK
RC = 8
BAND = 32
WARP_ROWS = 4


def exchange(x, axis, dim, width):
    count = lax.axis_size(axis)
    forward = [(i, i + 1) for i in range(count - 1)]
    backward = [(i + 1, i) for i in range(count - 1)]
    size = x.shape[dim]
    low = lax.ppermute(lax.slice_in_dim(x, size - width, size, axis=dim), axis, forward)
    high = lax.ppermute(lax.slice_in_dim(x, 0, width, axis=dim), axis, backward)
    return low, high


def ring(x):
    left, right = exchange(x, "col", 1, 1)
    last = x.shape[0] - 1
    count = lax.axis_size("row")
    forward = [(i, i + 1) for i in range(count - 1)]
    backward = [(i + 1, i) for i in range(count - 1)]
    down = jnp.concatenate([left[last:], x[last:], right[last:]], axis=1)
    up = jnp.concatenate([left[:1], x[:1], right[:1]], axis=1)
    top = lax.ppermute(down, "row", forward)[0]
    bottom = lax.ppermute(up, "row", backward)[0]
    width = x.shape[1]
    side_l = jnp.concatenate([top[:1], left[:, 0], bottom[:1]], axis=0)
    side_r = jnp.concatenate([top[width + 1:], right[:, 0], bottom[width + 1:]], axis=0)
    return side_l, side_r, top, bottom


def warp_kernel(srel_ref, *refs):
    hbm = refs[:11]
    out_ref = refs[11]
    canvas = refs[12]
    sem = refs[13]
    c_hbm, le_hbm, lm_hbm, re_hbm, rm_hbm, t_hbm, b_hbm, tl_hbm, tr_hbm, bl_hbm, br_hbm = hbm
    tile_h, per_row = c_hbm.shape[0], c_hbm.shape[1]
    side = le_hbm.shape[1]
    edge = le_hbm.shape[0] // 2
    band = pl.program_id(0)
    bands = pl.num_programs(0)

    def place(rows, cols):
        return canvas.at[pl.ds(rows[0], rows[1]), pl.ds(cols[0], cols[1])]

    mid = (HALO, tile_h)
    west, centre, east = (0, side), (side, per_row), (side + per_row, side)
    pairs = [
        (c_hbm, place(mid, centre)),
        (le_hbm.at[pl.ds(0, edge)], place((HALO, edge), west)),
        (le_hbm.at[pl.ds(edge, edge)], place((HALO + tile_h - edge, edge), west)),
        (lm_hbm, place((HALO + edge, tile_h - 2 * edge), west)),
        (re_hbm.at[pl.ds(0, edge)], place((HALO, edge), east)),
        (re_hbm.at[pl.ds(edge, edge)], place((HALO + tile_h - edge, edge), east)),
        (rm_hbm, place((HALO + edge, tile_h - 2 * edge), east)),
        (t_hbm, place((0, HALO), centre)),
        (b_hbm, place((HALO + tile_h, HALO), centre)),
        (tl_hbm, place((0, HALO), west)),
        (tr_hbm, place((0, HALO), east)),
        (bl_hbm, place((HALO + tile_h, HALO), west)),
        (br_hbm, place((HALO + tile_h, HALO), east)),
    ]
    copies = [pltpu.make_async_copy(h, v, sem.at[n]) for n, (h, v) in enumerate(pairs)]

    @pl.when(band == 0)
    def _():
        for c in copies:
            c.start()
        for c in copies:
            c.wait()

    def gather(n, carry):
        k = band * WARP_ROWS * per_row + n
        r0 = srel_ref[2 * k] * BLOCK + HALO
        cb = srel_ref[2 * k + 1] + side
        out_ref[pl.ds((n // per_row) * BLOCK, BLOCK), n % per_row] = canvas[pl.ds(r0, BLOCK), cb]
        return carry

    lax.fori_loop(0, WARP_ROWS * per_row, gather, 0, unroll=True)


def warp(srel, pieces):
    def blocked(x):
        return x.reshape(x.shape[0], x.shape[1] // BLOCK, BLOCK, x.shape[2])

    parts = [blocked(x) for x in pieces]
    any_spec = pl.BlockSpec(memory_space=pl.ANY)
    shape = parts[0].shape
    side = parts[1].shape[1]
    canvas = (shape[0] + 2 * HALO, shape[1] + 2 * side) + shape[2:]
    out = pl.pallas_call(
        warp_kernel,
        grid_spec=pltpu.PrefetchScalarGridSpec(
            num_scalar_prefetch=1,
            grid=(shape[0] // (BLOCK * WARP_ROWS),),
            in_specs=[any_spec] * len(parts),
            out_specs=pl.BlockSpec((BLOCK * WARP_ROWS,) + shape[1:], lambda g, s: (g, 0, 0, 0)),
            scratch_shapes=[pltpu.VMEM(canvas, parts[0].dtype),
                            pltpu.SemaphoreType.DMA((len(parts) + 2,))],
        ),
        out_shape=jax.ShapeDtypeStruct(shape, pieces[0].dtype),
        compiler_params=pltpu.CompilerParams(
            dimension_semantics=("arbitrary",), vmem_limit_bytes=60 * 1024 * 1024
        ),
    )(srel, *parts)
    return out.reshape(pieces[0].shape)


OFF = 8


def windows(band, bands, height, sources, sem):
    def copies(which, slot, lo, hi):
        src = pl.ds(which * height - 1 + lo, height + 2 - lo - hi)
        dst = pl.ds(lo, height + 2 - lo - hi)
        return [
            pltpu.make_async_copy(x_hbm.at[src], buf.at[slot, dst], sem.at[n, slot])
            for n, (x_hbm, buf, _, _) in enumerate(sources)
        ]

    def each_case(which, slot, fn):
        first = which == 0
        last = which == bands - 1

        @pl.when(first)
        def _():
            fn(copies(which, slot, 1, 0))

        @pl.when(last)
        def _():
            fn(copies(which, slot, 0, 1))

        @pl.when(jnp.logical_not(first | last))
        def _():
            fn(copies(which, slot, 0, 0))

    def start(cs):
        for c in cs:
            c.start()

    def wait(cs):
        for c in cs:
            c.wait()

    @pl.when(band == 0)
    def _():
        each_case(band, 0, start)

    @pl.when(band + 1 < bands)
    def _():
        each_case(band + 1, (band + 1) % 2, start)

    slot = band % 2
    each_case(band, slot, wait)

    span = pl.ds(band * height, height + 2)
    for _, buf, fl, (l_ref, r_ref, t_ref, b_ref) in sources:
        width = buf.shape[2]
        fl[:, pl.ds(OFF, width), :] = buf[slot].astype(jnp.float32)
        fl[:, pl.ds(OFF - 1, 1), :] = l_ref[span].astype(jnp.float32)[:, None, :]
        fl[:, pl.ds(OFF + width, 1), :] = r_ref[span].astype(jnp.float32)[:, None, :]

        @pl.when(band == 0)
        def _():
            fl[0, pl.ds(OFF - 1, width + 2), :] = t_ref[...].astype(jnp.float32)

        @pl.when(band == bands - 1)
        def _():
            fl[height + 1, pl.ds(OFF - 1, width + 2), :] = b_ref[...].astype(jnp.float32)


def depth(src, kern, r0, width):
    acc = jnp.zeros((RC, width, src.shape[2]), jnp.float32)
    for a in range(3):
        for b in range(3):
            acc = acc + src[pl.ds(r0 + a, RC), pl.ds(OFF - 1 + b, width), :] * kern[a, b]
    return acc.astype(jnp.bfloat16).reshape(RC * width, src.shape[2])


def depth_kernel(x_hbm, l_ref, r_ref, t_ref, b_ref, k_ref, out_ref, buf, fl, sem):
    band = pl.program_id(0)
    height, width, ch = out_ref.shape
    windows(band, pl.num_programs(0), height, [(x_hbm, buf, fl, (l_ref, r_ref, t_ref, b_ref))], sem)
    kern = k_ref[...]

    def chunk(step, carry):
        r0 = step * RC
        out_ref[pl.ds(r0, RC)] = depth(fl, kern, r0, width).reshape(RC, width, ch)
        return carry

    lax.fori_loop(0, height // RC, chunk, 0)


def sigmoid(x):
    return 0.5 * jnp.tanh(0.5 * x) + 0.5


def gru_kernel(din_ref, xhid_hbm, hl_ref, hr_ref, ht_ref, hb_ref,
               khid_ref, w_ref, bias_ref,
               out_ref, hbuf, hfl, sem):
    band = pl.program_id(0)
    height, width, ch = out_ref.shape
    windows(band, pl.num_programs(0), height,
            [(xhid_hbm, hbuf, hfl, (hl_ref, hr_ref, ht_ref, hb_ref))], sem)

    khid = khid_ref[...]
    weights = w_ref[...]
    bias = bias_ref[...]

    def chunk(step, carry):
        r0 = step * RC
        d_in = din_ref[pl.ds(r0, RC)].reshape(RC * width, ch)
        d_hid = depth(hfl, khid, r0, width)
        both = jnp.concatenate([d_in, d_hid], axis=1)
        gates = jnp.dot(both, weights, preferred_element_type=jnp.float32) + bias
        update = sigmoid(gates[:, :ch])
        reset = sigmoid(gates[:, ch:2 * ch])
        cand = jnp.tanh(gates[:, 2 * ch:3 * ch] + reset * gates[:, 3 * ch:])
        prev = hfl[pl.ds(r0 + 1, RC), pl.ds(OFF, width), :].reshape(RC * width, ch)
        new = cand + update * (prev - cand)
        out_ref[pl.ds(r0, RC)] = new.astype(out_ref.dtype).reshape(RC, width, ch)
        return carry

    lax.fori_loop(0, height // RC, chunk, 0)


def full(shape):
    return pl.BlockSpec(shape, lambda b: (0,) * len(shape))


def window_scratch(width, ch):
    return [
        pltpu.VMEM((2, BAND + 2, width, ch), jnp.bfloat16),
        pltpu.VMEM((BAND + 2, width + 2 * OFF, ch), jnp.float32),
        pltpu.SemaphoreType.DMA((1, 2)),
    ]


def depth_in(inputs, in_ring, kern_in):
    tile_h, width, ch = inputs.shape
    return pl.pallas_call(
        depth_kernel,
        grid=(tile_h // BAND,),
        in_specs=[pl.BlockSpec(memory_space=pl.ANY)]
        + [full(r.shape) for r in in_ring]
        + [full(kern_in.shape)],
        out_specs=pl.BlockSpec((BAND, width, ch), lambda b: (b, 0, 0)),
        out_shape=jax.ShapeDtypeStruct((tile_h, width, ch), jnp.bfloat16),
        scratch_shapes=window_scratch(width, ch),
        compiler_params=pltpu.CompilerParams(dimension_semantics=("arbitrary",)),
    )(inputs, *in_ring, kern_in)


def gru(d_in, warped, hid_ring, kern_hid, w_in, w_hid, bias_in, bias_hid):
    tile_h, width, ch = warped.shape
    band_spec = pl.BlockSpec((BAND, width, ch), lambda b: (b, 0, 0))
    zeros = jnp.zeros((ch, ch), w_in.dtype)
    weights = jnp.concatenate(
        [
            jnp.concatenate([w_in[:, :2 * ch], w_in[:, 2 * ch:], zeros], axis=1),
            jnp.concatenate([w_hid[:, :2 * ch], zeros, w_hid[:, 2 * ch:]], axis=1),
        ],
        axis=0,
    )
    bias = jnp.concatenate(
        [bias_in[:2 * ch] + bias_hid[:2 * ch], bias_in[2 * ch:], bias_hid[2 * ch:]]
    ).reshape(1, -1)
    return pl.pallas_call(
        gru_kernel,
        grid=(tile_h // BAND,),
        in_specs=[band_spec, pl.BlockSpec(memory_space=pl.ANY)]
        + [full(r.shape) for r in hid_ring]
        + [full(kern_hid.shape), full(weights.shape), full(bias.shape)],
        out_specs=band_spec,
        out_shape=jax.ShapeDtypeStruct((tile_h, width, ch), jnp.bfloat16),
        scratch_shapes=window_scratch(width, ch),
        compiler_params=pltpu.CompilerParams(dimension_semantics=("arbitrary",)),
    )(d_in, warped, *hid_ring, kern_hid, weights, bias)


def body(inputs, hidden, motion, kern_in, kern_hid, w_in, w_hid, bias_in, bias_hid):
    tile_h, tile_w, channels = hidden.shape
    block_count_r = tile_h // BLOCK
    block_count_c = tile_w // BLOCK
    row_base = lax.axis_index("row") * block_count_r
    col_base = lax.axis_index("col") * block_count_c
    anchor = jnp.zeros((), jnp.int32)

    edge_rows = jnp.concatenate([hidden[:HALO], hidden[tile_h - HALO:]], axis=0)
    left_edge, right_edge = exchange(edge_rows, "col", 1, HALO)
    top, bottom = exchange(hidden, "row", 0, HALO)
    top_left, bottom_left = exchange(left_edge, "row", 0, HALO)
    top_right, bottom_right = exchange(right_edge, "row", 0, HALO)
    middle, _, _ = lax.optimization_barrier((hidden[HALO:tile_h - HALO], left_edge, right_edge))
    left_mid, right_mid = exchange(middle, "col", 1, HALO)

    sources = lax.dynamic_slice(
        motion, (anchor, row_base, col_base), (2, block_count_r, block_count_c)
    )
    src_r = jnp.clip(sources[0] - row_base, -DISP, block_count_r + DISP - 1)
    src_c = jnp.clip(sources[1] - col_base, -DISP, block_count_c + DISP - 1)
    srel = jnp.stack([src_r, src_c], axis=-1).reshape(-1).astype(jnp.int32)

    d_in = depth_in(inputs, ring(inputs), kern_in)
    warped = warp(
        srel,
        (hidden, left_edge, left_mid, right_edge, right_mid, top, bottom,
         top_left, top_right, bottom_left, bottom_right),
    )
    return gru(d_in, warped, ring(warped), kern_hid, w_in, w_hid, bias_in, bias_hid)


def solution(mesh):
    in_specs = (P("row", "col", None), P("row", "col", None), P(), P(), P(), P(), P(), P(), P())
    out_specs = P("row", "col", None)
    return jax.shard_map(body, mesh=mesh, in_specs=in_specs, out_specs=out_specs, check_vma=False)
```

```python
import jax
import jax.numpy as jnp
from jax import lax
from jax.experimental import pallas as pl
from jax.experimental.pallas import tpu as pltpu
from jax.sharding import PartitionSpec as P

BLOCK = 16
DISP = 4
HALO = DISP * BLOCK
RC = 8
BAND = 32
WARP_ROWS = 4


def exchange(x, axis, dim, width):
    count = lax.axis_size(axis)
    forward = [(i, i + 1) for i in range(count - 1)]
    backward = [(i + 1, i) for i in range(count - 1)]
    size = x.shape[dim]
    low = lax.ppermute(lax.slice_in_dim(x, size - width, size, axis=dim), axis, forward)
    high = lax.ppermute(lax.slice_in_dim(x, 0, width, axis=dim), axis, backward)
    return low, high


def ring(x):
    left, right = exchange(x, "col", 1, 1)
    last = x.shape[0] - 1
    count = lax.axis_size("row")
    forward = [(i, i + 1) for i in range(count - 1)]
    backward = [(i + 1, i) for i in range(count - 1)]
    down = jnp.concatenate([left[last:], x[last:], right[last:]], axis=1)
    up = jnp.concatenate([left[:1], x[:1], right[:1]], axis=1)
    top = lax.ppermute(down, "row", forward)[0]
    bottom = lax.ppermute(up, "row", backward)[0]
    width = x.shape[1]
    side_l = jnp.concatenate([top[:1], left[:, 0], bottom[:1]], axis=0)
    side_r = jnp.concatenate([top[width + 1:], right[:, 0], bottom[width + 1:]], axis=0)
    return side_l, side_r, top, bottom


def warp_kernel(srel_ref, *refs):
    hbm = refs[:11]
    out_ref = refs[11]
    canvas = refs[12]
    sem = refs[13]
    c_hbm, le_hbm, lm_hbm, re_hbm, rm_hbm, t_hbm, b_hbm, tl_hbm, tr_hbm, bl_hbm, br_hbm = hbm
    tile_h, per_row = c_hbm.shape[0], c_hbm.shape[1]
    side = le_hbm.shape[1]
    edge = le_hbm.shape[0] // 2
    band = pl.program_id(0)
    bands = pl.num_programs(0)

    def place(rows, cols):
        return canvas.at[pl.ds(rows[0], rows[1]), pl.ds(cols[0], cols[1])]

    mid = (HALO, tile_h)
    west, centre, east = (0, side), (side, per_row), (side + per_row, side)
    pairs = [
        (c_hbm, place(mid, centre)),
        (le_hbm.at[pl.ds(0, edge)], place((HALO, edge), west)),
        (le_hbm.at[pl.ds(edge, edge)], place((HALO + tile_h - edge, edge), west)),
        (lm_hbm, place((HALO + edge, tile_h - 2 * edge), west)),
        (re_hbm.at[pl.ds(0, edge)], place((HALO, edge), east)),
        (re_hbm.at[pl.ds(edge, edge)], place((HALO + tile_h - edge, edge), east)),
        (rm_hbm, place((HALO + edge, tile_h - 2 * edge), east)),
        (t_hbm, place((0, HALO), centre)),
        (b_hbm, place((HALO + tile_h, HALO), centre)),
        (tl_hbm, place((0, HALO), west)),
        (tr_hbm, place((0, HALO), east)),
        (bl_hbm, place((HALO + tile_h, HALO), west)),
        (br_hbm, place((HALO + tile_h, HALO), east)),
    ]
    copies = [pltpu.make_async_copy(h, v, sem.at[n]) for n, (h, v) in enumerate(pairs)]

    @pl.when(band == 0)
    def _():
        for c in copies:
            c.start()
        for c in copies:
            c.wait()

    def gather(n, carry):
        k = band * WARP_ROWS * per_row + n
        r0 = srel_ref[2 * k] * BLOCK + HALO
        cb = srel_ref[2 * k + 1] + side
        out_ref[pl.ds((n // per_row) * BLOCK, BLOCK), n % per_row] = canvas[pl.ds(r0, BLOCK), cb]
        return carry

    lax.fori_loop(0, WARP_ROWS * per_row, gather, 0, unroll=True)


def warp(srel, pieces):
    def blocked(x):
        return x.reshape(x.shape[0], x.shape[1] // BLOCK, BLOCK, x.shape[2])

    parts = [blocked(x) for x in pieces]
    any_spec = pl.BlockSpec(memory_space=pl.ANY)
    shape = parts[0].shape
    side = parts[1].shape[1]
    canvas = (shape[0] + 2 * HALO, shape[1] + 2 * side) + shape[2:]
    out = pl.pallas_call(
        warp_kernel,
        grid_spec=pltpu.PrefetchScalarGridSpec(
            num_scalar_prefetch=1,
            grid=(shape[0] // (BLOCK * WARP_ROWS),),
            in_specs=[any_spec] * len(parts),
            out_specs=pl.BlockSpec((BLOCK * WARP_ROWS,) + shape[1:], lambda g, s: (g, 0, 0, 0)),
            scratch_shapes=[pltpu.VMEM(canvas, parts[0].dtype),
                            pltpu.SemaphoreType.DMA((len(parts) + 2,))],
        ),
        out_shape=jax.ShapeDtypeStruct(shape, pieces[0].dtype),
        compiler_params=pltpu.CompilerParams(
            dimension_semantics=("arbitrary",), vmem_limit_bytes=60 * 1024 * 1024
        ),
    )(srel, *parts)
    return out.reshape(pieces[0].shape)


OFF = 8


def windows(band, bands, height, sources, sem):
    def copies(which, slot, lo, hi):
        src = pl.ds(which * height - 1 + lo, height + 2 - lo - hi)
        dst = pl.ds(lo, height + 2 - lo - hi)
        return [
            pltpu.make_async_copy(x_hbm.at[src], buf.at[slot, dst], sem.at[n, slot])
            for n, (x_hbm, buf, _, _) in enumerate(sources)
        ]

    def each_case(which, slot, fn):
        first = which == 0
        last = which == bands - 1

        @pl.when(first)
        def _():
            fn(copies(which, slot, 1, 0))

        @pl.when(last)
        def _():
            fn(copies(which, slot, 0, 1))

        @pl.when(jnp.logical_not(first | last))
        def _():
            fn(copies(which, slot, 0, 0))

    def start(cs):
        for c in cs:
            c.start()

    def wait(cs):
        for c in cs:
            c.wait()

    @pl.when(band == 0)
    def _():
        each_case(band, 0, start)

    @pl.when(band + 1 < bands)
    def _():
        each_case(band + 1, (band + 1) % 2, start)

    slot = band % 2
    each_case(band, slot, wait)

    span = pl.ds(band * height, height + 2)
    for _, buf, fl, (l_ref, r_ref, t_ref, b_ref) in sources:
        width = buf.shape[2]
        fl[:, pl.ds(OFF, width), :] = buf[slot].astype(jnp.float32)
        fl[:, pl.ds(OFF - 1, 1), :] = l_ref[span].astype(jnp.float32)[:, None, :]
        fl[:, pl.ds(OFF + width, 1), :] = r_ref[span].astype(jnp.float32)[:, None, :]

        @pl.when(band == 0)
        def _():
            fl[0, pl.ds(OFF - 1, width + 2), :] = t_ref[...].astype(jnp.float32)

        @pl.when(band == bands - 1)
        def _():
            fl[height + 1, pl.ds(OFF - 1, width + 2), :] = b_ref[...].astype(jnp.float32)


def depth(src, kern, r0, width):
    acc = jnp.zeros((RC, width, src.shape[2]), jnp.float32)
    for a in range(3):
        for b in range(3):
            acc = acc + src[pl.ds(r0 + a, RC), pl.ds(OFF - 1 + b, width), :] * kern[a, b]
    return acc.astype(jnp.bfloat16).reshape(RC * width, src.shape[2])


def depth_kernel(x_hbm, l_ref, r_ref, t_ref, b_ref, k_ref, out_ref, buf, fl, sem):
    band = pl.program_id(0)
    height, width, ch = out_ref.shape
    windows(band, pl.num_programs(0), height, [(x_hbm, buf, fl, (l_ref, r_ref, t_ref, b_ref))], sem)
    kern = k_ref[...]

    def chunk(step, carry):
        r0 = step * RC
        out_ref[pl.ds(r0, RC)] = depth(fl, kern, r0, width).reshape(RC, width, ch)
        return carry

    lax.fori_loop(0, height // RC, chunk, 0)


def sigmoid(x):
    return 0.5 * jnp.tanh(0.5 * x) + 0.5


def gru_kernel(din_ref, xhid_hbm, hl_ref, hr_ref, ht_ref, hb_ref,
               khid_ref, w_ref, bias_ref,
               out_ref, hbuf, hfl, sem):
    band = pl.program_id(0)
    height, width, ch = out_ref.shape
    windows(band, pl.num_programs(0), height,
            [(xhid_hbm, hbuf, hfl, (hl_ref, hr_ref, ht_ref, hb_ref))], sem)

    khid = khid_ref[...]
    weights = w_ref[...]
    bias = bias_ref[...]

    def chunk(step, carry):
        r0 = step * RC
        d_in = din_ref[pl.ds(r0, RC)].reshape(RC * width, ch)
        d_hid = depth(hfl, khid, r0, width)
        both = jnp.concatenate([d_in, d_hid], axis=1)
        gates = jnp.dot(both, weights, preferred_element_type=jnp.float32) + bias
        update = sigmoid(gates[:, :ch])
        reset = sigmoid(gates[:, ch:2 * ch])
        cand = jnp.tanh(gates[:, 2 * ch:3 * ch] + reset * gates[:, 3 * ch:])
        prev = hfl[pl.ds(r0 + 1, RC), pl.ds(OFF, width), :].reshape(RC * width, ch)
        new = cand + update * (prev - cand)
        out_ref[pl.ds(r0, RC)] = new.astype(out_ref.dtype).reshape(RC, width, ch)
        return carry

    lax.fori_loop(0, height // RC, chunk, 0)


def full(shape):
    return pl.BlockSpec(shape, lambda b: (0,) * len(shape))


def window_scratch(width, ch):
    return [
        pltpu.VMEM((2, BAND + 2, width, ch), jnp.bfloat16),
        pltpu.VMEM((BAND + 2, width + 2 * OFF, ch), jnp.float32),
        pltpu.SemaphoreType.DMA((1, 2)),
    ]


def depth_in(inputs, in_ring, kern_in):
    tile_h, width, ch = inputs.shape
    return pl.pallas_call(
        depth_kernel,
        grid=(tile_h // BAND,),
        in_specs=[pl.BlockSpec(memory_space=pl.ANY)]
        + [full(r.shape) for r in in_ring]
        + [full(kern_in.shape)],
        out_specs=pl.BlockSpec((BAND, width, ch), lambda b: (b, 0, 0)),
        out_shape=jax.ShapeDtypeStruct((tile_h, width, ch), jnp.bfloat16),
        scratch_shapes=window_scratch(width, ch),
        compiler_params=pltpu.CompilerParams(dimension_semantics=("arbitrary",)),
    )(inputs, *in_ring, kern_in)


def gru(d_in, warped, hid_ring, kern_hid, w_in, w_hid, bias_in, bias_hid):
    tile_h, width, ch = warped.shape
    band_spec = pl.BlockSpec((BAND, width, ch), lambda b: (b, 0, 0))
    zeros = jnp.zeros((ch, ch), w_in.dtype)
    weights = jnp.concatenate(
        [
            jnp.concatenate([w_in[:, :2 * ch], w_in[:, 2 * ch:], zeros], axis=1),
            jnp.concatenate([w_hid[:, :2 * ch], zeros, w_hid[:, 2 * ch:]], axis=1),
        ],
        axis=0,
    )
    bias = jnp.concatenate(
        [bias_in[:2 * ch] + bias_hid[:2 * ch], bias_in[2 * ch:], bias_hid[2 * ch:]]
    ).reshape(1, -1)
    return pl.pallas_call(
        gru_kernel,
        grid=(tile_h // BAND,),
        in_specs=[band_spec, pl.BlockSpec(memory_space=pl.ANY)]
        + [full(r.shape) for r in hid_ring]
        + [full(kern_hid.shape), full(weights.shape), full(bias.shape)],
        out_specs=band_spec,
        out_shape=jax.ShapeDtypeStruct((tile_h, width, ch), jnp.bfloat16),
        scratch_shapes=window_scratch(width, ch),
        compiler_params=pltpu.CompilerParams(dimension_semantics=("arbitrary",)),
    )(d_in, warped, *hid_ring, kern_hid, weights, bias)


def body(inputs, hidden, motion, kern_in, kern_hid, w_in, w_hid, bias_in, bias_hid):
    tile_h, tile_w, channels = hidden.shape
    block_count_r = tile_h // BLOCK
    block_count_c = tile_w // BLOCK
    row_base = lax.axis_index("row") * block_count_r
    col_base = lax.axis_index("col") * block_count_c
    anchor = jnp.zeros((), jnp.int32)

    def edge_rows(cols):
        return jnp.concatenate([hidden[:HALO, cols], hidden[tile_h - HALO:, cols]], axis=0)

    cols = lax.axis_size("col")
    to_right = edge_rows(slice(tile_w - HALO, tile_w))
    to_left = edge_rows(slice(0, HALO))
    to_right, to_left = lax.optimization_barrier((to_right, to_left))
    left_edge = lax.ppermute(to_right, "col", [(i, i + 1) for i in range(cols - 1)])
    right_edge = lax.ppermute(to_left, "col", [(i + 1, i) for i in range(cols - 1)])
    held, _, _ = lax.optimization_barrier((hidden, to_right, to_left))
    top, bottom = exchange(held, "row", 0, HALO)
    top_left, bottom_left = exchange(left_edge, "row", 0, HALO)
    top_right, bottom_right = exchange(right_edge, "row", 0, HALO)
    middle, _, _ = lax.optimization_barrier((hidden[HALO:tile_h - HALO], left_edge, right_edge))
    left_mid, right_mid = exchange(middle, "col", 1, HALO)

    sources = lax.dynamic_slice(
        motion, (anchor, row_base, col_base), (2, block_count_r, block_count_c)
    )
    src_r = jnp.clip(sources[0] - row_base, -DISP, block_count_r + DISP - 1)
    src_c = jnp.clip(sources[1] - col_base, -DISP, block_count_c + DISP - 1)
    srel = jnp.stack([src_r, src_c], axis=-1).reshape(-1).astype(jnp.int32)

    d_in = depth_in(inputs, ring(inputs), kern_in)
    warped = warp(
        srel,
        (hidden, left_edge, left_mid, right_edge, right_mid, top, bottom,
         top_left, top_right, bottom_left, bottom_right),
    )
    return gru(d_in, warped, ring(warped), kern_hid, w_in, w_hid, bias_in, bias_hid)


def solution(mesh):
    in_specs = (P("row", "col", None), P("row", "col", None), P(), P(), P(), P(), P(), P(), P())
    out_specs = P("row", "col", None)
    return jax.shard_map(body, mesh=mesh, in_specs=in_specs, out_specs=out_specs, check_vma=False)
```

```python
import jax
import jax.numpy as jnp
from jax import lax
from jax.experimental import pallas as pl
from jax.experimental.pallas import tpu as pltpu
from jax.sharding import PartitionSpec as P

BLOCK = 16
DISP = 4
HALO = DISP * BLOCK
RC = 8
BAND = 32
WARP_ROWS = 4


def exchange(x, axis, dim, width):
    count = lax.axis_size(axis)
    forward = [(i, i + 1) for i in range(count - 1)]
    backward = [(i + 1, i) for i in range(count - 1)]
    size = x.shape[dim]
    low = lax.ppermute(lax.slice_in_dim(x, size - width, size, axis=dim), axis, forward)
    high = lax.ppermute(lax.slice_in_dim(x, 0, width, axis=dim), axis, backward)
    return low, high


def ring(x):
    left, right = exchange(x, "col", 1, 1)
    last = x.shape[0] - 1
    count = lax.axis_size("row")
    forward = [(i, i + 1) for i in range(count - 1)]
    backward = [(i + 1, i) for i in range(count - 1)]
    down = jnp.concatenate([left[last:], x[last:], right[last:]], axis=1)
    up = jnp.concatenate([left[:1], x[:1], right[:1]], axis=1)
    top = lax.ppermute(down, "row", forward)[0]
    bottom = lax.ppermute(up, "row", backward)[0]
    width = x.shape[1]
    side_l = jnp.concatenate([top[:1], left[:, 0], bottom[:1]], axis=0)
    side_r = jnp.concatenate([top[width + 1:], right[:, 0], bottom[width + 1:]], axis=0)
    return side_l, side_r, top, bottom


def warp_kernel(srel_ref, *refs):
    hbm = refs[:11]
    out_ref = refs[11]
    canvas = refs[12]
    sem = refs[13]
    c_hbm, le_hbm, lm_hbm, re_hbm, rm_hbm, t_hbm, b_hbm, tl_hbm, tr_hbm, bl_hbm, br_hbm = hbm
    tile_h, per_row = c_hbm.shape[0], c_hbm.shape[1]
    side = le_hbm.shape[1]
    edge = le_hbm.shape[0] // 2
    band = pl.program_id(0)
    bands = pl.num_programs(0)

    def place(rows, cols):
        return canvas.at[pl.ds(rows[0], rows[1]), pl.ds(cols[0], cols[1])]

    mid = (HALO, tile_h)
    west, centre, east = (0, side), (side, per_row), (side + per_row, side)
    pairs = [
        (c_hbm, place(mid, centre)),
        (le_hbm.at[pl.ds(0, edge)], place((HALO, edge), west)),
        (le_hbm.at[pl.ds(edge, edge)], place((HALO + tile_h - edge, edge), west)),
        (lm_hbm, place((HALO + edge, tile_h - 2 * edge), west)),
        (re_hbm.at[pl.ds(0, edge)], place((HALO, edge), east)),
        (re_hbm.at[pl.ds(edge, edge)], place((HALO + tile_h - edge, edge), east)),
        (rm_hbm, place((HALO + edge, tile_h - 2 * edge), east)),
        (t_hbm, place((0, HALO), centre)),
        (b_hbm, place((HALO + tile_h, HALO), centre)),
        (tl_hbm, place((0, HALO), west)),
        (tr_hbm, place((0, HALO), east)),
        (bl_hbm, place((HALO + tile_h, HALO), west)),
        (br_hbm, place((HALO + tile_h, HALO), east)),
    ]
    copies = [pltpu.make_async_copy(h, v, sem.at[n]) for n, (h, v) in enumerate(pairs)]

    @pl.when(band == 0)
    def _():
        for c in copies:
            c.start()
        for c in copies:
            c.wait()

    def gather(n, carry):
        k = band * WARP_ROWS * per_row + n
        r0 = srel_ref[2 * k] * BLOCK + HALO
        cb = srel_ref[2 * k + 1] + side
        out_ref[pl.ds((n // per_row) * BLOCK, BLOCK), n % per_row] = canvas[pl.ds(r0, BLOCK), cb]
        return carry

    lax.fori_loop(0, WARP_ROWS * per_row, gather, 0, unroll=True)


def warp(srel, pieces):
    def blocked(x):
        return x.reshape(x.shape[0], x.shape[1] // BLOCK, BLOCK, x.shape[2])

    parts = [blocked(x) for x in pieces]
    any_spec = pl.BlockSpec(memory_space=pl.ANY)
    shape = parts[0].shape
    side = parts[1].shape[1]
    canvas = (shape[0] + 2 * HALO, shape[1] + 2 * side) + shape[2:]
    out = pl.pallas_call(
        warp_kernel,
        grid_spec=pltpu.PrefetchScalarGridSpec(
            num_scalar_prefetch=1,
            grid=(shape[0] // (BLOCK * WARP_ROWS),),
            in_specs=[any_spec] * len(parts),
            out_specs=pl.BlockSpec((BLOCK * WARP_ROWS,) + shape[1:], lambda g, s: (g, 0, 0, 0)),
            scratch_shapes=[pltpu.VMEM(canvas, parts[0].dtype),
                            pltpu.SemaphoreType.DMA((len(parts) + 2,))],
        ),
        out_shape=jax.ShapeDtypeStruct(shape, pieces[0].dtype),
        compiler_params=pltpu.CompilerParams(
            dimension_semantics=("arbitrary",), vmem_limit_bytes=60 * 1024 * 1024
        ),
    )(srel, *parts)
    return out.reshape(pieces[0].shape)


OFF = 8


def windows(band, bands, height, sources, sem):
    def copies(which, slot, lo, hi):
        src = pl.ds(which * height - 1 + lo, height + 2 - lo - hi)
        dst = pl.ds(lo, height + 2 - lo - hi)
        return [
            pltpu.make_async_copy(x_hbm.at[src], buf.at[slot, dst], sem.at[n, slot])
            for n, (x_hbm, buf, _, _) in enumerate(sources)
        ]

    def each_case(which, slot, fn):
        first = which == 0
        last = which == bands - 1

        @pl.when(first)
        def _():
            fn(copies(which, slot, 1, 0))

        @pl.when(last)
        def _():
            fn(copies(which, slot, 0, 1))

        @pl.when(jnp.logical_not(first | last))
        def _():
            fn(copies(which, slot, 0, 0))

    def start(cs):
        for c in cs:
            c.start()

    def wait(cs):
        for c in cs:
            c.wait()

    @pl.when(band == 0)
    def _():
        each_case(band, 0, start)

    @pl.when(band + 1 < bands)
    def _():
        each_case(band + 1, (band + 1) % 2, start)

    slot = band % 2
    each_case(band, slot, wait)

    span = pl.ds(band * height, height + 2)
    for _, buf, fl, (l_ref, r_ref, t_ref, b_ref) in sources:
        width = buf.shape[2]
        fl[:, pl.ds(OFF, width), :] = buf[slot].astype(jnp.float32)
        fl[:, pl.ds(OFF - 1, 1), :] = l_ref[span].astype(jnp.float32)[:, None, :]
        fl[:, pl.ds(OFF + width, 1), :] = r_ref[span].astype(jnp.float32)[:, None, :]

        @pl.when(band == 0)
        def _():
            fl[0, pl.ds(OFF - 1, width + 2), :] = t_ref[...].astype(jnp.float32)

        @pl.when(band == bands - 1)
        def _():
            fl[height + 1, pl.ds(OFF - 1, width + 2), :] = b_ref[...].astype(jnp.float32)


def depth(src, kern, r0, width):
    acc = jnp.zeros((RC, width, src.shape[2]), jnp.float32)
    for a in range(3):
        for b in range(3):
            acc = acc + src[pl.ds(r0 + a, RC), pl.ds(OFF - 1 + b, width), :] * kern[a, b]
    return acc.astype(jnp.bfloat16).reshape(RC * width, src.shape[2])


def depth_kernel(x_hbm, l_ref, r_ref, t_ref, b_ref, k_ref, out_ref, buf, fl, sem):
    band = pl.program_id(0)
    height, width, ch = out_ref.shape
    windows(band, pl.num_programs(0), height, [(x_hbm, buf, fl, (l_ref, r_ref, t_ref, b_ref))], sem)
    kern = k_ref[...]

    def chunk(step, carry):
        r0 = step * RC
        out_ref[pl.ds(r0, RC)] = depth(fl, kern, r0, width).reshape(RC, width, ch)
        return carry

    lax.fori_loop(0, height // RC, chunk, 0)


def sigmoid(x):
    return 0.5 * jnp.tanh(0.5 * x) + 0.5


def gru_kernel(din_ref, xhid_hbm, hl_ref, hr_ref, ht_ref, hb_ref,
               khid_ref, w_ref, bias_ref,
               out_ref, hbuf, hfl, sem):
    band = pl.program_id(0)
    height, width, ch = out_ref.shape
    windows(band, pl.num_programs(0), height,
            [(xhid_hbm, hbuf, hfl, (hl_ref, hr_ref, ht_ref, hb_ref))], sem)

    khid = khid_ref[...]
    weights = w_ref[...]
    bias = bias_ref[...]

    def chunk(step, carry):
        r0 = step * RC
        d_in = din_ref[pl.ds(r0, RC)].reshape(RC * width, ch)
        d_hid = depth(hfl, khid, r0, width)
        both = jnp.concatenate([d_in, d_hid], axis=1)
        gates = jnp.dot(both, weights, preferred_element_type=jnp.float32) + bias
        update = sigmoid(gates[:, :ch])
        reset = sigmoid(gates[:, ch:2 * ch])
        cand = jnp.tanh(gates[:, 2 * ch:3 * ch] + reset * gates[:, 3 * ch:])
        prev = hfl[pl.ds(r0 + 1, RC), pl.ds(OFF, width), :].reshape(RC * width, ch)
        new = cand + update * (prev - cand)
        out_ref[pl.ds(r0, RC)] = new.astype(out_ref.dtype).reshape(RC, width, ch)
        return carry

    lax.fori_loop(0, height // RC, chunk, 0)


def full(shape):
    return pl.BlockSpec(shape, lambda b: (0,) * len(shape))


def window_scratch(width, ch):
    return [
        pltpu.VMEM((2, BAND + 2, width, ch), jnp.bfloat16),
        pltpu.VMEM((BAND + 2, width + 2 * OFF, ch), jnp.float32),
        pltpu.SemaphoreType.DMA((1, 2)),
    ]


def depth_in(inputs, in_ring, kern_in):
    tile_h, width, ch = inputs.shape
    return pl.pallas_call(
        depth_kernel,
        grid=(tile_h // BAND,),
        in_specs=[pl.BlockSpec(memory_space=pl.ANY)]
        + [full(r.shape) for r in in_ring]
        + [full(kern_in.shape)],
        out_specs=pl.BlockSpec((BAND, width, ch), lambda b: (b, 0, 0)),
        out_shape=jax.ShapeDtypeStruct((tile_h, width, ch), jnp.bfloat16),
        scratch_shapes=window_scratch(width, ch),
        compiler_params=pltpu.CompilerParams(dimension_semantics=("arbitrary",)),
    )(inputs, *in_ring, kern_in)


def gru(d_in, warped, hid_ring, kern_hid, w_in, w_hid, bias_in, bias_hid):
    tile_h, width, ch = warped.shape
    band_spec = pl.BlockSpec((BAND, width, ch), lambda b: (b, 0, 0))
    zeros = jnp.zeros((ch, ch), w_in.dtype)
    weights = jnp.concatenate(
        [
            jnp.concatenate([w_in[:, :2 * ch], w_in[:, 2 * ch:], zeros], axis=1),
            jnp.concatenate([w_hid[:, :2 * ch], zeros, w_hid[:, 2 * ch:]], axis=1),
        ],
        axis=0,
    )
    bias = jnp.concatenate(
        [bias_in[:2 * ch] + bias_hid[:2 * ch], bias_in[2 * ch:], bias_hid[2 * ch:]]
    ).reshape(1, -1)
    return pl.pallas_call(
        gru_kernel,
        grid=(tile_h // BAND,),
        in_specs=[band_spec, pl.BlockSpec(memory_space=pl.ANY)]
        + [full(r.shape) for r in hid_ring]
        + [full(kern_hid.shape), full(weights.shape), full(bias.shape)],
        out_specs=band_spec,
        out_shape=jax.ShapeDtypeStruct((tile_h, width, ch), jnp.bfloat16),
        scratch_shapes=window_scratch(width, ch),
        compiler_params=pltpu.CompilerParams(dimension_semantics=("arbitrary",)),
    )(d_in, warped, *hid_ring, kern_hid, weights, bias)


def body(inputs, hidden, motion, kern_in, kern_hid, w_in, w_hid, bias_in, bias_hid):
    tile_h, tile_w, channels = hidden.shape
    block_count_r = tile_h // BLOCK
    block_count_c = tile_w // BLOCK
    row_base = lax.axis_index("row") * block_count_r
    col_base = lax.axis_index("col") * block_count_c
    anchor = jnp.zeros((), jnp.int32)

    def edge_rows(cols):
        return jnp.concatenate([hidden[:HALO, cols], hidden[tile_h - HALO:, cols]], axis=0)

    cols = lax.axis_size("col")
    to_right = edge_rows(slice(tile_w - HALO, tile_w))
    to_left = edge_rows(slice(0, HALO))
    to_right, to_left = lax.optimization_barrier((to_right, to_left))
    left_edge = lax.ppermute(to_right, "col", [(i, i + 1) for i in range(cols - 1)])
    right_edge = lax.ppermute(to_left, "col", [(i + 1, i) for i in range(cols - 1)])
    mid_right = hidden[HALO:tile_h - HALO, tile_w - HALO:]
    mid_left = hidden[HALO:tile_h - HALO, :HALO]
    held, mid_right, mid_left, _, _ = lax.optimization_barrier(
        (hidden, mid_right, mid_left, to_right, to_left)
    )
    top, bottom = exchange(held, "row", 0, HALO)
    top_left, bottom_left = exchange(left_edge, "row", 0, HALO)
    top_right, bottom_right = exchange(right_edge, "row", 0, HALO)
    mid_right, mid_left, _, _ = lax.optimization_barrier((mid_right, mid_left, left_edge, right_edge))
    left_mid = lax.ppermute(mid_right, "col", [(i, i + 1) for i in range(cols - 1)])
    right_mid = lax.ppermute(mid_left, "col", [(i + 1, i) for i in range(cols - 1)])

    sources = lax.dynamic_slice(
        motion, (anchor, row_base, col_base), (2, block_count_r, block_count_c)
    )
    src_r = jnp.clip(sources[0] - row_base, -DISP, block_count_r + DISP - 1)
    src_c = jnp.clip(sources[1] - col_base, -DISP, block_count_c + DISP - 1)
    srel = jnp.stack([src_r, src_c], axis=-1).reshape(-1).astype(jnp.int32)

    d_in = depth_in(inputs, ring(inputs), kern_in)
    warped = warp(
        srel,
        (hidden, left_edge, left_mid, right_edge, right_mid, top, bottom,
         top_left, top_right, bottom_left, bottom_right),
    )
    return gru(d_in, warped, ring(warped), kern_hid, w_in, w_hid, bias_in, bias_hid)


def solution(mesh):
    in_specs = (P("row", "col", None), P("row", "col", None), P(), P(), P(), P(), P(), P(), P())
    out_specs = P("row", "col", None)
    return jax.shard_map(body, mesh=mesh, in_specs=in_specs, out_specs=out_specs, check_vma=False)
```

```python
import jax
import jax.numpy as jnp
from jax import lax
from jax.experimental import pallas as pl
from jax.experimental.pallas import tpu as pltpu
from jax.sharding import PartitionSpec as P

BLOCK = 16
DISP = 4
HALO = DISP * BLOCK
RC = 16
BAND = 32
WARP_ROWS = 4


def exchange(x, axis, dim, width):
    count = lax.axis_size(axis)
    forward = [(i, i + 1) for i in range(count - 1)]
    backward = [(i + 1, i) for i in range(count - 1)]
    size = x.shape[dim]
    low = lax.ppermute(lax.slice_in_dim(x, size - width, size, axis=dim), axis, forward)
    high = lax.ppermute(lax.slice_in_dim(x, 0, width, axis=dim), axis, backward)
    return low, high


def ring(x):
    left, right = exchange(x, "col", 1, 1)
    last = x.shape[0] - 1
    count = lax.axis_size("row")
    forward = [(i, i + 1) for i in range(count - 1)]
    backward = [(i + 1, i) for i in range(count - 1)]
    down = jnp.concatenate([left[last:], x[last:], right[last:]], axis=1)
    up = jnp.concatenate([left[:1], x[:1], right[:1]], axis=1)
    top = lax.ppermute(down, "row", forward)[0]
    bottom = lax.ppermute(up, "row", backward)[0]
    width = x.shape[1]
    side_l = jnp.concatenate([top[:1], left[:, 0], bottom[:1]], axis=0)
    side_r = jnp.concatenate([top[width + 1:], right[:, 0], bottom[width + 1:]], axis=0)
    return side_l, side_r, top, bottom


def warp_kernel(srel_ref, *refs):
    hbm = refs[:11]
    out_ref = refs[11]
    canvas = refs[12]
    sem = refs[13]
    c_hbm, le_hbm, lm_hbm, re_hbm, rm_hbm, t_hbm, b_hbm, tl_hbm, tr_hbm, bl_hbm, br_hbm = hbm
    tile_h, per_row = c_hbm.shape[0], c_hbm.shape[1]
    side = le_hbm.shape[1]
    edge = le_hbm.shape[0] // 2
    band = pl.program_id(0)
    bands = pl.num_programs(0)

    def place(rows, cols):
        return canvas.at[pl.ds(rows[0], rows[1]), pl.ds(cols[0], cols[1])]

    mid = (HALO, tile_h)
    west, centre, east = (0, side), (side, per_row), (side + per_row, side)
    pairs = [
        (c_hbm, place(mid, centre)),
        (le_hbm.at[pl.ds(0, edge)], place((HALO, edge), west)),
        (le_hbm.at[pl.ds(edge, edge)], place((HALO + tile_h - edge, edge), west)),
        (lm_hbm, place((HALO + edge, tile_h - 2 * edge), west)),
        (re_hbm.at[pl.ds(0, edge)], place((HALO, edge), east)),
        (re_hbm.at[pl.ds(edge, edge)], place((HALO + tile_h - edge, edge), east)),
        (rm_hbm, place((HALO + edge, tile_h - 2 * edge), east)),
        (t_hbm, place((0, HALO), centre)),
        (b_hbm, place((HALO + tile_h, HALO), centre)),
        (tl_hbm, place((0, HALO), west)),
        (tr_hbm, place((0, HALO), east)),
        (bl_hbm, place((HALO + tile_h, HALO), west)),
        (br_hbm, place((HALO + tile_h, HALO), east)),
    ]
    copies = [pltpu.make_async_copy(h, v, sem.at[n]) for n, (h, v) in enumerate(pairs)]

    @pl.when(band == 0)
    def _():
        for c in copies:
            c.start()
        for c in copies:
            c.wait()

    def gather(n, carry):
        k = band * WARP_ROWS * per_row + n
        r0 = srel_ref[2 * k] * BLOCK + HALO
        cb = srel_ref[2 * k + 1] + side
        out_ref[pl.ds((n // per_row) * BLOCK, BLOCK), n % per_row] = canvas[pl.ds(r0, BLOCK), cb]
        return carry

    lax.fori_loop(0, WARP_ROWS * per_row, gather, 0, unroll=True)


def warp(srel, pieces):
    def blocked(x):
        return x.reshape(x.shape[0], x.shape[1] // BLOCK, BLOCK, x.shape[2])

    parts = [blocked(x) for x in pieces]
    any_spec = pl.BlockSpec(memory_space=pl.ANY)
    shape = parts[0].shape
    side = parts[1].shape[1]
    canvas = (shape[0] + 2 * HALO, shape[1] + 2 * side) + shape[2:]
    out = pl.pallas_call(
        warp_kernel,
        grid_spec=pltpu.PrefetchScalarGridSpec(
            num_scalar_prefetch=1,
            grid=(shape[0] // (BLOCK * WARP_ROWS),),
            in_specs=[any_spec] * len(parts),
            out_specs=pl.BlockSpec((BLOCK * WARP_ROWS,) + shape[1:], lambda g, s: (g, 0, 0, 0)),
            scratch_shapes=[pltpu.VMEM(canvas, parts[0].dtype),
                            pltpu.SemaphoreType.DMA((len(parts) + 2,))],
        ),
        out_shape=jax.ShapeDtypeStruct(shape, pieces[0].dtype),
        compiler_params=pltpu.CompilerParams(
            dimension_semantics=("arbitrary",), vmem_limit_bytes=60 * 1024 * 1024
        ),
    )(srel, *parts)
    return out.reshape(pieces[0].shape)


OFF = 8


def windows(band, bands, height, sources, sem):
    def copies(which, slot, lo, hi):
        src = pl.ds(which * height - 1 + lo, height + 2 - lo - hi)
        dst = pl.ds(lo, height + 2 - lo - hi)
        return [
            pltpu.make_async_copy(x_hbm.at[src], buf.at[slot, dst], sem.at[n, slot])
            for n, (x_hbm, buf, _, _) in enumerate(sources)
        ]

    def each_case(which, slot, fn):
        first = which == 0
        last = which == bands - 1

        @pl.when(first)
        def _():
            fn(copies(which, slot, 1, 0))

        @pl.when(last)
        def _():
            fn(copies(which, slot, 0, 1))

        @pl.when(jnp.logical_not(first | last))
        def _():
            fn(copies(which, slot, 0, 0))

    def start(cs):
        for c in cs:
            c.start()

    def wait(cs):
        for c in cs:
            c.wait()

    @pl.when(band == 0)
    def _():
        each_case(band, 0, start)

    @pl.when(band + 1 < bands)
    def _():
        each_case(band + 1, (band + 1) % 2, start)

    slot = band % 2
    each_case(band, slot, wait)

    span = pl.ds(band * height, height + 2)
    for _, buf, fl, (l_ref, r_ref, t_ref, b_ref) in sources:
        width = buf.shape[2]
        fl[:, pl.ds(OFF, width), :] = buf[slot].astype(jnp.float32)
        fl[:, pl.ds(OFF - 1, 1), :] = l_ref[span].astype(jnp.float32)[:, None, :]
        fl[:, pl.ds(OFF + width, 1), :] = r_ref[span].astype(jnp.float32)[:, None, :]

        @pl.when(band == 0)
        def _():
            fl[0, pl.ds(OFF - 1, width + 2), :] = t_ref[...].astype(jnp.float32)

        @pl.when(band == bands - 1)
        def _():
            fl[height + 1, pl.ds(OFF - 1, width + 2), :] = b_ref[...].astype(jnp.float32)


def depth(src, kern, r0, width):
    acc = jnp.zeros((RC, width, src.shape[2]), jnp.float32)
    for a in range(3):
        for b in range(3):
            acc = acc + src[pl.ds(r0 + a, RC), pl.ds(OFF - 1 + b, width), :] * kern[a, b]
    return acc.astype(jnp.bfloat16).reshape(RC * width, src.shape[2])


def depth_kernel(x_hbm, l_ref, r_ref, t_ref, b_ref, k_ref, out_ref, buf, fl, sem):
    band = pl.program_id(0)
    height, width, ch = out_ref.shape
    windows(band, pl.num_programs(0), height, [(x_hbm, buf, fl, (l_ref, r_ref, t_ref, b_ref))], sem)
    kern = k_ref[...]

    def chunk(step, carry):
        r0 = step * RC
        out_ref[pl.ds(r0, RC)] = depth(fl, kern, r0, width).reshape(RC, width, ch)
        return carry

    lax.fori_loop(0, height // RC, chunk, 0)


def sigmoid(x):
    return 0.5 * jnp.tanh(0.5 * x) + 0.5


def gru_kernel(din_ref, xhid_hbm, hl_ref, hr_ref, ht_ref, hb_ref,
               khid_ref, w_ref, bias_ref,
               out_ref, hbuf, hfl, sem):
    band = pl.program_id(0)
    height, width, ch = out_ref.shape
    windows(band, pl.num_programs(0), height,
            [(xhid_hbm, hbuf, hfl, (hl_ref, hr_ref, ht_ref, hb_ref))], sem)

    khid = khid_ref[...]
    weights = w_ref[...]
    bias = bias_ref[...]

    def chunk(step, carry):
        r0 = step * RC
        d_in = din_ref[pl.ds(r0, RC)].reshape(RC * width, ch)
        d_hid = depth(hfl, khid, r0, width)
        both = jnp.concatenate([d_in, d_hid], axis=1)
        gates = jnp.dot(both, weights, preferred_element_type=jnp.float32) + bias
        update = sigmoid(gates[:, :ch])
        reset = sigmoid(gates[:, ch:2 * ch])
        cand = jnp.tanh(gates[:, 2 * ch:3 * ch] + reset * gates[:, 3 * ch:])
        prev = hfl[pl.ds(r0 + 1, RC), pl.ds(OFF, width), :].reshape(RC * width, ch)
        new = cand + update * (prev - cand)
        out_ref[pl.ds(r0, RC)] = new.astype(out_ref.dtype).reshape(RC, width, ch)
        return carry

    lax.fori_loop(0, height // RC, chunk, 0)


def full(shape):
    return pl.BlockSpec(shape, lambda b: (0,) * len(shape))


def window_scratch(width, ch):
    return [
        pltpu.VMEM((2, BAND + 2, width, ch), jnp.bfloat16),
        pltpu.VMEM((BAND + 2, width + 2 * OFF, ch), jnp.float32),
        pltpu.SemaphoreType.DMA((1, 2)),
    ]


def depth_in(inputs, in_ring, kern_in):
    tile_h, width, ch = inputs.shape
    return pl.pallas_call(
        depth_kernel,
        grid=(tile_h // BAND,),
        in_specs=[pl.BlockSpec(memory_space=pl.ANY)]
        + [full(r.shape) for r in in_ring]
        + [full(kern_in.shape)],
        out_specs=pl.BlockSpec((BAND, width, ch), lambda b: (b, 0, 0)),
        out_shape=jax.ShapeDtypeStruct((tile_h, width, ch), jnp.bfloat16),
        scratch_shapes=window_scratch(width, ch),
        compiler_params=pltpu.CompilerParams(dimension_semantics=("arbitrary",)),
    )(inputs, *in_ring, kern_in)


def gru(d_in, warped, hid_ring, kern_hid, w_in, w_hid, bias_in, bias_hid):
    tile_h, width, ch = warped.shape
    band_spec = pl.BlockSpec((BAND, width, ch), lambda b: (b, 0, 0))
    zeros = jnp.zeros((ch, ch), w_in.dtype)
    weights = jnp.concatenate(
        [
            jnp.concatenate([w_in[:, :2 * ch], w_in[:, 2 * ch:], zeros], axis=1),
            jnp.concatenate([w_hid[:, :2 * ch], zeros, w_hid[:, 2 * ch:]], axis=1),
        ],
        axis=0,
    )
    bias = jnp.concatenate(
        [bias_in[:2 * ch] + bias_hid[:2 * ch], bias_in[2 * ch:], bias_hid[2 * ch:]]
    ).reshape(1, -1)
    return pl.pallas_call(
        gru_kernel,
        grid=(tile_h // BAND,),
        in_specs=[band_spec, pl.BlockSpec(memory_space=pl.ANY)]
        + [full(r.shape) for r in hid_ring]
        + [full(kern_hid.shape), full(weights.shape), full(bias.shape)],
        out_specs=band_spec,
        out_shape=jax.ShapeDtypeStruct((tile_h, width, ch), jnp.bfloat16),
        scratch_shapes=window_scratch(width, ch),
        compiler_params=pltpu.CompilerParams(dimension_semantics=("arbitrary",)),
    )(d_in, warped, *hid_ring, kern_hid, weights, bias)


def body(inputs, hidden, motion, kern_in, kern_hid, w_in, w_hid, bias_in, bias_hid):
    tile_h, tile_w, channels = hidden.shape
    block_count_r = tile_h // BLOCK
    block_count_c = tile_w // BLOCK
    row_base = lax.axis_index("row") * block_count_r
    col_base = lax.axis_index("col") * block_count_c
    anchor = jnp.zeros((), jnp.int32)

    def edge_rows(cols):
        return jnp.concatenate([hidden[:HALO, cols], hidden[tile_h - HALO:, cols]], axis=0)

    cols = lax.axis_size("col")
    to_right = edge_rows(slice(tile_w - HALO, tile_w))
    to_left = edge_rows(slice(0, HALO))
    to_right, to_left = lax.optimization_barrier((to_right, to_left))
    left_edge = lax.ppermute(to_right, "col", [(i, i + 1) for i in range(cols - 1)])
    right_edge = lax.ppermute(to_left, "col", [(i + 1, i) for i in range(cols - 1)])
    mid_right = hidden[HALO:tile_h - HALO, tile_w - HALO:]
    mid_left = hidden[HALO:tile_h - HALO, :HALO]
    held, mid_right, mid_left, _, _ = lax.optimization_barrier(
        (hidden, mid_right, mid_left, to_right, to_left)
    )
    top, bottom = exchange(held, "row", 0, HALO)
    top_left, bottom_left = exchange(left_edge, "row", 0, HALO)
    top_right, bottom_right = exchange(right_edge, "row", 0, HALO)
    mid_right, mid_left, _, _ = lax.optimization_barrier((mid_right, mid_left, left_edge, right_edge))
    left_mid = lax.ppermute(mid_right, "col", [(i, i + 1) for i in range(cols - 1)])
    right_mid = lax.ppermute(mid_left, "col", [(i + 1, i) for i in range(cols - 1)])

    sources = lax.dynamic_slice(
        motion, (anchor, row_base, col_base), (2, block_count_r, block_count_c)
    )
    src_r = jnp.clip(sources[0] - row_base, -DISP, block_count_r + DISP - 1)
    src_c = jnp.clip(sources[1] - col_base, -DISP, block_count_c + DISP - 1)
    srel = jnp.stack([src_r, src_c], axis=-1).reshape(-1).astype(jnp.int32)

    d_in = depth_in(inputs, ring(inputs), kern_in)
    warped = warp(
        srel,
        (hidden, left_edge, left_mid, right_edge, right_mid, top, bottom,
         top_left, top_right, bottom_left, bottom_right),
    )
    return gru(d_in, warped, ring(warped), kern_hid, w_in, w_hid, bias_in, bias_hid)


def solution(mesh):
    in_specs = (P("row", "col", None), P("row", "col", None), P(), P(), P(), P(), P(), P(), P())
    out_specs = P("row", "col", None)
    return jax.shard_map(body, mesh=mesh, in_specs=in_specs, out_specs=out_specs, check_vma=False)
```

```python
import jax
import jax.numpy as jnp
from jax import lax
from jax.experimental import pallas as pl
from jax.experimental.pallas import tpu as pltpu
from jax.sharding import PartitionSpec as P

BLOCK = 16
DISP = 4
HALO = DISP * BLOCK
RC = 16
BAND = 64
WARP_ROWS = 4


def exchange(x, axis, dim, width):
    count = lax.axis_size(axis)
    forward = [(i, i + 1) for i in range(count - 1)]
    backward = [(i + 1, i) for i in range(count - 1)]
    size = x.shape[dim]
    low = lax.ppermute(lax.slice_in_dim(x, size - width, size, axis=dim), axis, forward)
    high = lax.ppermute(lax.slice_in_dim(x, 0, width, axis=dim), axis, backward)
    return low, high


def ring(x):
    left, right = exchange(x, "col", 1, 1)
    last = x.shape[0] - 1
    count = lax.axis_size("row")
    forward = [(i, i + 1) for i in range(count - 1)]
    backward = [(i + 1, i) for i in range(count - 1)]
    down = jnp.concatenate([left[last:], x[last:], right[last:]], axis=1)
    up = jnp.concatenate([left[:1], x[:1], right[:1]], axis=1)
    top = lax.ppermute(down, "row", forward)[0]
    bottom = lax.ppermute(up, "row", backward)[0]
    width = x.shape[1]
    side_l = jnp.concatenate([top[:1], left[:, 0], bottom[:1]], axis=0)
    side_r = jnp.concatenate([top[width + 1:], right[:, 0], bottom[width + 1:]], axis=0)
    return side_l, side_r, top, bottom


def warp_kernel(srel_ref, *refs):
    hbm = refs[:11]
    out_ref = refs[11]
    canvas = refs[12]
    sem = refs[13]
    c_hbm, le_hbm, lm_hbm, re_hbm, rm_hbm, t_hbm, b_hbm, tl_hbm, tr_hbm, bl_hbm, br_hbm = hbm
    tile_h, per_row = c_hbm.shape[0], c_hbm.shape[1]
    side = le_hbm.shape[1]
    edge = le_hbm.shape[0] // 2
    band = pl.program_id(0)
    bands = pl.num_programs(0)

    def place(rows, cols):
        return canvas.at[pl.ds(rows[0], rows[1]), pl.ds(cols[0], cols[1])]

    mid = (HALO, tile_h)
    west, centre, east = (0, side), (side, per_row), (side + per_row, side)
    pairs = [
        (c_hbm, place(mid, centre)),
        (le_hbm.at[pl.ds(0, edge)], place((HALO, edge), west)),
        (le_hbm.at[pl.ds(edge, edge)], place((HALO + tile_h - edge, edge), west)),
        (lm_hbm, place((HALO + edge, tile_h - 2 * edge), west)),
        (re_hbm.at[pl.ds(0, edge)], place((HALO, edge), east)),
        (re_hbm.at[pl.ds(edge, edge)], place((HALO + tile_h - edge, edge), east)),
        (rm_hbm, place((HALO + edge, tile_h - 2 * edge), east)),
        (t_hbm, place((0, HALO), centre)),
        (b_hbm, place((HALO + tile_h, HALO), centre)),
        (tl_hbm, place((0, HALO), west)),
        (tr_hbm, place((0, HALO), east)),
        (bl_hbm, place((HALO + tile_h, HALO), west)),
        (br_hbm, place((HALO + tile_h, HALO), east)),
    ]
    copies = [pltpu.make_async_copy(h, v, sem.at[n]) for n, (h, v) in enumerate(pairs)]

    @pl.when(band == 0)
    def _():
        for c in copies:
            c.start()
        for c in copies:
            c.wait()

    def gather(n, carry):
        k = band * WARP_ROWS * per_row + n
        r0 = srel_ref[2 * k] * BLOCK + HALO
        cb = srel_ref[2 * k + 1] + side
        out_ref[pl.ds((n // per_row) * BLOCK, BLOCK), n % per_row] = canvas[pl.ds(r0, BLOCK), cb]
        return carry

    lax.fori_loop(0, WARP_ROWS * per_row, gather, 0, unroll=True)


def warp(srel, pieces):
    def blocked(x):
        return x.reshape(x.shape[0], x.shape[1] // BLOCK, BLOCK, x.shape[2])

    parts = [blocked(x) for x in pieces]
    any_spec = pl.BlockSpec(memory_space=pl.ANY)
    shape = parts[0].shape
    side = parts[1].shape[1]
    canvas = (shape[0] + 2 * HALO, shape[1] + 2 * side) + shape[2:]
    out = pl.pallas_call(
        warp_kernel,
        grid_spec=pltpu.PrefetchScalarGridSpec(
            num_scalar_prefetch=1,
            grid=(shape[0] // (BLOCK * WARP_ROWS),),
            in_specs=[any_spec] * len(parts),
            out_specs=pl.BlockSpec((BLOCK * WARP_ROWS,) + shape[1:], lambda g, s: (g, 0, 0, 0)),
            scratch_shapes=[pltpu.VMEM(canvas, parts[0].dtype),
                            pltpu.SemaphoreType.DMA((len(parts) + 2,))],
        ),
        out_shape=jax.ShapeDtypeStruct(shape, pieces[0].dtype),
        compiler_params=pltpu.CompilerParams(
            dimension_semantics=("arbitrary",), vmem_limit_bytes=60 * 1024 * 1024
        ),
    )(srel, *parts)
    return out.reshape(pieces[0].shape)


OFF = 8


def windows(band, bands, height, sources, sem):
    def copies(which, slot, lo, hi):
        src = pl.ds(which * height - 1 + lo, height + 2 - lo - hi)
        dst = pl.ds(lo, height + 2 - lo - hi)
        return [
            pltpu.make_async_copy(x_hbm.at[src], buf.at[slot, dst], sem.at[n, slot])
            for n, (x_hbm, buf, _, _) in enumerate(sources)
        ]

    def each_case(which, slot, fn):
        first = which == 0
        last = which == bands - 1

        @pl.when(first)
        def _():
            fn(copies(which, slot, 1, 0))

        @pl.when(last)
        def _():
            fn(copies(which, slot, 0, 1))

        @pl.when(jnp.logical_not(first | last))
        def _():
            fn(copies(which, slot, 0, 0))

    def start(cs):
        for c in cs:
            c.start()

    def wait(cs):
        for c in cs:
            c.wait()

    @pl.when(band == 0)
    def _():
        each_case(band, 0, start)

    @pl.when(band + 1 < bands)
    def _():
        each_case(band + 1, (band + 1) % 2, start)

    slot = band % 2
    each_case(band, slot, wait)

    span = pl.ds(band * height, height + 2)
    for _, buf, fl, (l_ref, r_ref, t_ref, b_ref) in sources:
        width = buf.shape[2]
        fl[:, pl.ds(OFF, width), :] = buf[slot].astype(jnp.float32)
        fl[:, pl.ds(OFF - 1, 1), :] = l_ref[span].astype(jnp.float32)[:, None, :]
        fl[:, pl.ds(OFF + width, 1), :] = r_ref[span].astype(jnp.float32)[:, None, :]

        @pl.when(band == 0)
        def _():
            fl[0, pl.ds(OFF - 1, width + 2), :] = t_ref[...].astype(jnp.float32)

        @pl.when(band == bands - 1)
        def _():
            fl[height + 1, pl.ds(OFF - 1, width + 2), :] = b_ref[...].astype(jnp.float32)


def depth(src, kern, r0, width):
    acc = jnp.zeros((RC, width, src.shape[2]), jnp.float32)
    for a in range(3):
        for b in range(3):
            acc = acc + src[pl.ds(r0 + a, RC), pl.ds(OFF - 1 + b, width), :] * kern[a, b]
    return acc.astype(jnp.bfloat16).reshape(RC * width, src.shape[2])


def depth_kernel(x_hbm, l_ref, r_ref, t_ref, b_ref, k_ref, out_ref, buf, fl, sem):
    band = pl.program_id(0)
    height, width, ch = out_ref.shape
    windows(band, pl.num_programs(0), height, [(x_hbm, buf, fl, (l_ref, r_ref, t_ref, b_ref))], sem)
    kern = k_ref[...]

    def chunk(step, carry):
        r0 = step * RC
        out_ref[pl.ds(r0, RC)] = depth(fl, kern, r0, width).reshape(RC, width, ch)
        return carry

    lax.fori_loop(0, height // RC, chunk, 0)


def sigmoid(x):
    return 0.5 * jnp.tanh(0.5 * x) + 0.5


def gru_kernel(din_ref, xhid_hbm, hl_ref, hr_ref, ht_ref, hb_ref,
               khid_ref, w_ref, bias_ref,
               out_ref, hbuf, hfl, sem):
    band = pl.program_id(0)
    height, width, ch = out_ref.shape
    windows(band, pl.num_programs(0), height,
            [(xhid_hbm, hbuf, hfl, (hl_ref, hr_ref, ht_ref, hb_ref))], sem)

    khid = khid_ref[...]
    weights = w_ref[...]
    bias = bias_ref[...]

    def chunk(step, carry):
        r0 = step * RC
        d_in = din_ref[pl.ds(r0, RC)].reshape(RC * width, ch)
        d_hid = depth(hfl, khid, r0, width)
        both = jnp.concatenate([d_in, d_hid], axis=1)
        gates = jnp.dot(both, weights, preferred_element_type=jnp.float32) + bias
        update = sigmoid(gates[:, :ch])
        reset = sigmoid(gates[:, ch:2 * ch])
        cand = jnp.tanh(gates[:, 2 * ch:3 * ch] + reset * gates[:, 3 * ch:])
        prev = hfl[pl.ds(r0 + 1, RC), pl.ds(OFF, width), :].reshape(RC * width, ch)
        new = cand + update * (prev - cand)
        out_ref[pl.ds(r0, RC)] = new.astype(out_ref.dtype).reshape(RC, width, ch)
        return carry

    lax.fori_loop(0, height // RC, chunk, 0)


def full(shape):
    return pl.BlockSpec(shape, lambda b: (0,) * len(shape))


def window_scratch(width, ch):
    return [
        pltpu.VMEM((2, BAND + 2, width, ch), jnp.bfloat16),
        pltpu.VMEM((BAND + 2, width + 2 * OFF, ch), jnp.float32),
        pltpu.SemaphoreType.DMA((1, 2)),
    ]


def depth_in(inputs, in_ring, kern_in):
    tile_h, width, ch = inputs.shape
    return pl.pallas_call(
        depth_kernel,
        grid=(tile_h // BAND,),
        in_specs=[pl.BlockSpec(memory_space=pl.ANY)]
        + [full(r.shape) for r in in_ring]
        + [full(kern_in.shape)],
        out_specs=pl.BlockSpec((BAND, width, ch), lambda b: (b, 0, 0)),
        out_shape=jax.ShapeDtypeStruct((tile_h, width, ch), jnp.bfloat16),
        scratch_shapes=window_scratch(width, ch),
        compiler_params=pltpu.CompilerParams(dimension_semantics=("arbitrary",)),
    )(inputs, *in_ring, kern_in)


def gru(d_in, warped, hid_ring, kern_hid, w_in, w_hid, bias_in, bias_hid):
    tile_h, width, ch = warped.shape
    band_spec = pl.BlockSpec((BAND, width, ch), lambda b: (b, 0, 0))
    zeros = jnp.zeros((ch, ch), w_in.dtype)
    weights = jnp.concatenate(
        [
            jnp.concatenate([w_in[:, :2 * ch], w_in[:, 2 * ch:], zeros], axis=1),
            jnp.concatenate([w_hid[:, :2 * ch], zeros, w_hid[:, 2 * ch:]], axis=1),
        ],
        axis=0,
    )
    bias = jnp.concatenate(
        [bias_in[:2 * ch] + bias_hid[:2 * ch], bias_in[2 * ch:], bias_hid[2 * ch:]]
    ).reshape(1, -1)
    return pl.pallas_call(
        gru_kernel,
        grid=(tile_h // BAND,),
        in_specs=[band_spec, pl.BlockSpec(memory_space=pl.ANY)]
        + [full(r.shape) for r in hid_ring]
        + [full(kern_hid.shape), full(weights.shape), full(bias.shape)],
        out_specs=band_spec,
        out_shape=jax.ShapeDtypeStruct((tile_h, width, ch), jnp.bfloat16),
        scratch_shapes=window_scratch(width, ch),
        compiler_params=pltpu.CompilerParams(dimension_semantics=("arbitrary",)),
    )(d_in, warped, *hid_ring, kern_hid, weights, bias)


def body(inputs, hidden, motion, kern_in, kern_hid, w_in, w_hid, bias_in, bias_hid):
    tile_h, tile_w, channels = hidden.shape
    block_count_r = tile_h // BLOCK
    block_count_c = tile_w // BLOCK
    row_base = lax.axis_index("row") * block_count_r
    col_base = lax.axis_index("col") * block_count_c
    anchor = jnp.zeros((), jnp.int32)

    def edge_rows(cols):
        return jnp.concatenate([hidden[:HALO, cols], hidden[tile_h - HALO:, cols]], axis=0)

    cols = lax.axis_size("col")
    to_right = edge_rows(slice(tile_w - HALO, tile_w))
    to_left = edge_rows(slice(0, HALO))
    to_right, to_left = lax.optimization_barrier((to_right, to_left))
    left_edge = lax.ppermute(to_right, "col", [(i, i + 1) for i in range(cols - 1)])
    right_edge = lax.ppermute(to_left, "col", [(i + 1, i) for i in range(cols - 1)])
    mid_right = hidden[HALO:tile_h - HALO, tile_w - HALO:]
    mid_left = hidden[HALO:tile_h - HALO, :HALO]
    held, mid_right, mid_left, _, _ = lax.optimization_barrier(
        (hidden, mid_right, mid_left, to_right, to_left)
    )
    top, bottom = exchange(held, "row", 0, HALO)
    top_left, bottom_left = exchange(left_edge, "row", 0, HALO)
    top_right, bottom_right = exchange(right_edge, "row", 0, HALO)
    mid_right, mid_left, _, _ = lax.optimization_barrier((mid_right, mid_left, left_edge, right_edge))
    left_mid = lax.ppermute(mid_right, "col", [(i, i + 1) for i in range(cols - 1)])
    right_mid = lax.ppermute(mid_left, "col", [(i + 1, i) for i in range(cols - 1)])

    sources = lax.dynamic_slice(
        motion, (anchor, row_base, col_base), (2, block_count_r, block_count_c)
    )
    src_r = jnp.clip(sources[0] - row_base, -DISP, block_count_r + DISP - 1)
    src_c = jnp.clip(sources[1] - col_base, -DISP, block_count_c + DISP - 1)
    srel = jnp.stack([src_r, src_c], axis=-1).reshape(-1).astype(jnp.int32)

    d_in = depth_in(inputs, ring(inputs), kern_in)
    warped = warp(
        srel,
        (hidden, left_edge, left_mid, right_edge, right_mid, top, bottom,
         top_left, top_right, bottom_left, bottom_right),
    )
    return gru(d_in, warped, ring(warped), kern_hid, w_in, w_hid, bias_in, bias_hid)


def solution(mesh):
    in_specs = (P("row", "col", None), P("row", "col", None), P(), P(), P(), P(), P(), P(), P())
    out_specs = P("row", "col", None)
    return jax.shard_map(body, mesh=mesh, in_specs=in_specs, out_specs=out_specs, check_vma=False)
```

```python
import jax
import jax.numpy as jnp
from jax import lax
from jax.experimental import pallas as pl
from jax.experimental.pallas import tpu as pltpu
from jax.sharding import PartitionSpec as P

BLOCK = 16
DISP = 4
HALO = DISP * BLOCK
RC = 16
BAND = 32
WARP_ROWS = 4


def exchange(x, axis, dim, width):
    count = lax.axis_size(axis)
    forward = [(i, i + 1) for i in range(count - 1)]
    backward = [(i + 1, i) for i in range(count - 1)]
    size = x.shape[dim]
    low = lax.ppermute(lax.slice_in_dim(x, size - width, size, axis=dim), axis, forward)
    high = lax.ppermute(lax.slice_in_dim(x, 0, width, axis=dim), axis, backward)
    return low, high


def ring(x, left=None, right=None):
    if left is None:
        left, right = exchange(x, "col", 1, 1)
    last = x.shape[0] - 1
    count = lax.axis_size("row")
    forward = [(i, i + 1) for i in range(count - 1)]
    backward = [(i + 1, i) for i in range(count - 1)]
    down = jnp.concatenate([left[last:], x[last:], right[last:]], axis=1)
    up = jnp.concatenate([left[:1], x[:1], right[:1]], axis=1)
    top = lax.ppermute(down, "row", forward)[0]
    bottom = lax.ppermute(up, "row", backward)[0]
    width = x.shape[1]
    side_l = jnp.concatenate([top[:1], left[:, 0], bottom[:1]], axis=0)
    side_r = jnp.concatenate([top[width + 1:], right[:, 0], bottom[width + 1:]], axis=0)
    return side_l, side_r, top, bottom


def warp_kernel(srel_ref, *refs):
    hbm = refs[:11]
    out_ref, first_ref, last_ref = refs[11:14]
    canvas = refs[14]
    sem = refs[15]
    c_hbm, le_hbm, lm_hbm, re_hbm, rm_hbm, t_hbm, b_hbm, tl_hbm, tr_hbm, bl_hbm, br_hbm = hbm
    tile_h, per_row = c_hbm.shape[0], c_hbm.shape[1]
    side = le_hbm.shape[1]
    edge = le_hbm.shape[0] // 2
    band = pl.program_id(0)
    bands = pl.num_programs(0)

    def place(rows, cols):
        return canvas.at[pl.ds(rows[0], rows[1]), pl.ds(cols[0], cols[1])]

    mid = (HALO, tile_h)
    west, centre, east = (0, side), (side, per_row), (side + per_row, side)
    pairs = [
        (c_hbm, place(mid, centre)),
        (le_hbm.at[pl.ds(0, edge)], place((HALO, edge), west)),
        (le_hbm.at[pl.ds(edge, edge)], place((HALO + tile_h - edge, edge), west)),
        (lm_hbm, place((HALO + edge, tile_h - 2 * edge), west)),
        (re_hbm.at[pl.ds(0, edge)], place((HALO, edge), east)),
        (re_hbm.at[pl.ds(edge, edge)], place((HALO + tile_h - edge, edge), east)),
        (rm_hbm, place((HALO + edge, tile_h - 2 * edge), east)),
        (t_hbm, place((0, HALO), centre)),
        (b_hbm, place((HALO + tile_h, HALO), centre)),
        (tl_hbm, place((0, HALO), west)),
        (tr_hbm, place((0, HALO), east)),
        (bl_hbm, place((HALO + tile_h, HALO), west)),
        (br_hbm, place((HALO + tile_h, HALO), east)),
    ]
    copies = [pltpu.make_async_copy(h, v, sem.at[n]) for n, (h, v) in enumerate(pairs)]

    @pl.when(band == 0)
    def _():
        for c in copies:
            c.start()
        for c in copies:
            c.wait()

    for n in range(WARP_ROWS * per_row):
        k = band * WARP_ROWS * per_row + n
        r0 = srel_ref[2 * k] * BLOCK + HALO
        cb = srel_ref[2 * k + 1] + side
        rows = pl.ds((n // per_row) * BLOCK, BLOCK)
        out_ref[rows, n % per_row] = canvas[pl.ds(r0, BLOCK), cb]
        if n % per_row == 0:
            first_ref[rows] = canvas[pl.ds(r0, BLOCK), cb, 0]
        if n % per_row == per_row - 1:
            last_ref[rows] = canvas[pl.ds(r0, BLOCK), cb, BLOCK - 1]


def warp(srel, pieces):
    def blocked(x):
        return x.reshape(x.shape[0], x.shape[1] // BLOCK, BLOCK, x.shape[2])

    parts = [blocked(x) for x in pieces]
    any_spec = pl.BlockSpec(memory_space=pl.ANY)
    shape = parts[0].shape
    side = parts[1].shape[1]
    canvas = (shape[0] + 2 * HALO, shape[1] + 2 * side) + shape[2:]
    out = pl.pallas_call(
        warp_kernel,
        grid_spec=pltpu.PrefetchScalarGridSpec(
            num_scalar_prefetch=1,
            grid=(shape[0] // (BLOCK * WARP_ROWS),),
            in_specs=[any_spec] * len(parts),
            out_specs=[
                pl.BlockSpec((BLOCK * WARP_ROWS,) + shape[1:], lambda g, s: (g, 0, 0, 0)),
                pl.BlockSpec((BLOCK * WARP_ROWS, shape[3]), lambda g, s: (g, 0)),
                pl.BlockSpec((BLOCK * WARP_ROWS, shape[3]), lambda g, s: (g, 0)),
            ],
            scratch_shapes=[pltpu.VMEM(canvas, parts[0].dtype),
                            pltpu.SemaphoreType.DMA((len(parts) + 2,))],
        ),
        out_shape=[
            jax.ShapeDtypeStruct(shape, pieces[0].dtype),
            jax.ShapeDtypeStruct((shape[0], shape[3]), pieces[0].dtype),
            jax.ShapeDtypeStruct((shape[0], shape[3]), pieces[0].dtype),
        ],
        compiler_params=pltpu.CompilerParams(
            dimension_semantics=("arbitrary",), vmem_limit_bytes=60 * 1024 * 1024
        ),
    )(srel, *parts)
    return out[0].reshape(pieces[0].shape), out[1][:, None, :], out[2][:, None, :]


OFF = 8


def windows(band, bands, height, sources, sem):
    def copies(which, slot, lo, hi):
        src = pl.ds(which * height - 1 + lo, height + 2 - lo - hi)
        dst = pl.ds(lo, height + 2 - lo - hi)
        return [
            pltpu.make_async_copy(x_hbm.at[src], buf.at[slot, dst], sem.at[n, slot])
            for n, (x_hbm, buf, _, _) in enumerate(sources)
        ]

    def each_case(which, slot, fn):
        first = which == 0
        last = which == bands - 1

        @pl.when(first)
        def _():
            fn(copies(which, slot, 1, 0))

        @pl.when(last)
        def _():
            fn(copies(which, slot, 0, 1))

        @pl.when(jnp.logical_not(first | last))
        def _():
            fn(copies(which, slot, 0, 0))

    def start(cs):
        for c in cs:
            c.start()

    def wait(cs):
        for c in cs:
            c.wait()

    @pl.when(band == 0)
    def _():
        each_case(band, 0, start)

    @pl.when(band + 1 < bands)
    def _():
        each_case(band + 1, (band + 1) % 2, start)

    slot = band % 2
    each_case(band, slot, wait)

    span = pl.ds(band * height, height + 2)
    for _, buf, fl, (l_ref, r_ref, t_ref, b_ref) in sources:
        width = buf.shape[2]
        fl[:, pl.ds(OFF, width), :] = buf[slot].astype(jnp.float32)
        fl[:, pl.ds(OFF - 1, 1), :] = l_ref[span].astype(jnp.float32)[:, None, :]
        fl[:, pl.ds(OFF + width, 1), :] = r_ref[span].astype(jnp.float32)[:, None, :]

        @pl.when(band == 0)
        def _():
            fl[0, pl.ds(OFF - 1, width + 2), :] = t_ref[...].astype(jnp.float32)

        @pl.when(band == bands - 1)
        def _():
            fl[height + 1, pl.ds(OFF - 1, width + 2), :] = b_ref[...].astype(jnp.float32)


def depth(src, kern, r0, width):
    acc = jnp.zeros((RC, width, src.shape[2]), jnp.float32)
    for a in range(3):
        for b in range(3):
            acc = acc + src[pl.ds(r0 + a, RC), pl.ds(OFF - 1 + b, width), :] * kern[a, b]
    return acc.astype(jnp.bfloat16).reshape(RC * width, src.shape[2])


def depth_kernel(x_hbm, l_ref, r_ref, t_ref, b_ref, k_ref, out_ref, buf, fl, sem):
    band = pl.program_id(0)
    height, width, ch = out_ref.shape
    windows(band, pl.num_programs(0), height, [(x_hbm, buf, fl, (l_ref, r_ref, t_ref, b_ref))], sem)
    kern = k_ref[...]

    def chunk(step, carry):
        r0 = step * RC
        out_ref[pl.ds(r0, RC)] = depth(fl, kern, r0, width).reshape(RC, width, ch)
        return carry

    lax.fori_loop(0, height // RC, chunk, 0)


def sigmoid(x):
    return 0.5 * jnp.tanh(0.5 * x) + 0.5


def gru_kernel(din_ref, xhid_hbm, hl_ref, hr_ref, ht_ref, hb_ref,
               khid_ref, w_ref, bias_ref,
               out_ref, hbuf, hfl, sem):
    band = pl.program_id(0)
    height, width, ch = out_ref.shape
    windows(band, pl.num_programs(0), height,
            [(xhid_hbm, hbuf, hfl, (hl_ref, hr_ref, ht_ref, hb_ref))], sem)

    khid = khid_ref[...]
    weights = w_ref[...]
    bias = bias_ref[...]

    def chunk(step, carry):
        r0 = step * RC
        d_in = din_ref[pl.ds(r0, RC)].reshape(RC * width, ch)
        d_hid = depth(hfl, khid, r0, width)
        both = jnp.concatenate([d_in, d_hid], axis=1)
        gates = jnp.dot(both, weights, preferred_element_type=jnp.float32) + bias
        update = sigmoid(gates[:, :ch])
        reset = sigmoid(gates[:, ch:2 * ch])
        cand = jnp.tanh(gates[:, 2 * ch:3 * ch] + reset * gates[:, 3 * ch:])
        prev = hfl[pl.ds(r0 + 1, RC), pl.ds(OFF, width), :].reshape(RC * width, ch)
        new = cand + update * (prev - cand)
        out_ref[pl.ds(r0, RC)] = new.astype(out_ref.dtype).reshape(RC, width, ch)
        return carry

    lax.fori_loop(0, height // RC, chunk, 0)


def full(shape):
    return pl.BlockSpec(shape, lambda b: (0,) * len(shape))


def window_scratch(width, ch):
    return [
        pltpu.VMEM((2, BAND + 2, width, ch), jnp.bfloat16),
        pltpu.VMEM((BAND + 2, width + 2 * OFF, ch), jnp.float32),
        pltpu.SemaphoreType.DMA((1, 2)),
    ]


def depth_in(inputs, in_ring, kern_in):
    tile_h, width, ch = inputs.shape
    return pl.pallas_call(
        depth_kernel,
        grid=(tile_h // BAND,),
        in_specs=[pl.BlockSpec(memory_space=pl.ANY)]
        + [full(r.shape) for r in in_ring]
        + [full(kern_in.shape)],
        out_specs=pl.BlockSpec((BAND, width, ch), lambda b: (b, 0, 0)),
        out_shape=jax.ShapeDtypeStruct((tile_h, width, ch), jnp.bfloat16),
        scratch_shapes=window_scratch(width, ch),
        compiler_params=pltpu.CompilerParams(dimension_semantics=("arbitrary",)),
    )(inputs, *in_ring, kern_in)


def gru(d_in, warped, hid_ring, kern_hid, w_in, w_hid, bias_in, bias_hid):
    tile_h, width, ch = warped.shape
    band_spec = pl.BlockSpec((BAND, width, ch), lambda b: (b, 0, 0))
    zeros = jnp.zeros((ch, ch), w_in.dtype)
    weights = jnp.concatenate(
        [
            jnp.concatenate([w_in[:, :2 * ch], w_in[:, 2 * ch:], zeros], axis=1),
            jnp.concatenate([w_hid[:, :2 * ch], zeros, w_hid[:, 2 * ch:]], axis=1),
        ],
        axis=0,
    )
    bias = jnp.concatenate(
        [bias_in[:2 * ch] + bias_hid[:2 * ch], bias_in[2 * ch:], bias_hid[2 * ch:]]
    ).reshape(1, -1)
    return pl.pallas_call(
        gru_kernel,
        grid=(tile_h // BAND,),
        in_specs=[band_spec, pl.BlockSpec(memory_space=pl.ANY)]
        + [full(r.shape) for r in hid_ring]
        + [full(kern_hid.shape), full(weights.shape), full(bias.shape)],
        out_specs=band_spec,
        out_shape=jax.ShapeDtypeStruct((tile_h, width, ch), jnp.bfloat16),
        scratch_shapes=window_scratch(width, ch),
        compiler_params=pltpu.CompilerParams(dimension_semantics=("arbitrary",)),
    )(d_in, warped, *hid_ring, kern_hid, weights, bias)


def body(inputs, hidden, motion, kern_in, kern_hid, w_in, w_hid, bias_in, bias_hid):
    tile_h, tile_w, channels = hidden.shape
    block_count_r = tile_h // BLOCK
    block_count_c = tile_w // BLOCK
    row_base = lax.axis_index("row") * block_count_r
    col_base = lax.axis_index("col") * block_count_c
    anchor = jnp.zeros((), jnp.int32)

    def edge_rows(cols):
        return jnp.concatenate([hidden[:HALO, cols], hidden[tile_h - HALO:, cols]], axis=0)

    cols = lax.axis_size("col")
    to_right = edge_rows(slice(tile_w - HALO, tile_w))
    to_left = edge_rows(slice(0, HALO))
    to_right, to_left = lax.optimization_barrier((to_right, to_left))
    left_edge = lax.ppermute(to_right, "col", [(i, i + 1) for i in range(cols - 1)])
    right_edge = lax.ppermute(to_left, "col", [(i + 1, i) for i in range(cols - 1)])
    mid_right = hidden[HALO:tile_h - HALO, tile_w - HALO:]
    mid_left = hidden[HALO:tile_h - HALO, :HALO]
    held, mid_right, mid_left, _, _ = lax.optimization_barrier(
        (hidden, mid_right, mid_left, to_right, to_left)
    )
    top, bottom = exchange(held, "row", 0, HALO)
    top_left, bottom_left = exchange(left_edge, "row", 0, HALO)
    top_right, bottom_right = exchange(right_edge, "row", 0, HALO)
    mid_right, mid_left, _, _ = lax.optimization_barrier((mid_right, mid_left, left_edge, right_edge))
    left_mid = lax.ppermute(mid_right, "col", [(i, i + 1) for i in range(cols - 1)])
    right_mid = lax.ppermute(mid_left, "col", [(i + 1, i) for i in range(cols - 1)])

    sources = lax.dynamic_slice(
        motion, (anchor, row_base, col_base), (2, block_count_r, block_count_c)
    )
    src_r = jnp.clip(sources[0] - row_base, -DISP, block_count_r + DISP - 1)
    src_c = jnp.clip(sources[1] - col_base, -DISP, block_count_c + DISP - 1)
    srel = jnp.stack([src_r, src_c], axis=-1).reshape(-1).astype(jnp.int32)

    d_in = depth_in(inputs, ring(inputs), kern_in)
    warped = warp(
        srel,
        (hidden, left_edge, left_mid, right_edge, right_mid, top, bottom,
         top_left, top_right, bottom_left, bottom_right),
    )
    warped, first_col, last_col = warped
    cols_n = lax.axis_size("col")
    left = lax.ppermute(last_col, "col", [(i, i + 1) for i in range(cols_n - 1)])
    right = lax.ppermute(first_col, "col", [(i + 1, i) for i in range(cols_n - 1)])
    return gru(d_in, warped, ring(warped, left, right), kern_hid, w_in, w_hid, bias_in, bias_hid)


def solution(mesh):
    in_specs = (P("row", "col", None), P("row", "col", None), P(), P(), P(), P(), P(), P(), P())
    out_specs = P("row", "col", None)
    return jax.shard_map(body, mesh=mesh, in_specs=in_specs, out_specs=out_specs, check_vma=False)
```

```python
import jax
import jax.numpy as jnp
from jax import lax
from jax.experimental import pallas as pl
from jax.experimental.pallas import tpu as pltpu
from jax.sharding import PartitionSpec as P

BLOCK = 16
DISP = 4
HALO = DISP * BLOCK
RC = 16
BAND = 32
WARP_ROWS = 4


def exchange(x, axis, dim, width):
    count = lax.axis_size(axis)
    forward = [(i, i + 1) for i in range(count - 1)]
    backward = [(i + 1, i) for i in range(count - 1)]
    size = x.shape[dim]
    low = lax.ppermute(lax.slice_in_dim(x, size - width, size, axis=dim), axis, forward)
    high = lax.ppermute(lax.slice_in_dim(x, 0, width, axis=dim), axis, backward)
    return low, high


def ring(x):
    left, right = exchange(x, "col", 1, 1)
    last = x.shape[0] - 1
    count = lax.axis_size("row")
    forward = [(i, i + 1) for i in range(count - 1)]
    backward = [(i + 1, i) for i in range(count - 1)]
    down = jnp.concatenate([left[last:], x[last:], right[last:]], axis=1)
    up = jnp.concatenate([left[:1], x[:1], right[:1]], axis=1)
    top = lax.ppermute(down, "row", forward)[0]
    bottom = lax.ppermute(up, "row", backward)[0]
    width = x.shape[1]
    side_l = jnp.concatenate([top[:1], left[:, 0], bottom[:1]], axis=0)
    side_r = jnp.concatenate([top[width + 1:], right[:, 0], bottom[width + 1:]], axis=0)
    return side_l, side_r, top, bottom


def warp_kernel(srel_ref, *refs):
    hbm = refs[:11]
    out_ref = refs[11]
    canvas = refs[12]
    sem = refs[13]
    c_hbm, le_hbm, lm_hbm, re_hbm, rm_hbm, t_hbm, b_hbm, tl_hbm, tr_hbm, bl_hbm, br_hbm = hbm
    tile_h, per_row = c_hbm.shape[0], c_hbm.shape[1]
    side = le_hbm.shape[1]
    edge = le_hbm.shape[0] // 2
    band = pl.program_id(0)
    bands = pl.num_programs(0)

    def place(rows, cols):
        return canvas.at[pl.ds(rows[0], rows[1]), pl.ds(cols[0], cols[1])]

    mid = (HALO, tile_h)
    west, centre, east = (0, side), (side, per_row), (side + per_row, side)
    pairs = [
        (c_hbm, place(mid, centre)),
        (le_hbm.at[pl.ds(0, edge)], place((HALO, edge), west)),
        (le_hbm.at[pl.ds(edge, edge)], place((HALO + tile_h - edge, edge), west)),
        (lm_hbm, place((HALO + edge, tile_h - 2 * edge), west)),
        (re_hbm.at[pl.ds(0, edge)], place((HALO, edge), east)),
        (re_hbm.at[pl.ds(edge, edge)], place((HALO + tile_h - edge, edge), east)),
        (rm_hbm, place((HALO + edge, tile_h - 2 * edge), east)),
        (t_hbm, place((0, HALO), centre)),
        (b_hbm, place((HALO + tile_h, HALO), centre)),
        (tl_hbm, place((0, HALO), west)),
        (tr_hbm, place((0, HALO), east)),
        (bl_hbm, place((HALO + tile_h, HALO), west)),
        (br_hbm, place((HALO + tile_h, HALO), east)),
    ]
    copies = [pltpu.make_async_copy(h, v, sem.at[n]) for n, (h, v) in enumerate(pairs)]

    late = (8, 11, 12)

    @pl.when(band == 0)
    def _():
        for c in copies:
            c.start()
        for n, c in enumerate(copies):
            if n not in late:
                c.wait()

    @pl.when(band == bands - 1)
    def _():
        for n in late:
            copies[n].wait()

    def gather(n, carry):
        k = band * WARP_ROWS * per_row + n
        r0 = srel_ref[2 * k] * BLOCK + HALO
        cb = srel_ref[2 * k + 1] + side
        out_ref[pl.ds((n // per_row) * BLOCK, BLOCK), n % per_row] = canvas[pl.ds(r0, BLOCK), cb]
        return carry

    lax.fori_loop(0, WARP_ROWS * per_row, gather, 0, unroll=True)


def warp(srel, pieces):
    def blocked(x):
        return x.reshape(x.shape[0], x.shape[1] // BLOCK, BLOCK, x.shape[2])

    parts = [blocked(x) for x in pieces]
    any_spec = pl.BlockSpec(memory_space=pl.ANY)
    shape = parts[0].shape
    side = parts[1].shape[1]
    canvas = (shape[0] + 2 * HALO, shape[1] + 2 * side) + shape[2:]
    out = pl.pallas_call(
        warp_kernel,
        grid_spec=pltpu.PrefetchScalarGridSpec(
            num_scalar_prefetch=1,
            grid=(shape[0] // (BLOCK * WARP_ROWS),),
            in_specs=[any_spec] * len(parts),
            out_specs=pl.BlockSpec((BLOCK * WARP_ROWS,) + shape[1:], lambda g, s: (g, 0, 0, 0)),
            scratch_shapes=[pltpu.VMEM(canvas, parts[0].dtype),
                            pltpu.SemaphoreType.DMA((len(parts) + 2,))],
        ),
        out_shape=jax.ShapeDtypeStruct(shape, pieces[0].dtype),
        compiler_params=pltpu.CompilerParams(
            dimension_semantics=("arbitrary",), vmem_limit_bytes=60 * 1024 * 1024
        ),
    )(srel, *parts)
    return out.reshape(pieces[0].shape)


OFF = 8


def windows(band, bands, height, sources, sem):
    def copies(which, slot, lo, hi):
        src = pl.ds(which * height - 1 + lo, height + 2 - lo - hi)
        dst = pl.ds(lo, height + 2 - lo - hi)
        return [
            pltpu.make_async_copy(x_hbm.at[src], buf.at[slot, dst], sem.at[n, slot])
            for n, (x_hbm, buf, _, _) in enumerate(sources)
        ]

    def each_case(which, slot, fn):
        first = which == 0
        last = which == bands - 1

        @pl.when(first)
        def _():
            fn(copies(which, slot, 1, 0))

        @pl.when(last)
        def _():
            fn(copies(which, slot, 0, 1))

        @pl.when(jnp.logical_not(first | last))
        def _():
            fn(copies(which, slot, 0, 0))

    def start(cs):
        for c in cs:
            c.start()

    def wait(cs):
        for c in cs:
            c.wait()

    @pl.when(band == 0)
    def _():
        each_case(band, 0, start)

    @pl.when(band + 1 < bands)
    def _():
        each_case(band + 1, (band + 1) % 2, start)

    slot = band % 2
    each_case(band, slot, wait)

    span = pl.ds(band * height, height + 2)
    for _, buf, fl, (l_ref, r_ref, t_ref, b_ref) in sources:
        width = buf.shape[2]
        fl[:, pl.ds(OFF, width), :] = buf[slot].astype(jnp.float32)
        fl[:, pl.ds(OFF - 1, 1), :] = l_ref[span].astype(jnp.float32)[:, None, :]
        fl[:, pl.ds(OFF + width, 1), :] = r_ref[span].astype(jnp.float32)[:, None, :]

        @pl.when(band == 0)
        def _():
            fl[0, pl.ds(OFF - 1, width + 2), :] = t_ref[...].astype(jnp.float32)

        @pl.when(band == bands - 1)
        def _():
            fl[height + 1, pl.ds(OFF - 1, width + 2), :] = b_ref[...].astype(jnp.float32)


def depth(src, kern, r0, width):
    acc = jnp.zeros((RC, width, src.shape[2]), jnp.float32)
    for a in range(3):
        for b in range(3):
            acc = acc + src[pl.ds(r0 + a, RC), pl.ds(OFF - 1 + b, width), :] * kern[a, b]
    return acc.astype(jnp.bfloat16).reshape(RC * width, src.shape[2])


def depth_kernel(x_hbm, l_ref, r_ref, t_ref, b_ref, k_ref, out_ref, buf, fl, sem):
    band = pl.program_id(0)
    height, width, ch = out_ref.shape
    windows(band, pl.num_programs(0), height, [(x_hbm, buf, fl, (l_ref, r_ref, t_ref, b_ref))], sem)
    kern = k_ref[...]

    def chunk(step, carry):
        r0 = step * RC
        out_ref[pl.ds(r0, RC)] = depth(fl, kern, r0, width).reshape(RC, width, ch)
        return carry

    lax.fori_loop(0, height // RC, chunk, 0)


def sigmoid(x):
    return 0.5 * jnp.tanh(0.5 * x) + 0.5


def gru_kernel(din_ref, xhid_hbm, hl_ref, hr_ref, ht_ref, hb_ref,
               khid_ref, w_ref, bias_ref,
               out_ref, hbuf, hfl, sem):
    band = pl.program_id(0)
    height, width, ch = out_ref.shape
    windows(band, pl.num_programs(0), height,
            [(xhid_hbm, hbuf, hfl, (hl_ref, hr_ref, ht_ref, hb_ref))], sem)

    khid = khid_ref[...]
    weights = w_ref[...]
    bias = bias_ref[...]

    def chunk(step, carry):
        r0 = step * RC
        d_in = din_ref[pl.ds(r0, RC)].reshape(RC * width, ch)
        d_hid = depth(hfl, khid, r0, width)
        both = jnp.concatenate([d_in, d_hid], axis=1)
        gates = jnp.dot(both, weights, preferred_element_type=jnp.float32) + bias
        update = sigmoid(gates[:, :ch])
        reset = sigmoid(gates[:, ch:2 * ch])
        cand = jnp.tanh(gates[:, 2 * ch:3 * ch] + reset * gates[:, 3 * ch:])
        prev = hfl[pl.ds(r0 + 1, RC), pl.ds(OFF, width), :].reshape(RC * width, ch)
        new = cand + update * (prev - cand)
        out_ref[pl.ds(r0, RC)] = new.astype(out_ref.dtype).reshape(RC, width, ch)
        return carry

    lax.fori_loop(0, height // RC, chunk, 0)


def full(shape):
    return pl.BlockSpec(shape, lambda b: (0,) * len(shape))


def window_scratch(width, ch):
    return [
        pltpu.VMEM((2, BAND + 2, width, ch), jnp.bfloat16),
        pltpu.VMEM((BAND + 2, width + 2 * OFF, ch), jnp.float32),
        pltpu.SemaphoreType.DMA((1, 2)),
    ]


def depth_in(inputs, in_ring, kern_in):
    tile_h, width, ch = inputs.shape
    return pl.pallas_call(
        depth_kernel,
        grid=(tile_h // BAND,),
        in_specs=[pl.BlockSpec(memory_space=pl.ANY)]
        + [full(r.shape) for r in in_ring]
        + [full(kern_in.shape)],
        out_specs=pl.BlockSpec((BAND, width, ch), lambda b: (b, 0, 0)),
        out_shape=jax.ShapeDtypeStruct((tile_h, width, ch), jnp.bfloat16),
        scratch_shapes=window_scratch(width, ch),
        compiler_params=pltpu.CompilerParams(dimension_semantics=("arbitrary",)),
    )(inputs, *in_ring, kern_in)


def gru(d_in, warped, hid_ring, kern_hid, w_in, w_hid, bias_in, bias_hid):
    tile_h, width, ch = warped.shape
    band_spec = pl.BlockSpec((BAND, width, ch), lambda b: (b, 0, 0))
    zeros = jnp.zeros((ch, ch), w_in.dtype)
    weights = jnp.concatenate(
        [
            jnp.concatenate([w_in[:, :2 * ch], w_in[:, 2 * ch:], zeros], axis=1),
            jnp.concatenate([w_hid[:, :2 * ch], zeros, w_hid[:, 2 * ch:]], axis=1),
        ],
        axis=0,
    )
    bias = jnp.concatenate(
        [bias_in[:2 * ch] + bias_hid[:2 * ch], bias_in[2 * ch:], bias_hid[2 * ch:]]
    ).reshape(1, -1)
    return pl.pallas_call(
        gru_kernel,
        grid=(tile_h // BAND,),
        in_specs=[band_spec, pl.BlockSpec(memory_space=pl.ANY)]
        + [full(r.shape) for r in hid_ring]
        + [full(kern_hid.shape), full(weights.shape), full(bias.shape)],
        out_specs=band_spec,
        out_shape=jax.ShapeDtypeStruct((tile_h, width, ch), jnp.bfloat16),
        scratch_shapes=window_scratch(width, ch),
        compiler_params=pltpu.CompilerParams(dimension_semantics=("arbitrary",)),
    )(d_in, warped, *hid_ring, kern_hid, weights, bias)


def body(inputs, hidden, motion, kern_in, kern_hid, w_in, w_hid, bias_in, bias_hid):
    tile_h, tile_w, channels = hidden.shape
    block_count_r = tile_h // BLOCK
    block_count_c = tile_w // BLOCK
    row_base = lax.axis_index("row") * block_count_r
    col_base = lax.axis_index("col") * block_count_c
    anchor = jnp.zeros((), jnp.int32)

    def edge_rows(cols):
        return jnp.concatenate([hidden[:HALO, cols], hidden[tile_h - HALO:, cols]], axis=0)

    cols = lax.axis_size("col")
    to_right = edge_rows(slice(tile_w - HALO, tile_w))
    to_left = edge_rows(slice(0, HALO))
    to_right, to_left = lax.optimization_barrier((to_right, to_left))
    left_edge = lax.ppermute(to_right, "col", [(i, i + 1) for i in range(cols - 1)])
    right_edge = lax.ppermute(to_left, "col", [(i + 1, i) for i in range(cols - 1)])
    mid_right = hidden[HALO:tile_h - HALO, tile_w - HALO:]
    mid_left = hidden[HALO:tile_h - HALO, :HALO]
    held, mid_right, mid_left, _, _ = lax.optimization_barrier(
        (hidden, mid_right, mid_left, to_right, to_left)
    )
    top, bottom = exchange(held, "row", 0, HALO)
    top_left, bottom_left = exchange(left_edge, "row", 0, HALO)
    top_right, bottom_right = exchange(right_edge, "row", 0, HALO)
    mid_right, mid_left, _, _ = lax.optimization_barrier((mid_right, mid_left, left_edge, right_edge))
    left_mid = lax.ppermute(mid_right, "col", [(i, i + 1) for i in range(cols - 1)])
    right_mid = lax.ppermute(mid_left, "col", [(i + 1, i) for i in range(cols - 1)])

    sources = lax.dynamic_slice(
        motion, (anchor, row_base, col_base), (2, block_count_r, block_count_c)
    )
    src_r = jnp.clip(sources[0] - row_base, -DISP, block_count_r + DISP - 1)
    src_c = jnp.clip(sources[1] - col_base, -DISP, block_count_c + DISP - 1)
    srel = jnp.stack([src_r, src_c], axis=-1).reshape(-1).astype(jnp.int32)

    d_in = depth_in(inputs, ring(inputs), kern_in)
    warped = warp(
        srel,
        (hidden, left_edge, left_mid, right_edge, right_mid, top, bottom,
         top_left, top_right, bottom_left, bottom_right),
    )
    return gru(d_in, warped, ring(warped), kern_hid, w_in, w_hid, bias_in, bias_hid)


def solution(mesh):
    in_specs = (P("row", "col", None), P("row", "col", None), P(), P(), P(), P(), P(), P(), P())
    out_specs = P("row", "col", None)
    return jax.shard_map(body, mesh=mesh, in_specs=in_specs, out_specs=out_specs, check_vma=False)
```

```python
import jax
import jax.numpy as jnp
from jax import lax
from jax.experimental import pallas as pl
from jax.experimental.pallas import tpu as pltpu
from jax.sharding import PartitionSpec as P

BLOCK = 16
DISP = 4
HALO = DISP * BLOCK
RC = 32
BAND = 32
WARP_ROWS = 4


def exchange(x, axis, dim, width):
    count = lax.axis_size(axis)
    forward = [(i, i + 1) for i in range(count - 1)]
    backward = [(i + 1, i) for i in range(count - 1)]
    size = x.shape[dim]
    low = lax.ppermute(lax.slice_in_dim(x, size - width, size, axis=dim), axis, forward)
    high = lax.ppermute(lax.slice_in_dim(x, 0, width, axis=dim), axis, backward)
    return low, high


def ring(x):
    left, right = exchange(x, "col", 1, 1)
    last = x.shape[0] - 1
    count = lax.axis_size("row")
    forward = [(i, i + 1) for i in range(count - 1)]
    backward = [(i + 1, i) for i in range(count - 1)]
    down = jnp.concatenate([left[last:], x[last:], right[last:]], axis=1)
    up = jnp.concatenate([left[:1], x[:1], right[:1]], axis=1)
    top = lax.ppermute(down, "row", forward)[0]
    bottom = lax.ppermute(up, "row", backward)[0]
    width = x.shape[1]
    side_l = jnp.concatenate([top[:1], left[:, 0], bottom[:1]], axis=0)
    side_r = jnp.concatenate([top[width + 1:], right[:, 0], bottom[width + 1:]], axis=0)
    return side_l, side_r, top, bottom


def warp_kernel(srel_ref, *refs):
    hbm = refs[:11]
    out_ref = refs[11]
    canvas = refs[12]
    sem = refs[13]
    c_hbm, le_hbm, lm_hbm, re_hbm, rm_hbm, t_hbm, b_hbm, tl_hbm, tr_hbm, bl_hbm, br_hbm = hbm
    tile_h, per_row = c_hbm.shape[0], c_hbm.shape[1]
    side = le_hbm.shape[1]
    edge = le_hbm.shape[0] // 2
    band = pl.program_id(0)
    bands = pl.num_programs(0)

    def place(rows, cols):
        return canvas.at[pl.ds(rows[0], rows[1]), pl.ds(cols[0], cols[1])]

    mid = (HALO, tile_h)
    west, centre, east = (0, side), (side, per_row), (side + per_row, side)
    pairs = [
        (c_hbm, place(mid, centre)),
        (le_hbm.at[pl.ds(0, edge)], place((HALO, edge), west)),
        (le_hbm.at[pl.ds(edge, edge)], place((HALO + tile_h - edge, edge), west)),
        (lm_hbm, place((HALO + edge, tile_h - 2 * edge), west)),
        (re_hbm.at[pl.ds(0, edge)], place((HALO, edge), east)),
        (re_hbm.at[pl.ds(edge, edge)], place((HALO + tile_h - edge, edge), east)),
        (rm_hbm, place((HALO + edge, tile_h - 2 * edge), east)),
        (t_hbm, place((0, HALO), centre)),
        (b_hbm, place((HALO + tile_h, HALO), centre)),
        (tl_hbm, place((0, HALO), west)),
        (tr_hbm, place((0, HALO), east)),
        (bl_hbm, place((HALO + tile_h, HALO), west)),
        (br_hbm, place((HALO + tile_h, HALO), east)),
    ]
    copies = [pltpu.make_async_copy(h, v, sem.at[n]) for n, (h, v) in enumerate(pairs)]

    @pl.when(band == 0)
    def _():
        for c in copies:
            c.start()
        for c in copies:
            c.wait()

    def gather(n, carry):
        k = band * WARP_ROWS * per_row + n
        r0 = srel_ref[2 * k] * BLOCK + HALO
        cb = srel_ref[2 * k + 1] + side
        out_ref[pl.ds((n // per_row) * BLOCK, BLOCK), n % per_row] = canvas[pl.ds(r0, BLOCK), cb]
        return carry

    lax.fori_loop(0, WARP_ROWS * per_row, gather, 0, unroll=True)


def warp(srel, pieces):
    def blocked(x):
        return x.reshape(x.shape[0], x.shape[1] // BLOCK, BLOCK, x.shape[2])

    parts = [blocked(x) for x in pieces]
    any_spec = pl.BlockSpec(memory_space=pl.ANY)
    shape = parts[0].shape
    side = parts[1].shape[1]
    canvas = (shape[0] + 2 * HALO, shape[1] + 2 * side) + shape[2:]
    out = pl.pallas_call(
        warp_kernel,
        grid_spec=pltpu.PrefetchScalarGridSpec(
            num_scalar_prefetch=1,
            grid=(shape[0] // (BLOCK * WARP_ROWS),),
            in_specs=[any_spec] * len(parts),
            out_specs=pl.BlockSpec((BLOCK * WARP_ROWS,) + shape[1:], lambda g, s: (g, 0, 0, 0)),
            scratch_shapes=[pltpu.VMEM(canvas, parts[0].dtype),
                            pltpu.SemaphoreType.DMA((len(parts) + 2,))],
        ),
        out_shape=jax.ShapeDtypeStruct(shape, pieces[0].dtype),
        compiler_params=pltpu.CompilerParams(
            dimension_semantics=("arbitrary",), vmem_limit_bytes=60 * 1024 * 1024
        ),
    )(srel, *parts)
    return out.reshape(pieces[0].shape)


OFF = 8


def windows(band, bands, height, sources, sem):
    def copies(which, slot, lo, hi):
        src = pl.ds(which * height - 1 + lo, height + 2 - lo - hi)
        dst = pl.ds(lo, height + 2 - lo - hi)
        return [
            pltpu.make_async_copy(x_hbm.at[src], buf.at[slot, dst], sem.at[n, slot])
            for n, (x_hbm, buf, _, _) in enumerate(sources)
        ]

    def each_case(which, slot, fn):
        first = which == 0
        last = which == bands - 1

        @pl.when(first)
        def _():
            fn(copies(which, slot, 1, 0))

        @pl.when(last)
        def _():
            fn(copies(which, slot, 0, 1))

        @pl.when(jnp.logical_not(first | last))
        def _():
            fn(copies(which, slot, 0, 0))

    def start(cs):
        for c in cs:
            c.start()

    def wait(cs):
        for c in cs:
            c.wait()

    @pl.when(band == 0)
    def _():
        each_case(band, 0, start)

    @pl.when(band + 1 < bands)
    def _():
        each_case(band + 1, (band + 1) % 2, start)

    slot = band % 2
    each_case(band, slot, wait)

    span = pl.ds(band * height, height + 2)
    for _, buf, fl, (l_ref, r_ref, t_ref, b_ref) in sources:
        width = buf.shape[2]
        fl[:, pl.ds(OFF, width), :] = buf[slot].astype(jnp.float32)
        fl[:, pl.ds(OFF - 1, 1), :] = l_ref[span].astype(jnp.float32)[:, None, :]
        fl[:, pl.ds(OFF + width, 1), :] = r_ref[span].astype(jnp.float32)[:, None, :]

        @pl.when(band == 0)
        def _():
            fl[0, pl.ds(OFF - 1, width + 2), :] = t_ref[...].astype(jnp.float32)

        @pl.when(band == bands - 1)
        def _():
            fl[height + 1, pl.ds(OFF - 1, width + 2), :] = b_ref[...].astype(jnp.float32)


def depth(src, kern, r0, width):
    acc = jnp.zeros((RC, width, src.shape[2]), jnp.float32)
    for a in range(3):
        for b in range(3):
            acc = acc + src[pl.ds(r0 + a, RC), pl.ds(OFF - 1 + b, width), :] * kern[a, b]
    return acc.astype(jnp.bfloat16).reshape(RC * width, src.shape[2])


def depth_kernel(x_hbm, l_ref, r_ref, t_ref, b_ref, k_ref, out_ref, buf, fl, sem):
    band = pl.program_id(0)
    height, width, ch = out_ref.shape
    windows(band, pl.num_programs(0), height, [(x_hbm, buf, fl, (l_ref, r_ref, t_ref, b_ref))], sem)
    kern = k_ref[...]

    def chunk(step, carry):
        r0 = step * RC
        out_ref[pl.ds(r0, RC)] = depth(fl, kern, r0, width).reshape(RC, width, ch)
        return carry

    lax.fori_loop(0, height // RC, chunk, 0)


def sigmoid(x):
    return 0.5 * jnp.tanh(0.5 * x) + 0.5


def gru_kernel(din_ref, xhid_hbm, hl_ref, hr_ref, ht_ref, hb_ref,
               khid_ref, w_ref, bias_ref,
               out_ref, hbuf, hfl, sem):
    band = pl.program_id(0)
    height, width, ch = out_ref.shape
    windows(band, pl.num_programs(0), height,
            [(xhid_hbm, hbuf, hfl, (hl_ref, hr_ref, ht_ref, hb_ref))], sem)

    khid = khid_ref[...]
    weights = w_ref[...]
    bias = bias_ref[...]

    def chunk(step, carry):
        r0 = step * RC
        d_in = din_ref[pl.ds(r0, RC)].reshape(RC * width, ch)
        d_hid = depth(hfl, khid, r0, width)
        both = jnp.concatenate([d_in, d_hid], axis=1)
        gates = jnp.dot(both, weights, preferred_element_type=jnp.float32) + bias
        update = sigmoid(gates[:, :ch])
        reset = sigmoid(gates[:, ch:2 * ch])
        cand = jnp.tanh(gates[:, 2 * ch:3 * ch] + reset * gates[:, 3 * ch:])
        prev = hfl[pl.ds(r0 + 1, RC), pl.ds(OFF, width), :].reshape(RC * width, ch)
        new = cand + update * (prev - cand)
        out_ref[pl.ds(r0, RC)] = new.astype(out_ref.dtype).reshape(RC, width, ch)
        return carry

    lax.fori_loop(0, height // RC, chunk, 0)


def full(shape):
    return pl.BlockSpec(shape, lambda b: (0,) * len(shape))


def window_scratch(width, ch):
    return [
        pltpu.VMEM((2, BAND + 2, width, ch), jnp.bfloat16),
        pltpu.VMEM((BAND + 2, width + 2 * OFF, ch), jnp.float32),
        pltpu.SemaphoreType.DMA((1, 2)),
    ]


def depth_in(inputs, in_ring, kern_in):
    tile_h, width, ch = inputs.shape
    return pl.pallas_call(
        depth_kernel,
        grid=(tile_h // BAND,),
        in_specs=[pl.BlockSpec(memory_space=pl.ANY)]
        + [full(r.shape) for r in in_ring]
        + [full(kern_in.shape)],
        out_specs=pl.BlockSpec((BAND, width, ch), lambda b: (b, 0, 0)),
        out_shape=jax.ShapeDtypeStruct((tile_h, width, ch), jnp.bfloat16),
        scratch_shapes=window_scratch(width, ch),
        compiler_params=pltpu.CompilerParams(dimension_semantics=("arbitrary",)),
    )(inputs, *in_ring, kern_in)


def gru(d_in, warped, hid_ring, kern_hid, w_in, w_hid, bias_in, bias_hid):
    tile_h, width, ch = warped.shape
    band_spec = pl.BlockSpec((BAND, width, ch), lambda b: (b, 0, 0))
    zeros = jnp.zeros((ch, ch), w_in.dtype)
    weights = jnp.concatenate(
        [
            jnp.concatenate([w_in[:, :2 * ch], w_in[:, 2 * ch:], zeros], axis=1),
            jnp.concatenate([w_hid[:, :2 * ch], zeros, w_hid[:, 2 * ch:]], axis=1),
        ],
        axis=0,
    )
    bias = jnp.concatenate(
        [bias_in[:2 * ch] + bias_hid[:2 * ch], bias_in[2 * ch:], bias_hid[2 * ch:]]
    ).reshape(1, -1)
    return pl.pallas_call(
        gru_kernel,
        grid=(tile_h // BAND,),
        in_specs=[band_spec, pl.BlockSpec(memory_space=pl.ANY)]
        + [full(r.shape) for r in hid_ring]
        + [full(kern_hid.shape), full(weights.shape), full(bias.shape)],
        out_specs=band_spec,
        out_shape=jax.ShapeDtypeStruct((tile_h, width, ch), jnp.bfloat16),
        scratch_shapes=window_scratch(width, ch),
        compiler_params=pltpu.CompilerParams(dimension_semantics=("arbitrary",)),
    )(d_in, warped, *hid_ring, kern_hid, weights, bias)


def body(inputs, hidden, motion, kern_in, kern_hid, w_in, w_hid, bias_in, bias_hid):
    tile_h, tile_w, channels = hidden.shape
    block_count_r = tile_h // BLOCK
    block_count_c = tile_w // BLOCK
    row_base = lax.axis_index("row") * block_count_r
    col_base = lax.axis_index("col") * block_count_c
    anchor = jnp.zeros((), jnp.int32)

    def edge_rows(cols):
        return jnp.concatenate([hidden[:HALO, cols], hidden[tile_h - HALO:, cols]], axis=0)

    cols = lax.axis_size("col")
    to_right = edge_rows(slice(tile_w - HALO, tile_w))
    to_left = edge_rows(slice(0, HALO))
    to_right, to_left = lax.optimization_barrier((to_right, to_left))
    left_edge = lax.ppermute(to_right, "col", [(i, i + 1) for i in range(cols - 1)])
    right_edge = lax.ppermute(to_left, "col", [(i + 1, i) for i in range(cols - 1)])
    mid_right = hidden[HALO:tile_h - HALO, tile_w - HALO:]
    mid_left = hidden[HALO:tile_h - HALO, :HALO]
    held, mid_right, mid_left, _, _ = lax.optimization_barrier(
        (hidden, mid_right, mid_left, to_right, to_left)
    )
    top, bottom = exchange(held, "row", 0, HALO)
    top_left, bottom_left = exchange(left_edge, "row", 0, HALO)
    top_right, bottom_right = exchange(right_edge, "row", 0, HALO)
    mid_right, mid_left, _, _ = lax.optimization_barrier((mid_right, mid_left, left_edge, right_edge))
    left_mid = lax.ppermute(mid_right, "col", [(i, i + 1) for i in range(cols - 1)])
    right_mid = lax.ppermute(mid_left, "col", [(i + 1, i) for i in range(cols - 1)])

    sources = lax.dynamic_slice(
        motion, (anchor, row_base, col_base), (2, block_count_r, block_count_c)
    )
    src_r = jnp.clip(sources[0] - row_base, -DISP, block_count_r + DISP - 1)
    src_c = jnp.clip(sources[1] - col_base, -DISP, block_count_c + DISP - 1)
    srel = jnp.stack([src_r, src_c], axis=-1).reshape(-1).astype(jnp.int32)

    d_in = depth_in(inputs, ring(inputs), kern_in)
    warped = warp(
        srel,
        (hidden, left_edge, left_mid, right_edge, right_mid, top, bottom,
         top_left, top_right, bottom_left, bottom_right),
    )
    return gru(d_in, warped, ring(warped), kern_hid, w_in, w_hid, bias_in, bias_hid)


def solution(mesh):
    in_specs = (P("row", "col", None), P("row", "col", None), P(), P(), P(), P(), P(), P(), P())
    out_specs = P("row", "col", None)
    return jax.shard_map(body, mesh=mesh, in_specs=in_specs, out_specs=out_specs, check_vma=False)
```

```python
import jax
import jax.numpy as jnp
from jax import lax
from jax.experimental import pallas as pl
from jax.experimental.pallas import tpu as pltpu
from jax.sharding import PartitionSpec as P

BLOCK = 16
DISP = 4
HALO = DISP * BLOCK
RC = 16
BAND = 32
WARP_ROWS = 8


def exchange(x, axis, dim, width):
    count = lax.axis_size(axis)
    forward = [(i, i + 1) for i in range(count - 1)]
    backward = [(i + 1, i) for i in range(count - 1)]
    size = x.shape[dim]
    low = lax.ppermute(lax.slice_in_dim(x, size - width, size, axis=dim), axis, forward)
    high = lax.ppermute(lax.slice_in_dim(x, 0, width, axis=dim), axis, backward)
    return low, high


def ring(x):
    left, right = exchange(x, "col", 1, 1)
    last = x.shape[0] - 1
    count = lax.axis_size("row")
    forward = [(i, i + 1) for i in range(count - 1)]
    backward = [(i + 1, i) for i in range(count - 1)]
    down = jnp.concatenate([left[last:], x[last:], right[last:]], axis=1)
    up = jnp.concatenate([left[:1], x[:1], right[:1]], axis=1)
    top = lax.ppermute(down, "row", forward)[0]
    bottom = lax.ppermute(up, "row", backward)[0]
    width = x.shape[1]
    side_l = jnp.concatenate([top[:1], left[:, 0], bottom[:1]], axis=0)
    side_r = jnp.concatenate([top[width + 1:], right[:, 0], bottom[width + 1:]], axis=0)
    return side_l, side_r, top, bottom


def warp_kernel(srel_ref, *refs):
    hbm = refs[:11]
    out_ref = refs[11]
    canvas = refs[12]
    sem = refs[13]
    c_hbm, le_hbm, lm_hbm, re_hbm, rm_hbm, t_hbm, b_hbm, tl_hbm, tr_hbm, bl_hbm, br_hbm = hbm
    tile_h, per_row = c_hbm.shape[0], c_hbm.shape[1]
    side = le_hbm.shape[1]
    edge = le_hbm.shape[0] // 2
    band = pl.program_id(0)
    bands = pl.num_programs(0)

    def place(rows, cols):
        return canvas.at[pl.ds(rows[0], rows[1]), pl.ds(cols[0], cols[1])]

    mid = (HALO, tile_h)
    west, centre, east = (0, side), (side, per_row), (side + per_row, side)
    pairs = [
        (c_hbm, place(mid, centre)),
        (le_hbm.at[pl.ds(0, edge)], place((HALO, edge), west)),
        (le_hbm.at[pl.ds(edge, edge)], place((HALO + tile_h - edge, edge), west)),
        (lm_hbm, place((HALO + edge, tile_h - 2 * edge), west)),
        (re_hbm.at[pl.ds(0, edge)], place((HALO, edge), east)),
        (re_hbm.at[pl.ds(edge, edge)], place((HALO + tile_h - edge, edge), east)),
        (rm_hbm, place((HALO + edge, tile_h - 2 * edge), east)),
        (t_hbm, place((0, HALO), centre)),
        (b_hbm, place((HALO + tile_h, HALO), centre)),
        (tl_hbm, place((0, HALO), west)),
        (tr_hbm, place((0, HALO), east)),
        (bl_hbm, place((HALO + tile_h, HALO), west)),
        (br_hbm, place((HALO + tile_h, HALO), east)),
    ]
    copies = [pltpu.make_async_copy(h, v, sem.at[n]) for n, (h, v) in enumerate(pairs)]

    @pl.when(band == 0)
    def _():
        for c in copies:
            c.start()
        for c in copies:
            c.wait()

    def gather(n, carry):
        k = band * WARP_ROWS * per_row + n
        r0 = srel_ref[2 * k] * BLOCK + HALO
        cb = srel_ref[2 * k + 1] + side
        out_ref[pl.ds((n // per_row) * BLOCK, BLOCK), n % per_row] = canvas[pl.ds(r0, BLOCK), cb]
        return carry

    lax.fori_loop(0, WARP_ROWS * per_row, gather, 0, unroll=True)


def warp(srel, pieces):
    def blocked(x):
        return x.reshape(x.shape[0], x.shape[1] // BLOCK, BLOCK, x.shape[2])

    parts = [blocked(x) for x in pieces]
    any_spec = pl.BlockSpec(memory_space=pl.ANY)
    shape = parts[0].shape
    side = parts[1].shape[1]
    canvas = (shape[0] + 2 * HALO, shape[1] + 2 * side) + shape[2:]
    out = pl.pallas_call(
        warp_kernel,
        grid_spec=pltpu.PrefetchScalarGridSpec(
            num_scalar_prefetch=1,
            grid=(shape[0] // (BLOCK * WARP_ROWS),),
            in_specs=[any_spec] * len(parts),
            out_specs=pl.BlockSpec((BLOCK * WARP_ROWS,) + shape[1:], lambda g, s: (g, 0, 0, 0)),
            scratch_shapes=[pltpu.VMEM(canvas, parts[0].dtype),
                            pltpu.SemaphoreType.DMA((len(parts) + 2,))],
        ),
        out_shape=jax.ShapeDtypeStruct(shape, pieces[0].dtype),
        compiler_params=pltpu.CompilerParams(
            dimension_semantics=("arbitrary",), vmem_limit_bytes=60 * 1024 * 1024
        ),
    )(srel, *parts)
    return out.reshape(pieces[0].shape)


OFF = 8


def windows(band, bands, height, sources, sem):
    def copies(which, slot, lo, hi):
        src = pl.ds(which * height - 1 + lo, height + 2 - lo - hi)
        dst = pl.ds(lo, height + 2 - lo - hi)
        return [
            pltpu.make_async_copy(x_hbm.at[src], buf.at[slot, dst], sem.at[n, slot])
            for n, (x_hbm, buf, _, _) in enumerate(sources)
        ]

    def each_case(which, slot, fn):
        first = which == 0
        last = which == bands - 1

        @pl.when(first)
        def _():
            fn(copies(which, slot, 1, 0))

        @pl.when(last)
        def _():
            fn(copies(which, slot, 0, 1))

        @pl.when(jnp.logical_not(first | last))
        def _():
            fn(copies(which, slot, 0, 0))

    def start(cs):
        for c in cs:
            c.start()

    def wait(cs):
        for c in cs:
            c.wait()

    @pl.when(band == 0)
    def _():
        each_case(band, 0, start)

    @pl.when(band + 1 < bands)
    def _():
        each_case(band + 1, (band + 1) % 2, start)

    slot = band % 2
    each_case(band, slot, wait)

    span = pl.ds(band * height, height + 2)
    for _, buf, fl, (l_ref, r_ref, t_ref, b_ref) in sources:
        width = buf.shape[2]
        fl[:, pl.ds(OFF, width), :] = buf[slot].astype(jnp.float32)
        fl[:, pl.ds(OFF - 1, 1), :] = l_ref[span].astype(jnp.float32)[:, None, :]
        fl[:, pl.ds(OFF + width, 1), :] = r_ref[span].astype(jnp.float32)[:, None, :]

        @pl.when(band == 0)
        def _():
            fl[0, pl.ds(OFF - 1, width + 2), :] = t_ref[...].astype(jnp.float32)

        @pl.when(band == bands - 1)
        def _():
            fl[height + 1, pl.ds(OFF - 1, width + 2), :] = b_ref[...].astype(jnp.float32)


def depth(src, kern, r0, width):
    acc = jnp.zeros((RC, width, src.shape[2]), jnp.float32)
    for a in range(3):
        for b in range(3):
            acc = acc + src[pl.ds(r0 + a, RC), pl.ds(OFF - 1 + b, width), :] * kern[a, b]
    return acc.astype(jnp.bfloat16).reshape(RC * width, src.shape[2])


def depth_kernel(x_hbm, l_ref, r_ref, t_ref, b_ref, k_ref, out_ref, buf, fl, sem):
    band = pl.program_id(0)
    height, width, ch = out_ref.shape
    windows(band, pl.num_programs(0), height, [(x_hbm, buf, fl, (l_ref, r_ref, t_ref, b_ref))], sem)
    kern = k_ref[...]

    def chunk(step, carry):
        r0 = step * RC
        out_ref[pl.ds(r0, RC)] = depth(fl, kern, r0, width).reshape(RC, width, ch)
        return carry

    lax.fori_loop(0, height // RC, chunk, 0)


def sigmoid(x):
    return 0.5 * jnp.tanh(0.5 * x) + 0.5


def gru_kernel(din_ref, xhid_hbm, hl_ref, hr_ref, ht_ref, hb_ref,
               khid_ref, w_ref, bias_ref,
               out_ref, hbuf, hfl, sem):
    band = pl.program_id(0)
    height, width, ch = out_ref.shape
    windows(band, pl.num_programs(0), height,
            [(xhid_hbm, hbuf, hfl, (hl_ref, hr_ref, ht_ref, hb_ref))], sem)

    khid = khid_ref[...]
    weights = w_ref[...]
    bias = bias_ref[...]

    def chunk(step, carry):
        r0 = step * RC
        d_in = din_ref[pl.ds(r0, RC)].reshape(RC * width, ch)
        d_hid = depth(hfl, khid, r0, width)
        both = jnp.concatenate([d_in, d_hid], axis=1)
        gates = jnp.dot(both, weights, preferred_element_type=jnp.float32) + bias
        update = sigmoid(gates[:, :ch])
        reset = sigmoid(gates[:, ch:2 * ch])
        cand = jnp.tanh(gates[:, 2 * ch:3 * ch] + reset * gates[:, 3 * ch:])
        prev = hfl[pl.ds(r0 + 1, RC), pl.ds(OFF, width), :].reshape(RC * width, ch)
        new = cand + update * (prev - cand)
        out_ref[pl.ds(r0, RC)] = new.astype(out_ref.dtype).reshape(RC, width, ch)
        return carry

    lax.fori_loop(0, height // RC, chunk, 0)


def full(shape):
    return pl.BlockSpec(shape, lambda b: (0,) * len(shape))


def window_scratch(width, ch):
    return [
        pltpu.VMEM((2, BAND + 2, width, ch), jnp.bfloat16),
        pltpu.VMEM((BAND + 2, width + 2 * OFF, ch), jnp.float32),
        pltpu.SemaphoreType.DMA((1, 2)),
    ]


def depth_in(inputs, in_ring, kern_in):
    tile_h, width, ch = inputs.shape
    return pl.pallas_call(
        depth_kernel,
        grid=(tile_h // BAND,),
        in_specs=[pl.BlockSpec(memory_space=pl.ANY)]
        + [full(r.shape) for r in in_ring]
        + [full(kern_in.shape)],
        out_specs=pl.BlockSpec((BAND, width, ch), lambda b: (b, 0, 0)),
        out_shape=jax.ShapeDtypeStruct((tile_h, width, ch), jnp.bfloat16),
        scratch_shapes=window_scratch(width, ch),
        compiler_params=pltpu.CompilerParams(dimension_semantics=("arbitrary",)),
    )(inputs, *in_ring, kern_in)


def gru(d_in, warped, hid_ring, kern_hid, w_in, w_hid, bias_in, bias_hid):
    tile_h, width, ch = warped.shape
    band_spec = pl.BlockSpec((BAND, width, ch), lambda b: (b, 0, 0))
    zeros = jnp.zeros((ch, ch), w_in.dtype)
    weights = jnp.concatenate(
        [
            jnp.concatenate([w_in[:, :2 * ch], w_in[:, 2 * ch:], zeros], axis=1),
            jnp.concatenate([w_hid[:, :2 * ch], zeros, w_hid[:, 2 * ch:]], axis=1),
        ],
        axis=0,
    )
    bias = jnp.concatenate(
        [bias_in[:2 * ch] + bias_hid[:2 * ch], bias_in[2 * ch:], bias_hid[2 * ch:]]
    ).reshape(1, -1)
    return pl.pallas_call(
        gru_kernel,
        grid=(tile_h // BAND,),
        in_specs=[band_spec, pl.BlockSpec(memory_space=pl.ANY)]
        + [full(r.shape) for r in hid_ring]
        + [full(kern_hid.shape), full(weights.shape), full(bias.shape)],
        out_specs=band_spec,
        out_shape=jax.ShapeDtypeStruct((tile_h, width, ch), jnp.bfloat16),
        scratch_shapes=window_scratch(width, ch),
        compiler_params=pltpu.CompilerParams(dimension_semantics=("arbitrary",)),
    )(d_in, warped, *hid_ring, kern_hid, weights, bias)


def body(inputs, hidden, motion, kern_in, kern_hid, w_in, w_hid, bias_in, bias_hid):
    tile_h, tile_w, channels = hidden.shape
    block_count_r = tile_h // BLOCK
    block_count_c = tile_w // BLOCK
    row_base = lax.axis_index("row") * block_count_r
    col_base = lax.axis_index("col") * block_count_c
    anchor = jnp.zeros((), jnp.int32)

    def edge_rows(cols):
        return jnp.concatenate([hidden[:HALO, cols], hidden[tile_h - HALO:, cols]], axis=0)

    cols = lax.axis_size("col")
    to_right = edge_rows(slice(tile_w - HALO, tile_w))
    to_left = edge_rows(slice(0, HALO))
    to_right, to_left = lax.optimization_barrier((to_right, to_left))
    left_edge = lax.ppermute(to_right, "col", [(i, i + 1) for i in range(cols - 1)])
    right_edge = lax.ppermute(to_left, "col", [(i + 1, i) for i in range(cols - 1)])
    mid_right = hidden[HALO:tile_h - HALO, tile_w - HALO:]
    mid_left = hidden[HALO:tile_h - HALO, :HALO]
    held, mid_right, mid_left, _, _ = lax.optimization_barrier(
        (hidden, mid_right, mid_left, to_right, to_left)
    )
    top, bottom = exchange(held, "row", 0, HALO)
    top_left, bottom_left = exchange(left_edge, "row", 0, HALO)
    top_right, bottom_right = exchange(right_edge, "row", 0, HALO)
    mid_right, mid_left, _, _ = lax.optimization_barrier((mid_right, mid_left, left_edge, right_edge))
    left_mid = lax.ppermute(mid_right, "col", [(i, i + 1) for i in range(cols - 1)])
    right_mid = lax.ppermute(mid_left, "col", [(i + 1, i) for i in range(cols - 1)])

    sources = lax.dynamic_slice(
        motion, (anchor, row_base, col_base), (2, block_count_r, block_count_c)
    )
    src_r = jnp.clip(sources[0] - row_base, -DISP, block_count_r + DISP - 1)
    src_c = jnp.clip(sources[1] - col_base, -DISP, block_count_c + DISP - 1)
    srel = jnp.stack([src_r, src_c], axis=-1).reshape(-1).astype(jnp.int32)

    d_in = depth_in(inputs, ring(inputs), kern_in)
    warped = warp(
        srel,
        (hidden, left_edge, left_mid, right_edge, right_mid, top, bottom,
         top_left, top_right, bottom_left, bottom_right),
    )
    return gru(d_in, warped, ring(warped), kern_hid, w_in, w_hid, bias_in, bias_hid)


def solution(mesh):
    in_specs = (P("row", "col", None), P("row", "col", None), P(), P(), P(), P(), P(), P(), P())
    out_specs = P("row", "col", None)
    return jax.shard_map(body, mesh=mesh, in_specs=in_specs, out_specs=out_specs, check_vma=False)
```
